256 devices in a mesh: freq: 32 (over x, y, core), beam: 8 (over z).
Axes of the slice: x: 4, y: 4, z: 8, core: 2. Of those that a mesh axis runs over, the one named last changes fastest.
Arguments:
- block_samples: bfloat16 [8, 2048, 256], P('beam', 'freq'), may hold values from -6 to 6
- tail_samples: bfloat16 [8, 2048, 2048], P('beam', 'freq'), may hold values from -6 to 6
- tail_blocks: int32 [8], P('beam'), may hold values from 1 to 16, as said below
- dm_limit: int32 [8], P('beam'), may hold values from 256 to 2048, as said below
Outputs:
- peak_snr: float32 [8, 7, 2048], P('beam', None, 'freq')
- excess_snr: float32 [8, 7, 2048], P('beam', None, 'freq')
The draws below stay inside these ranges and needn't reach their ends.
Inputs may be any that keep to these rules, and one draw needn't show every extreme that they name: `tail_blocks`: some beam has a full tail in every draw. `dm_limit`: some beam searches all trials in every draw.
All inputs are finite; a program needn't handle non-finite values.
Results may differ from the reference program's by a relative error of at most 0.0003.
Values sent between devices are 32-bit elements; how exact they have to be, the bound alone decides.
No kernel may reach another device: no remote copies, remote signals or barrier semaphores. Data moves between devices by JAX's collectives and lax.ppermute only.
A program may use at most 64 MiB of HBM per device.

```python
import jax
import jax.numpy as jnp
from jax import lax

CHAN = 2048
BLOCK = 256
WIDTHS = 7
TAIL = 2048
BEAMS = 8


def draw_tail_blocks(key, part):
    most = TAIL // 128
    values = jax.random.randint(key, (BEAMS,), 1, most + 1, dtype=jnp.int32)
    chosen = jax.random.randint(jax.random.fold_in(key, 11), (), 0, BEAMS, dtype=jnp.int32)
    return values.at[chosen].set(most)


def draw_dm_limit(key, part):
    values = jax.random.randint(key, (BEAMS,), CHAN // 8, CHAN + 1, dtype=jnp.int32)
    chosen = jax.random.randint(jax.random.fold_in(key, 23), (), 0, BEAMS, dtype=jnp.int32)
    return values.at[chosen].set(CHAN)


def steps_of(rng, shape, cuts, low, high):
    def one(dim, parts):
        heights = jax.random.uniform(jax.random.fold_in(jax.random.fold_in(rng, 6), dim), (parts,), jnp.float32, low / len(cuts), high / len(cuts))
        return jnp.repeat(jnp.exp(heights), shape[dim] // parts).reshape((-1,) + (1,) * (len(shape) - dim - 1))

    level = one(*cuts[0])
    for cut in cuts[1:]:
        level = level * one(*cut)
    return level


def scatter_about(rng, dims, width, limit, cuts=(), held_as=jnp.bfloat16):
    result = width * jax.random.normal(rng, dims, jnp.float32)
    if cuts:
        result = result * steps_of(rng, dims, cuts, -0.22, 0.18)
    return jnp.clip(result, -limit, limit).astype(held_as)


def setup_inputs(seed: int = 0) -> dict:
    arg_keys = jax.random.split(jax.random.key(seed), 5)
    return {
        "block_samples": scatter_about(arg_keys[0], (BEAMS, CHAN, BLOCK), 1.0, 6.0, ((0, 8), (1, 32))),
        "tail_samples": scatter_about(arg_keys[1], (BEAMS, CHAN, TAIL), 1.0, 6.0, ((0, 8), (1, 32))),
        "tail_blocks": draw_tail_blocks(jax.random.fold_in(arg_keys[4], 71), 0),
        "dm_limit": draw_dm_limit(jax.random.fold_in(arg_keys[4], 71), 0),
    }


def delay_rows(series, shifts, reach_max):
    dims_of = series.shape
    flattened = series.reshape((-1,) + dims_of[-2:])
    padded = jnp.pad(flattened, ((0, 0), (0, 0), (reach_max, 0)))

    def slide_row(single_row, amount):
        return lax.dynamic_slice_in_dim(single_row, reach_max - amount, dims_of[-1], axis=1)
    moved_rows = jax.vmap(slide_row, in_axes=(1, 0), out_axes=1)(padded, shifts)
    return moved_rows.reshape(dims_of)

def tree_section(series, offset, reach_max):
    upper_half = jnp.repeat(series[..., 0::2, :, :], 2, axis=-2)
    lower_half = jnp.repeat(series[..., 1::2, :, :], 2, axis=-2)
    out_rows = upper_half.shape[-2]
    trials = offset + jnp.arange(out_rows, dtype=jnp.int32)
    shifts = (trials - trials // 2).astype(jnp.int32)
    return upper_half + delay_rows(lower_half, shifts, reach_max)

def peak_ratios(series, tail_len):
    searched = series[..., tail_len:]
    average = lax.optimization_barrier(jnp.mean(searched, axis=-1, keepdims=True))
    deviation = jnp.sqrt(lax.optimization_barrier(jnp.mean((searched - average) ** 2, axis=-1, keepdims=True)) + 1e-05)
    boxcar = series
    results = []
    for width_bit in range(WIDTHS):
        width_now = 2 ** width_bit
        if width_bit > 0:
            half_width = width_now // 2
            pad_spec = [(0, 0)] * (series.ndim - 1) + [(half_width, 0)]
            boxcar = boxcar + jnp.pad(boxcar[..., :-half_width], pad_spec)
        ratio = (boxcar[..., tail_len:] - width_now * average) / (jnp.sqrt(jnp.float32(width_now)) * deviation)
        results.append(lax.optimization_barrier(jnp.max(ratio, axis=-1)))
    return jnp.stack(results, axis=-2)

def reference(block_samples, tail_samples, tail_blocks, dm_limit):
    tail_len = tail_samples.shape[-1]

    def per_beam(pieces):
        block_row, tail_row, tail_count, limit_val = pieces
        valid_mask = jnp.arange(tail_len, dtype=jnp.int32)[None, :] >= tail_len - 128 * tail_count
        joined = jnp.concatenate([jnp.where(valid_mask, tail_row.astype(jnp.float32), jnp.float32(0.0)), block_row.astype(jnp.float32)], axis=-1)
        series = joined[:, None, :]
        while series.shape[0] > 1:
            series = tree_section(series, 0, series.shape[1])
        scores = peak_ratios(series[0], tail_len)
        trial_ids = jnp.arange(scores.shape[-1], dtype=jnp.int32)
        return jnp.where(trial_ids[None, :] < limit_val, scores, jnp.float32(0.0))
    peak_snr = lax.map(per_beam, (block_samples, tail_samples, tail_blocks, dm_limit))
    excess_snr = peak_snr - lax.optimization_barrier(jnp.sum(peak_snr, axis=0, keepdims=True)) / peak_snr.shape[0]
    return (peak_snr, excess_snr)
```

```python
import jax
import jax.numpy as jnp
import numpy as np
from jax import lax
from jax.sharding import PartitionSpec as P

WIDTHS = 7


def partner_2(block, axis, stride):
    count = lax.axis_size(axis)
    route = []
    for low in range(count):
        high = low | 1 << stride
        if high != low and high < count:
            route += [(low, high), (high, low)]
    return lax.ppermute(block, axis, route)


def skew_rows(series, step_size, base_shift, pad_width):
    dims_of = series.shape
    rows_count = dims_of[-2]
    length_now = dims_of[-1]
    flattened = series.reshape((-1, rows_count, length_now))
    padded = jnp.pad(flattened, ((0, 0), (0, 0), (pad_width, 0)))
    row_width = length_now + pad_width
    lined_up = padded.reshape((flattened.shape[0], rows_count * row_width))
    lined_up = jnp.pad(lined_up, ((0, 0), (0, pad_width)))
    window = lax.dynamic_slice_in_dim(
        lined_up, pad_width - base_shift, rows_count * (row_width - step_size), axis=1
    )
    moved_rows = window.reshape((flattened.shape[0], rows_count, row_width - step_size))[
        :, :, :length_now
    ]
    return moved_rows.reshape(dims_of)


def tree_section(series, offset, reach_max):
    upper_rows = series[..., 0::2, :, :]
    odd_rows = series[..., 1::2, :, :]
    even_moved = skew_rows(odd_rows, 1, (offset + 1) // 2, reach_max)
    odd_moved = skew_rows(odd_rows, 1, (offset + 2) // 2, reach_max)
    joined_rows = jnp.stack([upper_rows + even_moved, upper_rows + odd_moved], axis=-2)
    dims_of = upper_rows.shape
    return joined_rows.reshape(dims_of[:-2] + (2 * dims_of[-2], dims_of[-1]))


def peak_ratios(series, tail_len):
    searched = series[..., tail_len:]
    average = jnp.mean(searched, axis=-1, keepdims=True)
    deviation = jnp.sqrt(jnp.mean((searched - average) ** 2, axis=-1, keepdims=True) + 1e-05)
    reach_back = 2 ** (WIDTHS - 1)
    boxcar = series[..., tail_len - reach_back :]
    results = []
    for width_bit in range(WIDTHS):
        width_now = 2**width_bit
        if width_bit > 0:
            half_width = width_now // 2
            pad_spec = [(0, 0)] * (series.ndim - 1) + [(half_width, 0)]
            boxcar = boxcar + jnp.pad(boxcar[..., :-half_width], pad_spec)
        ratio = (boxcar[..., reach_back:] - width_now * average) / (
            jnp.sqrt(jnp.float32(width_now)) * deviation
        )
        results.append(jnp.max(ratio, axis=-1))
    return jnp.stack(results, axis=-2)


def local(block_samples, tail_samples, tail_blocks, dm_limit):
    beams_dev, local_chan, block_len = block_samples.shape
    tail_len = tail_samples.shape[2]
    valid_mask = (
        jnp.arange(tail_len, dtype=jnp.int32)[None, None, :]
        >= tail_len - 128 * tail_blocks[:, None, None]
    )
    joined = jnp.concatenate(
        [
            jnp.where(valid_mask, tail_samples.astype(jnp.float32), jnp.float32(0.0)),
            block_samples.astype(jnp.float32),
        ],
        axis=-1,
    )
    series = joined[:, :, None, :]
    while series.shape[1] > 1:
        series = tree_section(series, 0, series.shape[2])
    devices = lax.axis_size("freq")
    position = lax.axis_index("freq")
    series = lax.all_to_all(series, "freq", split_axis=2, concat_axis=1, tiled=True)
    per_dev = series.shape[2]
    first_trial = position * per_dev
    while series.shape[1] > 1:
        rows_now = series.shape[2]
        series = tree_section(series, 2 * first_trial, devices * rows_now)
        first_trial = 2 * first_trial
    dm_rows = series[:, 0]
    scores = peak_ratios(dm_rows, tail_len)
    out_rows = scores.shape[-1]
    trial_ids = position * out_rows + jnp.arange(out_rows, dtype=jnp.int32)
    peak_snr = jnp.where(
        trial_ids[None, None, :] < dm_limit[:, None, None], scores, jnp.float32(0.0)
    )
    beam_total = lax.psum(jnp.sum(peak_snr, axis=0), "beam")
    excess_snr = peak_snr - beam_total[None] / (beams_dev * lax.axis_size("beam"))
    return (peak_snr, excess_snr)


def solution(mesh):
    return jax.shard_map(
        local,
        mesh=mesh,
        in_specs=(P("beam", "freq", None), P("beam", "freq", None), P("beam"), P("beam")),
        out_specs=(P("beam", None, "freq"), P("beam", None, "freq")),
        check_vma=False,
    )
```

```python
import jax
import jax.numpy as jnp
import numpy as np
from jax import lax
from jax.experimental import pallas as pl
from jax.experimental.pallas import tpu as pltpu
from jax.sharding import PartitionSpec as P

WIDTHS = 7


def partner_2(block, axis, stride):
    count = lax.axis_size(axis)
    route = []
    for low in range(count):
        high = low | 1 << stride
        if high != low and high < count:
            route += [(low, high), (high, low)]
    return lax.ppermute(block, axis, route)


def skew_rows(series, step_size, base_shift, pad_width):
    dims_of = series.shape
    rows_count = dims_of[-2]
    length_now = dims_of[-1]
    flattened = series.reshape((-1, rows_count, length_now))
    padded = jnp.pad(flattened, ((0, 0), (0, 0), (pad_width, 0)))
    row_width = length_now + pad_width
    lined_up = padded.reshape((flattened.shape[0], rows_count * row_width))
    lined_up = jnp.pad(lined_up, ((0, 0), (0, pad_width)))
    window = lax.dynamic_slice_in_dim(
        lined_up, pad_width - base_shift, rows_count * (row_width - step_size), axis=1
    )
    moved_rows = window.reshape((flattened.shape[0], rows_count, row_width - step_size))[
        :, :, :length_now
    ]
    return moved_rows.reshape(dims_of)


def tree_section(series, offset, reach_max):
    upper_rows = series[..., 0::2, :, :]
    odd_rows = series[..., 1::2, :, :]
    even_moved = skew_rows(odd_rows, 1, (offset + 1) // 2, reach_max)
    odd_moved = skew_rows(odd_rows, 1, (offset + 2) // 2, reach_max)
    joined_rows = jnp.stack([upper_rows + even_moved, upper_rows + odd_moved], axis=-2)
    dims_of = upper_rows.shape
    return joined_rows.reshape(dims_of[:-2] + (2 * dims_of[-2], dims_of[-1]))


def peak_ratios(series, tail_len):
    searched = series[..., tail_len:]
    average = jnp.mean(searched, axis=-1, keepdims=True)
    deviation = jnp.sqrt(jnp.mean((searched - average) ** 2, axis=-1, keepdims=True) + 1e-05)
    reach_back = 2 ** (WIDTHS - 1)
    boxcar = series[..., tail_len - reach_back :]
    results = []
    for width_bit in range(WIDTHS):
        width_now = 2**width_bit
        if width_bit > 0:
            half_width = width_now // 2
            pad_spec = [(0, 0)] * (series.ndim - 1) + [(half_width, 0)]
            boxcar = boxcar + jnp.pad(boxcar[..., :-half_width], pad_spec)
        ratio = (boxcar[..., reach_back:] - width_now * average) / (
            jnp.sqrt(jnp.float32(width_now)) * deviation
        )
        results.append(jnp.max(ratio, axis=-1))
    return jnp.stack(results, axis=-2)


def shift_in(row_block, amount, lanes, rows_vary):
    if rows_vary:
        moved = pltpu.roll(row_block, amount, 1, stride=1, stride_axis=0)
        limit = lax.broadcasted_iota(jnp.int32, row_block.shape, 0) + amount
    else:
        moved = pltpu.roll(row_block, amount, 1)
        limit = amount
    return jnp.where(lanes >= limit, moved, jnp.float32(0.0))


def tree_in_place(buf, subbands, trials, first_trial):
    length = buf.shape[1]
    while subbands > 1:
        half = subbands // 2
        lanes = lax.broadcasted_iota(jnp.int32, (half, length), 1)
        for k in range(trials):
            top = k * subbands
            upper = buf[top : top + half, :]
            lower = buf[top + half : top + subbands, :]
            buf[top : top + half, :] = upper + shift_in(lower, first_trial + k, lanes, False)
            buf[top + half : top + subbands, :] = upper + shift_in(
                lower, first_trial + k + 1, lanes, False
            )
        subbands = half
        trials = 2 * trials
        first_trial = 2 * first_trial


def bit_reversed(count):
    bits = count.bit_length() - 1
    return np.array([int(format(i, f"0{bits}b")[::-1], 2) for i in range(count)], np.int32)


def local_tree(joined):
    beams_dev, rows, length = joined.shape

    def body(x_ref, o_ref):
        o_ref[...] = x_ref[...]
        tree_in_place(o_ref, rows, 1, 0)

    spec = pl.BlockSpec((None, rows, length), lambda b: (b, 0, 0))
    return pl.pallas_call(
        body,
        grid=(beams_dev,),
        in_specs=[spec],
        out_specs=spec,
        out_shape=jax.ShapeDtypeStruct(joined.shape, jnp.float32),
    )(joined)


def merge_tree(parts, first_trial):
    beams_dev, subbands, trials, length = parts.shape
    rows = subbands * trials
    order = bit_reversed(subbands)
    laid = jnp.swapaxes(parts[:, order], 1, 2).reshape(beams_dev, rows, length)

    def body(off_ref, x_ref, o_ref):
        o_ref[...] = x_ref[...]
        tree_in_place(o_ref, subbands, trials, off_ref[0])

    spec = pl.BlockSpec((None, rows, length), lambda b: (b, 0, 0))
    return pl.pallas_call(
        body,
        grid=(beams_dev,),
        in_specs=[pl.BlockSpec(memory_space=pltpu.SMEM), spec],
        out_specs=spec,
        out_shape=jax.ShapeDtypeStruct((beams_dev, rows, length), jnp.float32),
    )(jnp.reshape(first_trial, (1,)).astype(jnp.int32), laid)


def local(block_samples, tail_samples, tail_blocks, dm_limit):
    beams_dev, local_chan, block_len = block_samples.shape
    tail_len = tail_samples.shape[2]
    valid_mask = (
        jnp.arange(tail_len, dtype=jnp.int32)[None, None, :]
        >= tail_len - 128 * tail_blocks[:, None, None]
    )
    joined = jnp.concatenate(
        [
            jnp.where(valid_mask, tail_samples.astype(jnp.float32), jnp.float32(0.0)),
            block_samples.astype(jnp.float32),
        ],
        axis=-1,
    )
    joined = joined[:, bit_reversed(local_chan)]
    series = local_tree(joined)[:, None]
    devices = lax.axis_size("freq")
    position = lax.axis_index("freq")
    series = lax.all_to_all(series, "freq", split_axis=2, concat_axis=1, tiled=True)
    per_dev = series.shape[2]
    dm_rows = merge_tree(series, position * per_dev)
    scores = peak_ratios(dm_rows, tail_len)
    out_rows = scores.shape[-1]
    trial_ids = position * out_rows + jnp.arange(out_rows, dtype=jnp.int32)
    peak_snr = jnp.where(
        trial_ids[None, None, :] < dm_limit[:, None, None], scores, jnp.float32(0.0)
    )
    beam_total = lax.psum(jnp.sum(peak_snr, axis=0), "beam")
    excess_snr = peak_snr - beam_total[None] / (beams_dev * lax.axis_size("beam"))
    return (peak_snr, excess_snr)


def solution(mesh):
    return jax.shard_map(
        local,
        mesh=mesh,
        in_specs=(P("beam", "freq", None), P("beam", "freq", None), P("beam"), P("beam")),
        out_specs=(P("beam", None, "freq"), P("beam", None, "freq")),
        check_vma=False,
    )
```

```python
import jax
import jax.numpy as jnp
import numpy as np
from jax import lax
from jax.experimental import pallas as pl
from jax.experimental.pallas import tpu as pltpu
from jax.sharding import PartitionSpec as P

WIDTHS = 7


def partner_2(block, axis, stride):
    count = lax.axis_size(axis)
    route = []
    for low in range(count):
        high = low | 1 << stride
        if high != low and high < count:
            route += [(low, high), (high, low)]
    return lax.ppermute(block, axis, route)


def skew_rows(series, step_size, base_shift, pad_width):
    dims_of = series.shape
    rows_count = dims_of[-2]
    length_now = dims_of[-1]
    flattened = series.reshape((-1, rows_count, length_now))
    padded = jnp.pad(flattened, ((0, 0), (0, 0), (pad_width, 0)))
    row_width = length_now + pad_width
    lined_up = padded.reshape((flattened.shape[0], rows_count * row_width))
    lined_up = jnp.pad(lined_up, ((0, 0), (0, pad_width)))
    window = lax.dynamic_slice_in_dim(
        lined_up, pad_width - base_shift, rows_count * (row_width - step_size), axis=1
    )
    moved_rows = window.reshape((flattened.shape[0], rows_count, row_width - step_size))[
        :, :, :length_now
    ]
    return moved_rows.reshape(dims_of)


def tree_section(series, offset, reach_max):
    upper_rows = series[..., 0::2, :, :]
    odd_rows = series[..., 1::2, :, :]
    even_moved = skew_rows(odd_rows, 1, (offset + 1) // 2, reach_max)
    odd_moved = skew_rows(odd_rows, 1, (offset + 2) // 2, reach_max)
    joined_rows = jnp.stack([upper_rows + even_moved, upper_rows + odd_moved], axis=-2)
    dims_of = upper_rows.shape
    return joined_rows.reshape(dims_of[:-2] + (2 * dims_of[-2], dims_of[-1]))


def peak_ratios(series, tail_len):
    searched = series[..., tail_len:]
    average = jnp.mean(searched, axis=-1, keepdims=True)
    deviation = jnp.sqrt(jnp.mean((searched - average) ** 2, axis=-1, keepdims=True) + 1e-05)
    reach_back = 2 ** (WIDTHS - 1)
    boxcar = series[..., tail_len - reach_back :]
    results = []
    for width_bit in range(WIDTHS):
        width_now = 2**width_bit
        if width_bit > 0:
            half_width = width_now // 2
            pad_spec = [(0, 0)] * (series.ndim - 1) + [(half_width, 0)]
            boxcar = boxcar + jnp.pad(boxcar[..., :-half_width], pad_spec)
        ratio = (boxcar[..., reach_back:] - width_now * average) / (
            jnp.sqrt(jnp.float32(width_now)) * deviation
        )
        results.append(jnp.max(ratio, axis=-1))
    return jnp.stack(results, axis=-2)


def shift_in(row_block, amount, lanes, rows_vary):
    if rows_vary:
        moved = pltpu.roll(row_block, amount, 1, stride=1, stride_axis=0)
        limit = lax.broadcasted_iota(jnp.int32, row_block.shape, 0) + amount
    else:
        moved = pltpu.roll(row_block, amount, 1)
        limit = amount
    return jnp.where(lanes >= limit, moved, jnp.float32(0.0))


def tree_in_place(buf, subbands, trials, first_trial):
    length = buf.shape[1]
    while subbands > 1:
        half = subbands // 2
        lanes = lax.broadcasted_iota(jnp.int32, (half, length), 1)
        for k in range(trials):
            top = k * subbands
            upper = buf[top : top + half, :]
            lower = buf[top + half : top + subbands, :]
            buf[top : top + half, :] = upper + shift_in(lower, first_trial + k, lanes, False)
            buf[top + half : top + subbands, :] = upper + shift_in(
                lower, first_trial + k + 1, lanes, False
            )
        subbands = half
        trials = 2 * trials
        first_trial = 2 * first_trial


def bit_reversed(count):
    bits = count.bit_length() - 1
    return np.array([int(format(i, f"0{bits}b")[::-1], 2) for i in range(count)], np.int32)


def local_tree(joined):
    beams_dev, rows, length = joined.shape

    def body(x_ref, o_ref):
        o_ref[...] = x_ref[...]
        tree_in_place(o_ref, rows, 1, 0)

    spec = pl.BlockSpec((None, rows, length), lambda b: (b, 0, 0))
    return pl.pallas_call(
        body,
        grid=(beams_dev,),
        in_specs=[spec],
        out_specs=spec,
        out_shape=jax.ShapeDtypeStruct(joined.shape, jnp.float32),
    )(joined)


def merge_tree(parts, first_trial):
    beams_dev, subbands, trials, length = parts.shape
    rows = subbands * trials
    order = bit_reversed(subbands)
    laid = jnp.swapaxes(parts[:, order], 1, 2).reshape(beams_dev, rows, length)

    def body(off_ref, x_ref, o_ref):
        o_ref[...] = x_ref[...]
        tree_in_place(o_ref, subbands, trials, off_ref[0])

    spec = pl.BlockSpec((None, rows, length), lambda b: (b, 0, 0))
    return pl.pallas_call(
        body,
        grid=(beams_dev,),
        in_specs=[pl.BlockSpec(memory_space=pltpu.SMEM), spec],
        out_specs=spec,
        out_shape=jax.ShapeDtypeStruct((beams_dev, rows, length), jnp.float32),
    )(jnp.reshape(first_trial, (1,)).astype(jnp.int32), laid)


def local(block_samples, tail_samples, tail_blocks, dm_limit):
    beams_dev, local_chan, block_len = block_samples.shape
    tail_len = tail_samples.shape[2]
    valid_mask = (
        jnp.arange(tail_len, dtype=jnp.int32)[None, None, :]
        >= tail_len - 128 * tail_blocks[:, None, None]
    )
    joined = jnp.concatenate(
        [
            jnp.where(valid_mask, tail_samples.astype(jnp.float32), jnp.float32(0.0)),
            block_samples.astype(jnp.float32),
        ],
        axis=-1,
    )
    joined = joined[:, bit_reversed(local_chan)]
    series = local_tree(joined)[:, None]
    devices = lax.axis_size("freq")
    position = lax.axis_index("freq")
    series = lax.all_to_all(series, "freq", split_axis=2, concat_axis=1, tiled=True)
    per_dev = series.shape[2]
    dm_rows = merge_tree(series, position * per_dev)
    scores = peak_ratios(dm_rows, tail_len)
    out_rows = scores.shape[-1]
    trial_ids = position * out_rows + jnp.arange(out_rows, dtype=jnp.int32)
    peak_snr = jnp.where(
        trial_ids[None, None, :] < dm_limit[:, None, None], scores, jnp.float32(0.0)
    )
    beam_total = jnp.sum(peak_snr, axis=0)
    beam_count = lax.axis_size("beam")
    for level_bit in range(beam_count.bit_length() - 1):
        pairs = [(i, i ^ (1 << level_bit)) for i in range(beam_count)]
        beam_total = beam_total + lax.ppermute(beam_total, "beam", pairs)
    excess_snr = peak_snr - beam_total[None] / (beams_dev * lax.axis_size("beam"))
    return (peak_snr, excess_snr)


def solution(mesh):
    return jax.shard_map(
        local,
        mesh=mesh,
        in_specs=(P("beam", "freq", None), P("beam", "freq", None), P("beam"), P("beam")),
        out_specs=(P("beam", None, "freq"), P("beam", None, "freq")),
        check_vma=False,
    )
```

```python
import jax
import jax.numpy as jnp
import numpy as np
from jax import lax
from jax.experimental import pallas as pl
from jax.experimental.pallas import tpu as pltpu
from jax.sharding import PartitionSpec as P

WIDTHS = 7


def partner_2(block, axis, stride):
    count = lax.axis_size(axis)
    route = []
    for low in range(count):
        high = low | 1 << stride
        if high != low and high < count:
            route += [(low, high), (high, low)]
    return lax.ppermute(block, axis, route)


def skew_rows(series, step_size, base_shift, pad_width):
    dims_of = series.shape
    rows_count = dims_of[-2]
    length_now = dims_of[-1]
    flattened = series.reshape((-1, rows_count, length_now))
    padded = jnp.pad(flattened, ((0, 0), (0, 0), (pad_width, 0)))
    row_width = length_now + pad_width
    lined_up = padded.reshape((flattened.shape[0], rows_count * row_width))
    lined_up = jnp.pad(lined_up, ((0, 0), (0, pad_width)))
    window = lax.dynamic_slice_in_dim(
        lined_up, pad_width - base_shift, rows_count * (row_width - step_size), axis=1
    )
    moved_rows = window.reshape((flattened.shape[0], rows_count, row_width - step_size))[
        :, :, :length_now
    ]
    return moved_rows.reshape(dims_of)


def tree_section(series, offset, reach_max):
    upper_rows = series[..., 0::2, :, :]
    odd_rows = series[..., 1::2, :, :]
    even_moved = skew_rows(odd_rows, 1, (offset + 1) // 2, reach_max)
    odd_moved = skew_rows(odd_rows, 1, (offset + 2) // 2, reach_max)
    joined_rows = jnp.stack([upper_rows + even_moved, upper_rows + odd_moved], axis=-2)
    dims_of = upper_rows.shape
    return joined_rows.reshape(dims_of[:-2] + (2 * dims_of[-2], dims_of[-1]))


def peak_ratios(series, tail_len):
    searched = series[..., tail_len:]
    average = jnp.mean(searched, axis=-1, keepdims=True)
    deviation = jnp.sqrt(jnp.mean((searched - average) ** 2, axis=-1, keepdims=True) + 1e-05)
    reach_back = 2 ** (WIDTHS - 1)
    boxcar = series[..., tail_len - reach_back :]
    results = []
    for width_bit in range(WIDTHS):
        width_now = 2**width_bit
        if width_bit > 0:
            half_width = width_now // 2
            pad_spec = [(0, 0)] * (series.ndim - 1) + [(half_width, 0)]
            boxcar = boxcar + jnp.pad(boxcar[..., :-half_width], pad_spec)
        ratio = (boxcar[..., reach_back:] - width_now * average) / (
            jnp.sqrt(jnp.float32(width_now)) * deviation
        )
        results.append(jnp.max(ratio, axis=-1))
    return jnp.stack(results, axis=-2)


def shift_in(row_block, amount, lanes, stride):
    if stride:
        moved = pltpu.roll(row_block, amount, 1, stride=stride, stride_axis=0)
        limit = lax.broadcasted_iota(jnp.int32, row_block.shape, 0) * stride + amount
    else:
        moved = pltpu.roll(row_block, amount, 1)
        limit = amount
    return jnp.where(lanes >= limit, moved, jnp.float32(0.0))


def permute_rows(matrix, rows):
    return jnp.dot(matrix, rows, precision=lax.Precision.HIGHEST, preferred_element_type=jnp.float32)


def tree_in_place(buf, mid_ref, subbands, trials, first_trial, tile):
    length = buf.shape[1]
    while subbands > 1 and subbands // 2 >= tile:
        half = subbands // 2
        lanes = lax.broadcasted_iota(jnp.int32, (half, length), 1)
        for k in range(trials):
            top = k * subbands
            upper = buf[top : top + half, :]
            lower = buf[top + half : top + subbands, :]
            buf[top : top + half, :] = upper + shift_in(lower, first_trial + k, lanes, 0)
            buf[top + half : top + subbands, :] = upper + shift_in(
                lower, first_trial + k + 1, lanes, 0
            )
        subbands = half
        trials = 2 * trials
        first_trial = 2 * first_trial
    buf[...] = permute_rows(mid_ref[...], buf[...])
    groups, step = 1, 1
    lanes = lax.broadcasted_iota(jnp.int32, (tile, length), 1)
    if not isinstance(first_trial, int):
        order = bit_reversed(subbands)
        for pos in range(subbands):
            rows = slice(pos * tile, (pos + 1) * tile)
            buf[rows, :] = shift_in(buf[rows, :], first_trial * int(order[pos]), lanes, 0)
        first_trial = 0
    while subbands > 1:
        half = subbands // 2
        for group in range(groups):
            for pos in range(half):
                top = (group * subbands + pos) * tile
                low = (group * subbands + pos + half) * tile
                upper = buf[top : top + tile, :]
                lower = buf[low : low + tile, :]
                buf[top : top + tile, :] = upper + shift_in(lower, first_trial + group, lanes, step)
                buf[low : low + tile, :] = upper + shift_in(
                    lower, first_trial + group + 1, lanes, step
                )
        subbands = half
        groups = 2 * groups
        step = 2 * step
        first_trial = 2 * first_trial
    return groups


def bit_reversed(count):
    bits = count.bit_length() - 1
    return np.array([int(format(i, f"0{bits}b")[::-1], 2) for i in range(count)], np.int32)


def one_hot(targets):
    return np.eye(len(targets), dtype=np.float32)[targets]


def tables(subbands, trials, tile):
    rows = subbands * trials
    order = bit_reversed(subbands)
    entry = one_hot([order[r % subbands] * trials + r // subbands for r in range(rows)])
    at_switch = rows // tile
    mid = one_hot([(r % tile) * at_switch + r // tile for r in range(rows)])
    groups = rows // tile
    leave = one_hot([(d % groups) * tile + d // groups for d in range(rows)])
    return entry, mid, leave


TILE = 8


def local_tree(tail_samples, block_samples, tail_blocks):
    beams_dev, rows, tail_len = tail_samples.shape
    length = tail_len + block_samples.shape[2]
    entry, mid, leave = tables(rows, 1, TILE)

    def body(count_ref, tail_ref, block_ref, entry_ref, mid_ref, leave_ref, o_ref, buf):
        beam = pl.program_id(0)
        lanes = lax.broadcasted_iota(jnp.int32, (rows, tail_len), 1)
        keep = lanes >= tail_len - 128 * count_ref[beam]
        buf[:, :tail_len] = jnp.where(keep, tail_ref[...].astype(jnp.float32), jnp.float32(0.0))
        buf[:, tail_len:] = block_ref[...].astype(jnp.float32)
        buf[...] = permute_rows(entry_ref[...], buf[...])
        tree_in_place(buf, mid_ref, rows, 1, 0, TILE)
        o_ref[...] = permute_rows(leave_ref[...], buf[...])

    table_spec = pl.BlockSpec((rows, rows), lambda b: (0, 0))
    return pl.pallas_call(
        body,
        grid=(beams_dev,),
        in_specs=[
            pl.BlockSpec(memory_space=pltpu.SMEM),
            pl.BlockSpec((None, rows, tail_len), lambda b: (b, 0, 0)),
            pl.BlockSpec((None, rows, block_samples.shape[2]), lambda b: (b, 0, 0)),
            table_spec,
            table_spec,
            table_spec,
        ],
        out_specs=pl.BlockSpec((None, rows, length), lambda b: (b, 0, 0)),
        out_shape=jax.ShapeDtypeStruct((beams_dev, rows, length), jnp.float32),
        scratch_shapes=[pltpu.VMEM((rows, length), jnp.float32)],
    )(tail_blocks.astype(jnp.int32), tail_samples, block_samples, entry, mid, leave)


def merge_tree(parts, first_trial):
    beams_dev, subbands, trials, length = parts.shape
    rows = subbands * trials
    entry, mid, leave = tables(subbands, trials, TILE)

    def body(off_ref, x_ref, entry_ref, mid_ref, leave_ref, o_ref, buf):
        buf[...] = permute_rows(entry_ref[...], x_ref[...])
        tree_in_place(buf, mid_ref, subbands, trials, off_ref[0], TILE)
        o_ref[...] = permute_rows(leave_ref[...], buf[...])

    spec = pl.BlockSpec((None, rows, length), lambda b: (b, 0, 0))
    table_spec = pl.BlockSpec((rows, rows), lambda b: (0, 0))
    return pl.pallas_call(
        body,
        grid=(beams_dev,),
        in_specs=[pl.BlockSpec(memory_space=pltpu.SMEM), spec, table_spec, table_spec, table_spec],
        out_specs=spec,
        out_shape=jax.ShapeDtypeStruct((beams_dev, rows, length), jnp.float32),
        scratch_shapes=[pltpu.VMEM((rows, length), jnp.float32)],
    )(
        jnp.reshape(first_trial, (1,)).astype(jnp.int32),
        parts.reshape(beams_dev, rows, length),
        entry,
        mid,
        leave,
    )


def local(block_samples, tail_samples, tail_blocks, dm_limit):
    beams_dev, local_chan, block_len = block_samples.shape
    tail_len = tail_samples.shape[2]
    series = local_tree(tail_samples, block_samples, tail_blocks)[:, None]
    devices = lax.axis_size("freq")
    position = lax.axis_index("freq")
    series = lax.all_to_all(series, "freq", split_axis=2, concat_axis=1, tiled=True)
    per_dev = series.shape[2]
    dm_rows = merge_tree(series, position * per_dev)
    scores = peak_ratios(dm_rows, tail_len)
    out_rows = scores.shape[-1]
    trial_ids = position * out_rows + jnp.arange(out_rows, dtype=jnp.int32)
    peak_snr = jnp.where(
        trial_ids[None, None, :] < dm_limit[:, None, None], scores, jnp.float32(0.0)
    )
    beam_total = jnp.sum(peak_snr, axis=0)
    beam_count = lax.axis_size("beam")
    for level_bit in range(beam_count.bit_length() - 1):
        pairs = [(i, i ^ (1 << level_bit)) for i in range(beam_count)]
        beam_total = beam_total + lax.ppermute(beam_total, "beam", pairs)
    excess_snr = peak_snr - beam_total[None] / (beams_dev * lax.axis_size("beam"))
    return (peak_snr, excess_snr)


def solution(mesh):
    return jax.shard_map(
        local,
        mesh=mesh,
        in_specs=(P("beam", "freq", None), P("beam", "freq", None), P("beam"), P("beam")),
        out_specs=(P("beam", None, "freq"), P("beam", None, "freq")),
        check_vma=False,
    )
```

```python
import jax
import jax.numpy as jnp
import numpy as np
from jax import lax
from jax.experimental import pallas as pl
from jax.experimental.pallas import tpu as pltpu
from jax.sharding import PartitionSpec as P

WIDTHS = 7


def partner_2(block, axis, stride):
    count = lax.axis_size(axis)
    route = []
    for low in range(count):
        high = low | 1 << stride
        if high != low and high < count:
            route += [(low, high), (high, low)]
    return lax.ppermute(block, axis, route)


def skew_rows(series, step_size, base_shift, pad_width):
    dims_of = series.shape
    rows_count = dims_of[-2]
    length_now = dims_of[-1]
    flattened = series.reshape((-1, rows_count, length_now))
    padded = jnp.pad(flattened, ((0, 0), (0, 0), (pad_width, 0)))
    row_width = length_now + pad_width
    lined_up = padded.reshape((flattened.shape[0], rows_count * row_width))
    lined_up = jnp.pad(lined_up, ((0, 0), (0, pad_width)))
    window = lax.dynamic_slice_in_dim(
        lined_up, pad_width - base_shift, rows_count * (row_width - step_size), axis=1
    )
    moved_rows = window.reshape((flattened.shape[0], rows_count, row_width - step_size))[
        :, :, :length_now
    ]
    return moved_rows.reshape(dims_of)


def tree_section(series, offset, reach_max):
    upper_rows = series[..., 0::2, :, :]
    odd_rows = series[..., 1::2, :, :]
    even_moved = skew_rows(odd_rows, 1, (offset + 1) // 2, reach_max)
    odd_moved = skew_rows(odd_rows, 1, (offset + 2) // 2, reach_max)
    joined_rows = jnp.stack([upper_rows + even_moved, upper_rows + odd_moved], axis=-2)
    dims_of = upper_rows.shape
    return joined_rows.reshape(dims_of[:-2] + (2 * dims_of[-2], dims_of[-1]))


def peak_ratios(series, tail_len):
    searched = series[..., tail_len:]
    average = jnp.mean(searched, axis=-1, keepdims=True)
    deviation = jnp.sqrt(jnp.mean((searched - average) ** 2, axis=-1, keepdims=True) + 1e-05)
    reach_back = 2 ** (WIDTHS - 1)
    boxcar = series[..., tail_len - reach_back :]
    results = []
    for width_bit in range(WIDTHS):
        width_now = 2**width_bit
        if width_bit > 0:
            half_width = width_now // 2
            pad_spec = [(0, 0)] * (series.ndim - 1) + [(half_width, 0)]
            boxcar = boxcar + jnp.pad(boxcar[..., :-half_width], pad_spec)
        ratio = (boxcar[..., reach_back:] - width_now * average) / (
            jnp.sqrt(jnp.float32(width_now)) * deviation
        )
        results.append(jnp.max(ratio, axis=-1))
    return jnp.stack(results, axis=-2)


def shift_in(row_block, amount, lanes, stride):
    if stride:
        moved = pltpu.roll(row_block, amount, 1, stride=stride, stride_axis=0)
        limit = lax.broadcasted_iota(jnp.int32, row_block.shape, 0) * stride + amount
    else:
        moved = pltpu.roll(row_block, amount, 1)
        limit = amount
    return jnp.where(lanes >= limit, moved, jnp.float32(0.0))


def permute_rows(matrix, rows):
    return jnp.dot(matrix, rows, precision=lax.Precision.HIGHEST, preferred_element_type=jnp.float32)


def tree_in_place(buf, mid_ref, subbands, trials, first_trial, tile):
    length = buf.shape[1]
    while subbands > 1 and trials < tile:
        half = subbands // 2
        lanes = lax.broadcasted_iota(jnp.int32, (half, length), 1)
        for k in range(trials):
            top = k * subbands
            upper = buf[top : top + half, :]
            lower = buf[top + half : top + subbands, :]
            buf[top : top + half, :] = upper + shift_in(lower, first_trial + k, lanes, 0)
            buf[top + half : top + subbands, :] = upper + shift_in(
                lower, first_trial + k + 1, lanes, 0
            )
        subbands = half
        trials = 2 * trials
        first_trial = 2 * first_trial
    buf[...] = permute_rows(mid_ref[...], buf[...])
    groups, step = 1, 1
    lanes = lax.broadcasted_iota(jnp.int32, (tile, length), 1)
    if not isinstance(first_trial, int):
        order = bit_reversed(subbands)
        for pos in range(subbands):
            rows = slice(pos * tile, (pos + 1) * tile)
            buf[rows, :] = shift_in(buf[rows, :], first_trial * int(order[pos]), lanes, 0)
        first_trial = 0
    while subbands > 1:
        half = subbands // 2
        for group in range(groups):
            for pos in range(half):
                top = (group * subbands + pos) * tile
                low = (group * subbands + pos + half) * tile
                upper = buf[top : top + tile, :]
                lower = buf[low : low + tile, :]
                buf[top : top + tile, :] = upper + shift_in(lower, first_trial + group, lanes, step)
                buf[low : low + tile, :] = upper + shift_in(
                    lower, first_trial + group + 1, lanes, step
                )
        subbands = half
        groups = 2 * groups
        step = 2 * step
        first_trial = 2 * first_trial
    return groups


def bit_reversed(count):
    bits = count.bit_length() - 1
    return np.array([int(format(i, f"0{bits}b")[::-1], 2) for i in range(count)], np.int32)


def one_hot(targets):
    return np.eye(len(targets), dtype=np.float32)[targets]


def tables(subbands, trials, tile, split=False):
    rows = subbands * trials
    order = bit_reversed(subbands)
    entry = one_hot([order[r % subbands] * trials + r // subbands for r in range(rows)])
    at_switch = rows // tile
    mid = one_hot([(r % tile) * at_switch + r // tile for r in range(rows)])
    groups = rows // tile
    leave = one_hot([(d % groups) * tile + d // groups for d in range(rows)])
    if split:
        leave = leave[np.concatenate([np.arange(0, rows, 2), np.arange(1, rows, 2)])]
    return entry, mid, leave


TILE = 8


def local_tree(tail_samples, block_samples, tail_blocks):
    beams_dev, rows, tail_len = tail_samples.shape
    length = tail_len + block_samples.shape[2]
    entry, mid, leave = tables(rows, 1, TILE, split=True)

    def body(count_ref, tail_ref, block_ref, entry_ref, mid_ref, leave_ref, o_ref, buf):
        beam = pl.program_id(0)
        lanes = lax.broadcasted_iota(jnp.int32, (rows, tail_len), 1)
        keep = lanes >= tail_len - 128 * count_ref[beam]
        buf[:, :tail_len] = jnp.where(keep, tail_ref[...].astype(jnp.float32), jnp.float32(0.0))
        buf[:, tail_len:] = block_ref[...].astype(jnp.float32)
        buf[...] = permute_rows(entry_ref[...], buf[...])
        tree_in_place(buf, mid_ref, rows, 1, 0, TILE)
        o_ref[...] = permute_rows(leave_ref[...], buf[...])

    table_spec = pl.BlockSpec((rows, rows), lambda b: (0, 0))
    return pl.pallas_call(
        body,
        grid=(beams_dev,),
        in_specs=[
            pl.BlockSpec(memory_space=pltpu.SMEM),
            pl.BlockSpec((None, rows, tail_len), lambda b: (b, 0, 0)),
            pl.BlockSpec((None, rows, block_samples.shape[2]), lambda b: (b, 0, 0)),
            table_spec,
            table_spec,
            table_spec,
        ],
        out_specs=pl.BlockSpec((None, rows, length), lambda b: (b, 0, 0)),
        out_shape=jax.ShapeDtypeStruct((beams_dev, rows, length), jnp.float32),
        scratch_shapes=[pltpu.VMEM((rows, length), jnp.float32)],
    )(tail_blocks.astype(jnp.int32), tail_samples, block_samples, entry, mid, leave)


def merge_tree(parts, first_trial):
    beams_dev, subbands, trials, length = parts.shape
    rows = subbands * trials
    entry, mid, leave = tables(subbands, trials, TILE)

    def body(off_ref, x_ref, entry_ref, mid_ref, leave_ref, o_ref, buf):
        buf[...] = permute_rows(entry_ref[...], x_ref[...])
        tree_in_place(buf, mid_ref, subbands, trials, off_ref[0], TILE)
        o_ref[...] = permute_rows(leave_ref[...], buf[...])

    spec = pl.BlockSpec((None, rows, length), lambda b: (b, 0, 0))
    table_spec = pl.BlockSpec((rows, rows), lambda b: (0, 0))
    return pl.pallas_call(
        body,
        grid=(beams_dev,),
        in_specs=[pl.BlockSpec(memory_space=pltpu.SMEM), spec, table_spec, table_spec, table_spec],
        out_specs=spec,
        out_shape=jax.ShapeDtypeStruct((beams_dev, rows, length), jnp.float32),
        scratch_shapes=[pltpu.VMEM((rows, length), jnp.float32)],
    )(
        jnp.reshape(first_trial, (1,)).astype(jnp.int32),
        parts.reshape(beams_dev, rows, length),
        entry,
        mid,
        leave,
    )


def local(block_samples, tail_samples, tail_blocks, dm_limit):
    beams_dev, local_chan, block_len = block_samples.shape
    tail_len = tail_samples.shape[2]
    series = local_tree(tail_samples, block_samples, tail_blocks)
    position = lax.axis_index("freq")
    beam_count = lax.axis_size("beam")
    halves = series.reshape(beams_dev, 2, local_chan // 2, series.shape[-1])
    peak_parts, excess_parts = [], []
    for parity in range(2):
        part = lax.all_to_all(halves[:, parity][:, None], "freq", split_axis=2, concat_axis=1, tiled=True)
        dm_rows = merge_tree(part, 2 * position + parity)
        scores = peak_ratios(dm_rows, tail_len)
        out_rows = scores.shape[-1]
        trial_ids = (2 * position + parity) * out_rows + jnp.arange(out_rows, dtype=jnp.int32)
        peak_snr = jnp.where(
            trial_ids[None, None, :] < dm_limit[:, None, None], scores, jnp.float32(0.0)
        )
        beam_total = jnp.sum(peak_snr, axis=0)
        for level_bit in range(beam_count.bit_length() - 1):
            pairs = [(i, i ^ (1 << level_bit)) for i in range(beam_count)]
            beam_total = beam_total + lax.ppermute(beam_total, "beam", pairs)
        peak_parts.append(peak_snr)
        excess_parts.append(peak_snr - beam_total[None] / (beams_dev * beam_count))
    return (jnp.concatenate(peak_parts, axis=-1), jnp.concatenate(excess_parts, axis=-1))


def solution(mesh):
    return jax.shard_map(
        local,
        mesh=mesh,
        in_specs=(P("beam", "freq", None), P("beam", "freq", None), P("beam"), P("beam")),
        out_specs=(P("beam", None, "freq"), P("beam", None, "freq")),
        check_vma=False,
    )
```

```python
import jax
import jax.numpy as jnp
import numpy as np
from jax import lax
from jax.experimental import pallas as pl
from jax.experimental.pallas import tpu as pltpu
from jax.sharding import PartitionSpec as P

WIDTHS = 7


def partner_2(block, axis, stride):
    count = lax.axis_size(axis)
    route = []
    for low in range(count):
        high = low | 1 << stride
        if high != low and high < count:
            route += [(low, high), (high, low)]
    return lax.ppermute(block, axis, route)


def skew_rows(series, step_size, base_shift, pad_width):
    dims_of = series.shape
    rows_count = dims_of[-2]
    length_now = dims_of[-1]
    flattened = series.reshape((-1, rows_count, length_now))
    padded = jnp.pad(flattened, ((0, 0), (0, 0), (pad_width, 0)))
    row_width = length_now + pad_width
    lined_up = padded.reshape((flattened.shape[0], rows_count * row_width))
    lined_up = jnp.pad(lined_up, ((0, 0), (0, pad_width)))
    window = lax.dynamic_slice_in_dim(
        lined_up, pad_width - base_shift, rows_count * (row_width - step_size), axis=1
    )
    moved_rows = window.reshape((flattened.shape[0], rows_count, row_width - step_size))[
        :, :, :length_now
    ]
    return moved_rows.reshape(dims_of)


def tree_section(series, offset, reach_max):
    upper_rows = series[..., 0::2, :, :]
    odd_rows = series[..., 1::2, :, :]
    even_moved = skew_rows(odd_rows, 1, (offset + 1) // 2, reach_max)
    odd_moved = skew_rows(odd_rows, 1, (offset + 2) // 2, reach_max)
    joined_rows = jnp.stack([upper_rows + even_moved, upper_rows + odd_moved], axis=-2)
    dims_of = upper_rows.shape
    return joined_rows.reshape(dims_of[:-2] + (2 * dims_of[-2], dims_of[-1]))


def peak_ratios(series, tail_len):
    searched = series[..., tail_len:]
    average = jnp.mean(searched, axis=-1, keepdims=True)
    deviation = jnp.sqrt(jnp.mean((searched - average) ** 2, axis=-1, keepdims=True) + 1e-05)
    reach_back = 2 ** (WIDTHS - 1)
    boxcar = series[..., tail_len - reach_back :]
    results = []
    for width_bit in range(WIDTHS):
        width_now = 2**width_bit
        if width_bit > 0:
            half_width = width_now // 2
            pad_spec = [(0, 0)] * (series.ndim - 1) + [(half_width, 0)]
            boxcar = boxcar + jnp.pad(boxcar[..., :-half_width], pad_spec)
        ratio = (boxcar[..., reach_back:] - width_now * average) / (
            jnp.sqrt(jnp.float32(width_now)) * deviation
        )
        results.append(jnp.max(ratio, axis=-1))
    return jnp.stack(results, axis=-2)


def shift_in(row_block, amount, lanes, stride):
    if stride:
        moved = pltpu.roll(row_block, amount, 1, stride=stride, stride_axis=0)
        limit = lax.broadcasted_iota(jnp.int32, row_block.shape, 0) * stride + amount
    else:
        moved = pltpu.roll(row_block, amount, 1)
        limit = amount
    return jnp.where(lanes >= limit, moved, jnp.float32(0.0))


def permute_rows(matrix, rows):
    return jnp.dot(matrix, rows, precision=lax.Precision.HIGHEST, preferred_element_type=jnp.float32)


def tree_in_place(buf, mid_ref, subbands, trials, first_trial, tile):
    length = buf.shape[1]
    while subbands > 1 and subbands // 2 >= tile:
        half = subbands // 2
        lanes = lax.broadcasted_iota(jnp.int32, (half, length), 1)
        for k in range(trials):
            top = k * subbands
            upper = buf[top : top + half, :]
            lower = buf[top + half : top + subbands, :]
            buf[top : top + half, :] = upper + shift_in(lower, first_trial + k, lanes, 0)
            buf[top + half : top + subbands, :] = upper + shift_in(
                lower, first_trial + k + 1, lanes, 0
            )
        subbands = half
        trials = 2 * trials
        first_trial = 2 * first_trial
    buf[...] = permute_rows(mid_ref[...], buf[...])
    groups, step = 1, 1
    lanes = lax.broadcasted_iota(jnp.int32, (tile, length), 1)
    if not isinstance(first_trial, int):
        order = bit_reversed(subbands)
        for pos in range(subbands):
            rows = slice(pos * tile, (pos + 1) * tile)
            buf[rows, :] = shift_in(buf[rows, :], first_trial * int(order[pos]), lanes, 0)
        first_trial = 0
    while subbands > 1:
        half = subbands // 2
        for group in range(groups):
            for pos in range(half):
                top = (group * subbands + pos) * tile
                low = (group * subbands + pos + half) * tile
                upper = buf[top : top + tile, :]
                lower = buf[low : low + tile, :]
                buf[top : top + tile, :] = upper + shift_in(lower, first_trial + group, lanes, step)
                buf[low : low + tile, :] = upper + shift_in(
                    lower, first_trial + group + 1, lanes, step
                )
        subbands = half
        groups = 2 * groups
        step = 2 * step
        first_trial = 2 * first_trial
    return groups


def bit_reversed(count):
    bits = count.bit_length() - 1
    return np.array([int(format(i, f"0{bits}b")[::-1], 2) for i in range(count)], np.int32)


def one_hot(targets):
    return np.eye(len(targets), dtype=np.float32)[targets]


def tables(subbands, trials, tile):
    rows = subbands * trials
    order = bit_reversed(subbands)
    entry = one_hot([order[r % subbands] * trials + r // subbands for r in range(rows)])
    at_switch = rows // tile
    mid = one_hot([(r % tile) * at_switch + r // tile for r in range(rows)])
    groups = rows // tile
    leave = one_hot([(d % groups) * tile + d // groups for d in range(rows)])
    return entry, mid, leave


TILE = 8


def local_tree(tail_samples, block_samples, tail_blocks):
    beams_dev, rows, tail_len = tail_samples.shape
    length = tail_len + block_samples.shape[2]
    entry, mid, leave = tables(rows, 1, TILE)

    def body(count_ref, tail_ref, block_ref, entry_ref, mid_ref, leave_ref, o_ref, buf):
        beam = pl.program_id(0)
        lanes = lax.broadcasted_iota(jnp.int32, (rows, tail_len), 1)
        keep = lanes >= tail_len - 128 * count_ref[beam]
        buf[:, :tail_len] = jnp.where(keep, tail_ref[...].astype(jnp.float32), jnp.float32(0.0))
        buf[:, tail_len:] = block_ref[...].astype(jnp.float32)
        buf[...] = permute_rows(entry_ref[...], buf[...])
        tree_in_place(buf, mid_ref, rows, 1, 0, TILE)
        o_ref[...] = permute_rows(leave_ref[...], buf[...])

    table_spec = pl.BlockSpec((rows, rows), lambda b: (0, 0))
    return pl.pallas_call(
        body,
        grid=(beams_dev,),
        in_specs=[
            pl.BlockSpec(memory_space=pltpu.SMEM),
            pl.BlockSpec((None, rows, tail_len), lambda b: (b, 0, 0)),
            pl.BlockSpec((None, rows, block_samples.shape[2]), lambda b: (b, 0, 0)),
            table_spec,
            table_spec,
            table_spec,
        ],
        out_specs=pl.BlockSpec((None, rows, length), lambda b: (b, 0, 0)),
        out_shape=jax.ShapeDtypeStruct((beams_dev, rows, length), jnp.float32),
        scratch_shapes=[pltpu.VMEM((rows, length), jnp.float32)],
    )(tail_blocks.astype(jnp.int32), tail_samples, block_samples, entry, mid, leave)


def merge_tree(parts, first_trial):
    beams_dev, subbands, trials, length = parts.shape
    rows = subbands * trials
    entry, mid, leave = tables(subbands, trials, TILE)

    def body(off_ref, x_ref, entry_ref, mid_ref, leave_ref, o_ref, buf):
        buf[...] = permute_rows(entry_ref[...], x_ref[...])
        tree_in_place(buf, mid_ref, subbands, trials, off_ref[0], TILE)
        o_ref[...] = permute_rows(leave_ref[...], buf[...])

    spec = pl.BlockSpec((None, rows, length), lambda b: (b, 0, 0))
    table_spec = pl.BlockSpec((rows, rows), lambda b: (0, 0))
    return pl.pallas_call(
        body,
        grid=(beams_dev,),
        in_specs=[pl.BlockSpec(memory_space=pltpu.SMEM), spec, table_spec, table_spec, table_spec],
        out_specs=spec,
        out_shape=jax.ShapeDtypeStruct((beams_dev, rows, length), jnp.float32),
        scratch_shapes=[pltpu.VMEM((rows, length), jnp.float32)],
    )(
        jnp.reshape(first_trial, (1,)).astype(jnp.int32),
        parts.reshape(beams_dev, rows, length),
        entry,
        mid,
        leave,
    )


def local(block_samples, tail_samples, tail_blocks, dm_limit):
    beams_dev, local_chan, block_len = block_samples.shape
    tail_len = tail_samples.shape[2]
    series = local_tree(tail_samples, block_samples, tail_blocks)[:, None]
    devices = lax.axis_size("freq")
    position = lax.axis_index("freq")
    series = lax.all_to_all(series, "freq", split_axis=2, concat_axis=1, tiled=True)
    per_dev = series.shape[2]
    dm_rows = merge_tree(series, position * per_dev)
    scores = peak_ratios(dm_rows, tail_len)
    out_rows = scores.shape[-1]
    trial_ids = position * out_rows + jnp.arange(out_rows, dtype=jnp.int32)
    peak_snr = jnp.where(
        trial_ids[None, None, :] < dm_limit[:, None, None], scores, jnp.float32(0.0)
    )
    beam_total = jnp.sum(peak_snr, axis=0)
    beam_count = lax.axis_size("beam")
    copies = jnp.broadcast_to(beam_total[None], (beam_count,) + beam_total.shape)
    gathered = lax.all_to_all(copies, "beam", split_axis=0, concat_axis=0, tiled=True)
    beam_total = jnp.sum(gathered, axis=0)
    excess_snr = peak_snr - beam_total[None] / (beams_dev * lax.axis_size("beam"))
    return (peak_snr, excess_snr)


def solution(mesh):
    return jax.shard_map(
        local,
        mesh=mesh,
        in_specs=(P("beam", "freq", None), P("beam", "freq", None), P("beam"), P("beam")),
        out_specs=(P("beam", None, "freq"), P("beam", None, "freq")),
        check_vma=False,
    )
```

```python
import jax
import jax.numpy as jnp
import numpy as np
from jax import lax
from jax.experimental import pallas as pl
from jax.experimental.pallas import tpu as pltpu
from jax.sharding import PartitionSpec as P

WIDTHS = 7


def partner_2(block, axis, stride):
    count = lax.axis_size(axis)
    route = []
    for low in range(count):
        high = low | 1 << stride
        if high != low and high < count:
            route += [(low, high), (high, low)]
    return lax.ppermute(block, axis, route)


def skew_rows(series, step_size, base_shift, pad_width):
    dims_of = series.shape
    rows_count = dims_of[-2]
    length_now = dims_of[-1]
    flattened = series.reshape((-1, rows_count, length_now))
    padded = jnp.pad(flattened, ((0, 0), (0, 0), (pad_width, 0)))
    row_width = length_now + pad_width
    lined_up = padded.reshape((flattened.shape[0], rows_count * row_width))
    lined_up = jnp.pad(lined_up, ((0, 0), (0, pad_width)))
    window = lax.dynamic_slice_in_dim(
        lined_up, pad_width - base_shift, rows_count * (row_width - step_size), axis=1
    )
    moved_rows = window.reshape((flattened.shape[0], rows_count, row_width - step_size))[
        :, :, :length_now
    ]
    return moved_rows.reshape(dims_of)


def tree_section(series, offset, reach_max):
    upper_rows = series[..., 0::2, :, :]
    odd_rows = series[..., 1::2, :, :]
    even_moved = skew_rows(odd_rows, 1, (offset + 1) // 2, reach_max)
    odd_moved = skew_rows(odd_rows, 1, (offset + 2) // 2, reach_max)
    joined_rows = jnp.stack([upper_rows + even_moved, upper_rows + odd_moved], axis=-2)
    dims_of = upper_rows.shape
    return joined_rows.reshape(dims_of[:-2] + (2 * dims_of[-2], dims_of[-1]))


def peak_ratios(series, tail_len):
    searched = series[..., tail_len:]
    average = jnp.mean(searched, axis=-1, keepdims=True)
    deviation = jnp.sqrt(jnp.mean((searched - average) ** 2, axis=-1, keepdims=True) + 1e-05)
    reach_back = 2 ** (WIDTHS - 1)
    boxcar = series[..., tail_len - reach_back :]
    results = []
    for width_bit in range(WIDTHS):
        width_now = 2**width_bit
        if width_bit > 0:
            half_width = width_now // 2
            pad_spec = [(0, 0)] * (series.ndim - 1) + [(half_width, 0)]
            boxcar = boxcar + jnp.pad(boxcar[..., :-half_width], pad_spec)
        ratio = (boxcar[..., reach_back:] - width_now * average) / (
            jnp.sqrt(jnp.float32(width_now)) * deviation
        )
        results.append(jnp.max(ratio, axis=-1))
    return jnp.stack(results, axis=-2)


def shift_in(row_block, amount, lanes, stride):
    if stride:
        moved = pltpu.roll(row_block, amount, 1, stride=stride, stride_axis=0)
        limit = lax.broadcasted_iota(jnp.int32, row_block.shape, 0) * stride + amount
    else:
        moved = pltpu.roll(row_block, amount, 1)
        limit = amount
    return jnp.where(lanes >= limit, moved, jnp.float32(0.0))


def permute_rows(matrix, rows):
    return jnp.dot(matrix, rows, precision=lax.Precision.HIGHEST, preferred_element_type=jnp.float32)


def tree_in_place(buf, mid_ref, subbands, trials, first_trial, tile):
    length = buf.shape[1]
    while subbands > 1 and subbands // 2 >= tile:
        half = subbands // 2
        lanes = lax.broadcasted_iota(jnp.int32, (half, length), 1)
        for k in range(trials):
            top = k * subbands
            upper = buf[top : top + half, :]
            lower = buf[top + half : top + subbands, :]
            buf[top : top + half, :] = upper + shift_in(lower, first_trial + k, lanes, 0)
            buf[top + half : top + subbands, :] = upper + shift_in(
                lower, first_trial + k + 1, lanes, 0
            )
        subbands = half
        trials = 2 * trials
        first_trial = 2 * first_trial
    buf[...] = permute_rows(mid_ref[...], buf[...])
    groups, step = 1, 1
    lanes = lax.broadcasted_iota(jnp.int32, (tile, length), 1)
    if not isinstance(first_trial, int):
        order = bit_reversed(subbands)
        for pos in range(subbands):
            rows = slice(pos * tile, (pos + 1) * tile)
            buf[rows, :] = shift_in(buf[rows, :], first_trial * int(order[pos]), lanes, 0)
        first_trial = 0
    while subbands > 1:
        half = subbands // 2
        for group in range(groups):
            for pos in range(half):
                top = (group * subbands + pos) * tile
                low = (group * subbands + pos + half) * tile
                upper = buf[top : top + tile, :]
                lower = buf[low : low + tile, :]
                buf[top : top + tile, :] = upper + shift_in(lower, first_trial + group, lanes, step)
                buf[low : low + tile, :] = upper + shift_in(
                    lower, first_trial + group + 1, lanes, step
                )
        subbands = half
        groups = 2 * groups
        step = 2 * step
        first_trial = 2 * first_trial
    return groups


def bit_reversed(count):
    bits = count.bit_length() - 1
    return np.array([int(format(i, f"0{bits}b")[::-1], 2) for i in range(count)], np.int32)


def one_hot(targets):
    return np.eye(len(targets), dtype=np.float32)[targets]


def tables(subbands, trials, tile):
    rows = subbands * trials
    order = bit_reversed(subbands)
    entry = one_hot([order[r % subbands] * trials + r // subbands for r in range(rows)])
    at_switch = rows // tile
    mid = one_hot([(r % tile) * at_switch + r // tile for r in range(rows)])
    groups = rows // tile
    leave = one_hot([(d % groups) * tile + d // groups for d in range(rows)])
    return entry, mid, leave


TILE = 8


def local_tree(tail_samples, block_samples, tail_blocks):
    beams_dev, rows, tail_len = tail_samples.shape
    length = tail_len + block_samples.shape[2]
    entry, mid, leave = tables(rows, 1, TILE)

    def body(count_ref, tail_ref, block_ref, entry_ref, mid_ref, leave_ref, o_ref, buf):
        beam = pl.program_id(0)
        lanes = lax.broadcasted_iota(jnp.int32, (rows, tail_len), 1)
        keep = lanes >= tail_len - 128 * count_ref[beam]
        buf[:, :tail_len] = jnp.where(keep, tail_ref[...].astype(jnp.float32), jnp.float32(0.0))
        buf[:, tail_len:] = block_ref[...].astype(jnp.float32)
        buf[...] = permute_rows(entry_ref[...], buf[...])
        tree_in_place(buf, mid_ref, rows, 1, 0, TILE)
        o_ref[...] = permute_rows(leave_ref[...], buf[...])

    table_spec = pl.BlockSpec((rows, rows), lambda b: (0, 0))
    return pl.pallas_call(
        body,
        grid=(beams_dev,),
        in_specs=[
            pl.BlockSpec(memory_space=pltpu.SMEM),
            pl.BlockSpec((None, rows, tail_len), lambda b: (b, 0, 0)),
            pl.BlockSpec((None, rows, block_samples.shape[2]), lambda b: (b, 0, 0)),
            table_spec,
            table_spec,
            table_spec,
        ],
        out_specs=pl.BlockSpec((None, rows, length), lambda b: (b, 0, 0)),
        out_shape=jax.ShapeDtypeStruct((beams_dev, rows, length), jnp.float32),
        scratch_shapes=[pltpu.VMEM((rows, length), jnp.float32)],
    )(tail_blocks.astype(jnp.int32), tail_samples, block_samples, entry, mid, leave)


def peaks_of(dm_rows, tail_len, block_len):
    trials = dm_rows.shape[0]
    searched = dm_rows[:, tail_len:]
    average = jnp.sum(searched, axis=1, keepdims=True) / jnp.float32(block_len)
    spread = jnp.sum((searched - average) ** 2, axis=1, keepdims=True) / jnp.float32(block_len)
    deviation = jnp.sqrt(spread + jnp.float32(1e-05))
    boxcar = dm_rows[:, tail_len - 128 :]
    lane_ids = lax.broadcasted_iota(jnp.int32, (trials, 128), 1)
    table = jnp.zeros((trials, 128), jnp.float32)
    for width_bit in range(WIDTHS):
        width_now = 2**width_bit
        if width_bit > 0:
            boxcar = boxcar + pltpu.roll(boxcar, width_now // 2, 1)
        top = jnp.max(boxcar[:, 128:], axis=1, keepdims=True)
        ratio = (top - width_now * average) / (np.sqrt(np.float32(width_now)) * deviation)
        table = jnp.where(lane_ids == width_bit, ratio, table)
    return table.T[:8]


def merge_tree(parts, first_trial, tail_len):
    beams_dev, subbands, trials, length = parts.shape
    rows = subbands * trials
    entry, mid, leave = tables(subbands, trials, TILE)

    def body(off_ref, x_ref, entry_ref, mid_ref, leave_ref, o_ref, buf):
        buf[...] = permute_rows(entry_ref[...], x_ref[...])
        tree_in_place(buf, mid_ref, subbands, trials, off_ref[0], TILE)
        buf[...] = permute_rows(leave_ref[...], buf[...])
        o_ref[...] = peaks_of(buf[...], tail_len, length - tail_len)

    spec = pl.BlockSpec((None, rows, length), lambda b: (b, 0, 0))
    table_spec = pl.BlockSpec((rows, rows), lambda b: (0, 0))
    return pl.pallas_call(
        body,
        grid=(beams_dev,),
        in_specs=[pl.BlockSpec(memory_space=pltpu.SMEM), spec, table_spec, table_spec, table_spec],
        out_specs=pl.BlockSpec((None, 8, rows), lambda b: (b, 0, 0)),
        out_shape=jax.ShapeDtypeStruct((beams_dev, 8, rows), jnp.float32),
        scratch_shapes=[pltpu.VMEM((rows, length), jnp.float32)],
    )(
        jnp.reshape(first_trial, (1,)).astype(jnp.int32),
        parts.reshape(beams_dev, rows, length),
        entry,
        mid,
        leave,
    )[:, :WIDTHS]


def local(block_samples, tail_samples, tail_blocks, dm_limit):
    beams_dev, local_chan, block_len = block_samples.shape
    tail_len = tail_samples.shape[2]
    series = local_tree(tail_samples, block_samples, tail_blocks)[:, None]
    devices = lax.axis_size("freq")
    position = lax.axis_index("freq")
    series = lax.all_to_all(series, "freq", split_axis=2, concat_axis=1, tiled=True)
    per_dev = series.shape[2]
    scores = merge_tree(series, position * per_dev, tail_len)
    out_rows = scores.shape[-1]
    trial_ids = position * out_rows + jnp.arange(out_rows, dtype=jnp.int32)
    peak_snr = jnp.where(
        trial_ids[None, None, :] < dm_limit[:, None, None], scores, jnp.float32(0.0)
    )
    beam_total = jnp.sum(peak_snr, axis=0)
    beam_count = lax.axis_size("beam")
    for level_bit in range(beam_count.bit_length() - 1):
        pairs = [(i, i ^ (1 << level_bit)) for i in range(beam_count)]
        beam_total = beam_total + lax.ppermute(beam_total, "beam", pairs)
    excess_snr = peak_snr - beam_total[None] / (beams_dev * lax.axis_size("beam"))
    return (peak_snr, excess_snr)


def solution(mesh):
    return jax.shard_map(
        local,
        mesh=mesh,
        in_specs=(P("beam", "freq", None), P("beam", "freq", None), P("beam"), P("beam")),
        out_specs=(P("beam", None, "freq"), P("beam", None, "freq")),
        check_vma=False,
    )
```

```python
import jax
import jax.numpy as jnp
import numpy as np
from jax import lax
from jax.experimental import pallas as pl
from jax.experimental.pallas import tpu as pltpu
from jax.sharding import PartitionSpec as P

WIDTHS = 7


def partner_2(block, axis, stride):
    count = lax.axis_size(axis)
    route = []
    for low in range(count):
        high = low | 1 << stride
        if high != low and high < count:
            route += [(low, high), (high, low)]
    return lax.ppermute(block, axis, route)


def skew_rows(series, step_size, base_shift, pad_width):
    dims_of = series.shape
    rows_count = dims_of[-2]
    length_now = dims_of[-1]
    flattened = series.reshape((-1, rows_count, length_now))
    padded = jnp.pad(flattened, ((0, 0), (0, 0), (pad_width, 0)))
    row_width = length_now + pad_width
    lined_up = padded.reshape((flattened.shape[0], rows_count * row_width))
    lined_up = jnp.pad(lined_up, ((0, 0), (0, pad_width)))
    window = lax.dynamic_slice_in_dim(
        lined_up, pad_width - base_shift, rows_count * (row_width - step_size), axis=1
    )
    moved_rows = window.reshape((flattened.shape[0], rows_count, row_width - step_size))[
        :, :, :length_now
    ]
    return moved_rows.reshape(dims_of)


def tree_section(series, offset, reach_max):
    upper_rows = series[..., 0::2, :, :]
    odd_rows = series[..., 1::2, :, :]
    even_moved = skew_rows(odd_rows, 1, (offset + 1) // 2, reach_max)
    odd_moved = skew_rows(odd_rows, 1, (offset + 2) // 2, reach_max)
    joined_rows = jnp.stack([upper_rows + even_moved, upper_rows + odd_moved], axis=-2)
    dims_of = upper_rows.shape
    return joined_rows.reshape(dims_of[:-2] + (2 * dims_of[-2], dims_of[-1]))


def peak_ratios(series, tail_len):
    searched = series[..., tail_len:]
    average = jnp.mean(searched, axis=-1, keepdims=True)
    deviation = jnp.sqrt(jnp.mean((searched - average) ** 2, axis=-1, keepdims=True) + 1e-05)
    reach_back = 2 ** (WIDTHS - 1)
    boxcar = series[..., tail_len - reach_back :]
    results = []
    for width_bit in range(WIDTHS):
        width_now = 2**width_bit
        if width_bit > 0:
            half_width = width_now // 2
            pad_spec = [(0, 0)] * (series.ndim - 1) + [(half_width, 0)]
            boxcar = boxcar + jnp.pad(boxcar[..., :-half_width], pad_spec)
        ratio = (boxcar[..., reach_back:] - width_now * average) / (
            jnp.sqrt(jnp.float32(width_now)) * deviation
        )
        results.append(jnp.max(ratio, axis=-1))
    return jnp.stack(results, axis=-2)


def shift_in(row_block, amount, lanes, stride):
    if stride:
        moved = pltpu.roll(row_block, amount, 1, stride=stride, stride_axis=0)
        limit = lax.broadcasted_iota(jnp.int32, row_block.shape, 0) * stride + amount
    else:
        moved = pltpu.roll(row_block, amount, 1)
        limit = amount
    return jnp.where(lanes >= limit, moved, jnp.float32(0.0))


def permute_rows(matrix, rows):
    return jnp.dot(matrix, rows, precision=lax.Precision.HIGHEST, preferred_element_type=jnp.float32)


def tree_in_place(buf, mid_ref, subbands, trials, first_trial, tile):
    length = buf.shape[1]
    while subbands > 1 and subbands // 2 >= tile:
        half = subbands // 2
        lanes = lax.broadcasted_iota(jnp.int32, (half, length), 1)
        for k in range(trials):
            top = k * subbands
            upper = buf[top : top + half, :]
            lower = buf[top + half : top + subbands, :]
            buf[top : top + half, :] = upper + shift_in(lower, first_trial + k, lanes, 0)
            buf[top + half : top + subbands, :] = upper + shift_in(
                lower, first_trial + k + 1, lanes, 0
            )
        subbands = half
        trials = 2 * trials
        first_trial = 2 * first_trial
    buf[...] = permute_rows(mid_ref[...], buf[...])
    groups, step = 1, 1
    lanes = lax.broadcasted_iota(jnp.int32, (tile, length), 1)
    if not isinstance(first_trial, int):
        order = bit_reversed(subbands)
        for pos in range(subbands):
            rows = slice(pos * tile, (pos + 1) * tile)
            buf[rows, :] = shift_in(buf[rows, :], first_trial * int(order[pos]), lanes, 0)
        first_trial = 0
    while subbands > 1:
        half = subbands // 2
        for group in range(groups):
            for pos in range(half):
                top = (group * subbands + pos) * tile
                low = (group * subbands + pos + half) * tile
                upper = buf[top : top + tile, :]
                lower = buf[low : low + tile, :]
                buf[top : top + tile, :] = upper + shift_in(lower, first_trial + group, lanes, step)
                buf[low : low + tile, :] = upper + shift_in(
                    lower, first_trial + group + 1, lanes, step
                )
        subbands = half
        groups = 2 * groups
        step = 2 * step
        first_trial = 2 * first_trial
    return groups


def bit_reversed(count):
    bits = count.bit_length() - 1
    return np.array([int(format(i, f"0{bits}b")[::-1], 2) for i in range(count)], np.int32)


def one_hot(targets):
    return np.eye(len(targets), dtype=np.float32)[targets]


def tables(subbands, trials, tile):
    rows = subbands * trials
    order = bit_reversed(subbands)
    entry = one_hot([order[r % subbands] * trials + r // subbands for r in range(rows)])
    at_switch = rows // tile
    mid = one_hot([(r % tile) * at_switch + r // tile for r in range(rows)])
    groups = rows // tile
    leave = one_hot([(d % groups) * tile + d // groups for d in range(rows)])
    return entry, mid, leave


TILE = 8


def local_tree(tail_samples, block_samples, tail_blocks):
    beams_dev, rows, tail_len = tail_samples.shape
    length = tail_len + block_samples.shape[2]
    entry, mid, leave = tables(rows, 1, TILE)

    def body(count_ref, tail_ref, block_ref, entry_ref, mid_ref, leave_ref, o_ref, buf):
        beam = pl.program_id(0)
        lanes = lax.broadcasted_iota(jnp.int32, (rows, tail_len), 1)
        keep = lanes >= tail_len - 128 * count_ref[beam]
        order = entry_ref[...].astype(jnp.bfloat16)
        tail = jnp.dot(order, tail_ref[...], preferred_element_type=jnp.float32)
        buf[:, :tail_len] = jnp.where(keep, tail, jnp.float32(0.0))
        buf[:, tail_len:] = jnp.dot(order, block_ref[...], preferred_element_type=jnp.float32)
        tree_in_place(buf, mid_ref, rows, 1, 0, TILE)
        o_ref[...] = permute_rows(leave_ref[...], buf[...])

    table_spec = pl.BlockSpec((rows, rows), lambda b: (0, 0))
    return pl.pallas_call(
        body,
        grid=(beams_dev,),
        in_specs=[
            pl.BlockSpec(memory_space=pltpu.SMEM),
            pl.BlockSpec((None, rows, tail_len), lambda b: (b, 0, 0)),
            pl.BlockSpec((None, rows, block_samples.shape[2]), lambda b: (b, 0, 0)),
            table_spec,
            table_spec,
            table_spec,
        ],
        out_specs=pl.BlockSpec((None, rows, length), lambda b: (b, 0, 0)),
        out_shape=jax.ShapeDtypeStruct((beams_dev, rows, length), jnp.float32),
        scratch_shapes=[pltpu.VMEM((rows, length), jnp.float32)],
    )(tail_blocks.astype(jnp.int32), tail_samples, block_samples, entry, mid, leave)


def peaks_of(dm_rows, tail_len, block_len, leave):
    trials = dm_rows.shape[0]
    searched = dm_rows[:, tail_len:]
    average = jnp.sum(searched, axis=1, keepdims=True) / jnp.float32(block_len)
    spread = jnp.sum((searched - average) ** 2, axis=1, keepdims=True) / jnp.float32(block_len)
    deviation = jnp.sqrt(spread + jnp.float32(1e-05))
    boxcar = dm_rows[:, tail_len - 128 :]
    lane_ids = lax.broadcasted_iota(jnp.int32, (trials, 128), 1)
    table = jnp.zeros((trials, 128), jnp.float32)
    for width_bit in range(WIDTHS):
        width_now = 2**width_bit
        if width_bit > 0:
            boxcar = boxcar + pltpu.roll(boxcar, width_now // 2, 1)
        top = jnp.max(boxcar[:, 128:], axis=1, keepdims=True)
        ratio = (top - width_now * average) / (np.sqrt(np.float32(width_now)) * deviation)
        table = jnp.where(lane_ids == width_bit, ratio, table)
    return permute_rows(leave, table).T[:8]


def merge_tree(parts, first_trial, tail_len):
    beams_dev, subbands, trials, length = parts.shape
    rows = subbands * trials
    entry, mid, leave = tables(subbands, trials, TILE)

    def body(off_ref, x_ref, entry_ref, mid_ref, leave_ref, o_ref, buf):
        buf[...] = permute_rows(entry_ref[...], x_ref[...])
        tree_in_place(buf, mid_ref, subbands, trials, off_ref[0], TILE)
        o_ref[...] = peaks_of(buf[...], tail_len, length - tail_len, leave_ref[...])

    spec = pl.BlockSpec((None, rows, length), lambda b: (b, 0, 0))
    table_spec = pl.BlockSpec((rows, rows), lambda b: (0, 0))
    return pl.pallas_call(
        body,
        grid=(beams_dev,),
        in_specs=[pl.BlockSpec(memory_space=pltpu.SMEM), spec, table_spec, table_spec, table_spec],
        out_specs=pl.BlockSpec((None, 8, rows), lambda b: (b, 0, 0)),
        out_shape=jax.ShapeDtypeStruct((beams_dev, 8, rows), jnp.float32),
        scratch_shapes=[pltpu.VMEM((rows, length), jnp.float32)],
    )(
        jnp.reshape(first_trial, (1,)).astype(jnp.int32),
        parts.reshape(beams_dev, rows, length),
        entry,
        mid,
        leave,
    )[:, :WIDTHS]


def local(block_samples, tail_samples, tail_blocks, dm_limit):
    beams_dev, local_chan, block_len = block_samples.shape
    tail_len = tail_samples.shape[2]
    series = local_tree(tail_samples, block_samples, tail_blocks)[:, None]
    devices = lax.axis_size("freq")
    position = lax.axis_index("freq")
    series = lax.all_to_all(series, "freq", split_axis=2, concat_axis=1, tiled=True)
    per_dev = series.shape[2]
    scores = merge_tree(series, position * per_dev, tail_len)
    out_rows = scores.shape[-1]
    trial_ids = position * out_rows + jnp.arange(out_rows, dtype=jnp.int32)
    peak_snr = jnp.where(
        trial_ids[None, None, :] < dm_limit[:, None, None], scores, jnp.float32(0.0)
    )
    beam_total = jnp.sum(peak_snr, axis=0)
    beam_count = lax.axis_size("beam")
    for level_bit in range(beam_count.bit_length() - 1):
        pairs = [(i, i ^ (1 << level_bit)) for i in range(beam_count)]
        beam_total = beam_total + lax.ppermute(beam_total, "beam", pairs)
    excess_snr = peak_snr - beam_total[None] / (beams_dev * lax.axis_size("beam"))
    return (peak_snr, excess_snr)


def solution(mesh):
    return jax.shard_map(
        local,
        mesh=mesh,
        in_specs=(P("beam", "freq", None), P("beam", "freq", None), P("beam"), P("beam")),
        out_specs=(P("beam", None, "freq"), P("beam", None, "freq")),
        check_vma=False,
    )
```

```python
import jax
import jax.numpy as jnp
import numpy as np
from jax import lax
from jax.experimental import pallas as pl
from jax.experimental.pallas import tpu as pltpu
from jax.sharding import PartitionSpec as P

WIDTHS = 7


def partner_2(block, axis, stride):
    count = lax.axis_size(axis)
    route = []
    for low in range(count):
        high = low | 1 << stride
        if high != low and high < count:
            route += [(low, high), (high, low)]
    return lax.ppermute(block, axis, route)


def skew_rows(series, step_size, base_shift, pad_width):
    dims_of = series.shape
    rows_count = dims_of[-2]
    length_now = dims_of[-1]
    flattened = series.reshape((-1, rows_count, length_now))
    padded = jnp.pad(flattened, ((0, 0), (0, 0), (pad_width, 0)))
    row_width = length_now + pad_width
    lined_up = padded.reshape((flattened.shape[0], rows_count * row_width))
    lined_up = jnp.pad(lined_up, ((0, 0), (0, pad_width)))
    window = lax.dynamic_slice_in_dim(
        lined_up, pad_width - base_shift, rows_count * (row_width - step_size), axis=1
    )
    moved_rows = window.reshape((flattened.shape[0], rows_count, row_width - step_size))[
        :, :, :length_now
    ]
    return moved_rows.reshape(dims_of)


def tree_section(series, offset, reach_max):
    upper_rows = series[..., 0::2, :, :]
    odd_rows = series[..., 1::2, :, :]
    even_moved = skew_rows(odd_rows, 1, (offset + 1) // 2, reach_max)
    odd_moved = skew_rows(odd_rows, 1, (offset + 2) // 2, reach_max)
    joined_rows = jnp.stack([upper_rows + even_moved, upper_rows + odd_moved], axis=-2)
    dims_of = upper_rows.shape
    return joined_rows.reshape(dims_of[:-2] + (2 * dims_of[-2], dims_of[-1]))


def peak_ratios(series, tail_len):
    searched = series[..., tail_len:]
    average = jnp.mean(searched, axis=-1, keepdims=True)
    deviation = jnp.sqrt(jnp.mean((searched - average) ** 2, axis=-1, keepdims=True) + 1e-05)
    reach_back = 2 ** (WIDTHS - 1)
    boxcar = series[..., tail_len - reach_back :]
    results = []
    for width_bit in range(WIDTHS):
        width_now = 2**width_bit
        if width_bit > 0:
            half_width = width_now // 2
            pad_spec = [(0, 0)] * (series.ndim - 1) + [(half_width, 0)]
            boxcar = boxcar + jnp.pad(boxcar[..., :-half_width], pad_spec)
        ratio = (boxcar[..., reach_back:] - width_now * average) / (
            jnp.sqrt(jnp.float32(width_now)) * deviation
        )
        results.append(jnp.max(ratio, axis=-1))
    return jnp.stack(results, axis=-2)


def shift_in(row_block, amount, lanes, stride):
    if stride:
        moved = pltpu.roll(row_block, amount, 1, stride=stride, stride_axis=0)
        limit = lax.broadcasted_iota(jnp.int32, row_block.shape, 0) * stride + amount
    else:
        moved = pltpu.roll(row_block, amount, 1)
        limit = amount
    return jnp.where(lanes >= limit, moved, jnp.float32(0.0))


def permute_rows(matrix, rows):
    return jnp.dot(matrix, rows, precision=lax.Precision.HIGHEST, preferred_element_type=jnp.float32)


def swap_blocks(rows, tile):
    length = rows.shape[1]
    blocks = rows.reshape(tile, tile, length)
    return pltpu.einshape("abt->bat", blocks).reshape(tile * tile, length)


def tree_in_place(buf, mid_ref, subbands, trials, first_trial, tile):
    length = buf.shape[1]
    while subbands > 1 and subbands // 2 >= tile:
        half = subbands // 2
        lanes = lax.broadcasted_iota(jnp.int32, (half, length), 1)
        for k in range(trials):
            top = k * subbands
            upper = buf[top : top + half, :]
            lower = buf[top + half : top + subbands, :]
            buf[top : top + half, :] = upper + shift_in(lower, first_trial + k, lanes, 0)
            buf[top + half : top + subbands, :] = upper + shift_in(
                lower, first_trial + k + 1, lanes, 0
            )
        subbands = half
        trials = 2 * trials
        first_trial = 2 * first_trial
    if subbands == tile and buf.shape[0] == tile * tile:
        buf[...] = swap_blocks(buf[...], tile)
    else:
        buf[...] = permute_rows(mid_ref[...], buf[...])
    groups, step = 1, 1
    lanes = lax.broadcasted_iota(jnp.int32, (tile, length), 1)
    if not isinstance(first_trial, int):
        order = bit_reversed(subbands)
        for pos in range(subbands):
            rows = slice(pos * tile, (pos + 1) * tile)
            buf[rows, :] = shift_in(buf[rows, :], first_trial * int(order[pos]), lanes, 0)
        first_trial = 0
    while subbands > 1:
        half = subbands // 2
        for group in range(groups):
            for pos in range(half):
                top = (group * subbands + pos) * tile
                low = (group * subbands + pos + half) * tile
                upper = buf[top : top + tile, :]
                lower = buf[low : low + tile, :]
                buf[top : top + tile, :] = upper + shift_in(lower, first_trial + group, lanes, step)
                buf[low : low + tile, :] = upper + shift_in(
                    lower, first_trial + group + 1, lanes, step
                )
        subbands = half
        groups = 2 * groups
        step = 2 * step
        first_trial = 2 * first_trial
    return groups


def bit_reversed(count):
    bits = count.bit_length() - 1
    return np.array([int(format(i, f"0{bits}b")[::-1], 2) for i in range(count)], np.int32)


def one_hot(targets):
    return np.eye(len(targets), dtype=np.float32)[targets]


def tables(subbands, trials, tile):
    rows = subbands * trials
    order = bit_reversed(subbands)
    entry = one_hot([order[r % subbands] * trials + r // subbands for r in range(rows)])
    at_switch = rows // tile
    mid = one_hot([(r % tile) * at_switch + r // tile for r in range(rows)])
    groups = rows // tile
    leave = one_hot([(d % groups) * tile + d // groups for d in range(rows)])
    return entry, mid, leave


TILE = 8


def local_tree(tail_samples, block_samples, tail_blocks):
    beams_dev, rows, tail_len = tail_samples.shape
    length = tail_len + block_samples.shape[2]
    entry, mid, leave = tables(rows, 1, TILE)

    def body(count_ref, tail_ref, block_ref, entry_ref, mid_ref, leave_ref, o_ref, buf):
        beam = pl.program_id(0)
        lanes = lax.broadcasted_iota(jnp.int32, (rows, tail_len), 1)
        keep = lanes >= tail_len - 128 * count_ref[beam]
        order = entry_ref[...].astype(jnp.bfloat16)
        tail = jnp.dot(order, tail_ref[...], preferred_element_type=jnp.float32)
        buf[:, :tail_len] = jnp.where(keep, tail, jnp.float32(0.0))
        buf[:, tail_len:] = jnp.dot(order, block_ref[...], preferred_element_type=jnp.float32)
        tree_in_place(buf, mid_ref, rows, 1, 0, TILE)
        o_ref[...] = swap_blocks(buf[...], TILE)

    table_spec = pl.BlockSpec((rows, rows), lambda b: (0, 0))
    return pl.pallas_call(
        body,
        grid=(beams_dev,),
        in_specs=[
            pl.BlockSpec(memory_space=pltpu.SMEM),
            pl.BlockSpec((None, rows, tail_len), lambda b: (b, 0, 0)),
            pl.BlockSpec((None, rows, block_samples.shape[2]), lambda b: (b, 0, 0)),
            table_spec,
            table_spec,
            table_spec,
        ],
        out_specs=pl.BlockSpec((None, rows, length), lambda b: (b, 0, 0)),
        out_shape=jax.ShapeDtypeStruct((beams_dev, rows, length), jnp.float32),
        scratch_shapes=[pltpu.VMEM((rows, length), jnp.float32)],
    )(tail_blocks.astype(jnp.int32), tail_samples, block_samples, entry, mid, leave)


def peaks_of(dm_rows, tail_len, block_len, leave):
    trials = dm_rows.shape[0]
    searched = dm_rows[:, tail_len:]
    average = jnp.sum(searched, axis=1, keepdims=True) / jnp.float32(block_len)
    spread = jnp.sum((searched - average) ** 2, axis=1, keepdims=True) / jnp.float32(block_len)
    deviation = jnp.sqrt(spread + jnp.float32(1e-05))
    boxcar = dm_rows[:, tail_len - 128 :]
    lane_ids = lax.broadcasted_iota(jnp.int32, (trials, 128), 1)
    table = jnp.zeros((trials, 128), jnp.float32)
    for width_bit in range(WIDTHS):
        width_now = 2**width_bit
        if width_bit > 0:
            boxcar = boxcar + pltpu.roll(boxcar, width_now // 2, 1)
        top = jnp.max(boxcar[:, 128:], axis=1, keepdims=True)
        ratio = (top - width_now * average) / (np.sqrt(np.float32(width_now)) * deviation)
        table = jnp.where(lane_ids == width_bit, ratio, table)
    return permute_rows(leave, table).T[:8]


def merge_tree(parts, first_trial, tail_len):
    beams_dev, subbands, trials, length = parts.shape
    rows = subbands * trials
    entry, mid, leave = tables(subbands, trials, TILE)

    def body(off_ref, x_ref, entry_ref, mid_ref, leave_ref, o_ref, buf):
        buf[...] = permute_rows(entry_ref[...], x_ref[...])
        tree_in_place(buf, mid_ref, subbands, trials, off_ref[0], TILE)
        o_ref[...] = peaks_of(buf[...], tail_len, length - tail_len, leave_ref[...])

    spec = pl.BlockSpec((None, rows, length), lambda b: (b, 0, 0))
    table_spec = pl.BlockSpec((rows, rows), lambda b: (0, 0))
    return pl.pallas_call(
        body,
        grid=(beams_dev,),
        in_specs=[pl.BlockSpec(memory_space=pltpu.SMEM), spec, table_spec, table_spec, table_spec],
        out_specs=pl.BlockSpec((None, 8, rows), lambda b: (b, 0, 0)),
        out_shape=jax.ShapeDtypeStruct((beams_dev, 8, rows), jnp.float32),
        scratch_shapes=[pltpu.VMEM((rows, length), jnp.float32)],
    )(
        jnp.reshape(first_trial, (1,)).astype(jnp.int32),
        parts.reshape(beams_dev, rows, length),
        entry,
        mid,
        leave,
    )[:, :WIDTHS]


def local(block_samples, tail_samples, tail_blocks, dm_limit):
    beams_dev, local_chan, block_len = block_samples.shape
    tail_len = tail_samples.shape[2]
    series = local_tree(tail_samples, block_samples, tail_blocks)[:, None]
    devices = lax.axis_size("freq")
    position = lax.axis_index("freq")
    series = lax.all_to_all(series, "freq", split_axis=2, concat_axis=1, tiled=True)
    per_dev = series.shape[2]
    scores = merge_tree(series, position * per_dev, tail_len)
    out_rows = scores.shape[-1]
    trial_ids = position * out_rows + jnp.arange(out_rows, dtype=jnp.int32)
    peak_snr = jnp.where(
        trial_ids[None, None, :] < dm_limit[:, None, None], scores, jnp.float32(0.0)
    )
    beam_total = jnp.sum(peak_snr, axis=0)
    beam_count = lax.axis_size("beam")
    for level_bit in range(beam_count.bit_length() - 1):
        pairs = [(i, i ^ (1 << level_bit)) for i in range(beam_count)]
        beam_total = beam_total + lax.ppermute(beam_total, "beam", pairs)
    excess_snr = peak_snr - beam_total[None] / (beams_dev * lax.axis_size("beam"))
    return (peak_snr, excess_snr)


def solution(mesh):
    return jax.shard_map(
        local,
        mesh=mesh,
        in_specs=(P("beam", "freq", None), P("beam", "freq", None), P("beam"), P("beam")),
        out_specs=(P("beam", None, "freq"), P("beam", None, "freq")),
        check_vma=False,
    )
```

```python
import jax
import jax.numpy as jnp
import numpy as np
from jax import lax
from jax.experimental import pallas as pl
from jax.experimental.pallas import tpu as pltpu
from jax.sharding import PartitionSpec as P

WIDTHS = 7


def partner_2(block, axis, stride):
    count = lax.axis_size(axis)
    route = []
    for low in range(count):
        high = low | 1 << stride
        if high != low and high < count:
            route += [(low, high), (high, low)]
    return lax.ppermute(block, axis, route)


def skew_rows(series, step_size, base_shift, pad_width):
    dims_of = series.shape
    rows_count = dims_of[-2]
    length_now = dims_of[-1]
    flattened = series.reshape((-1, rows_count, length_now))
    padded = jnp.pad(flattened, ((0, 0), (0, 0), (pad_width, 0)))
    row_width = length_now + pad_width
    lined_up = padded.reshape((flattened.shape[0], rows_count * row_width))
    lined_up = jnp.pad(lined_up, ((0, 0), (0, pad_width)))
    window = lax.dynamic_slice_in_dim(
        lined_up, pad_width - base_shift, rows_count * (row_width - step_size), axis=1
    )
    moved_rows = window.reshape((flattened.shape[0], rows_count, row_width - step_size))[
        :, :, :length_now
    ]
    return moved_rows.reshape(dims_of)


def tree_section(series, offset, reach_max):
    upper_rows = series[..., 0::2, :, :]
    odd_rows = series[..., 1::2, :, :]
    even_moved = skew_rows(odd_rows, 1, (offset + 1) // 2, reach_max)
    odd_moved = skew_rows(odd_rows, 1, (offset + 2) // 2, reach_max)
    joined_rows = jnp.stack([upper_rows + even_moved, upper_rows + odd_moved], axis=-2)
    dims_of = upper_rows.shape
    return joined_rows.reshape(dims_of[:-2] + (2 * dims_of[-2], dims_of[-1]))


def peak_ratios(series, tail_len):
    searched = series[..., tail_len:]
    average = jnp.mean(searched, axis=-1, keepdims=True)
    deviation = jnp.sqrt(jnp.mean((searched - average) ** 2, axis=-1, keepdims=True) + 1e-05)
    reach_back = 2 ** (WIDTHS - 1)
    boxcar = series[..., tail_len - reach_back :]
    results = []
    for width_bit in range(WIDTHS):
        width_now = 2**width_bit
        if width_bit > 0:
            half_width = width_now // 2
            pad_spec = [(0, 0)] * (series.ndim - 1) + [(half_width, 0)]
            boxcar = boxcar + jnp.pad(boxcar[..., :-half_width], pad_spec)
        ratio = (boxcar[..., reach_back:] - width_now * average) / (
            jnp.sqrt(jnp.float32(width_now)) * deviation
        )
        results.append(jnp.max(ratio, axis=-1))
    return jnp.stack(results, axis=-2)


def shift_in(row_block, amount, lanes, stride):
    if stride:
        moved = pltpu.roll(row_block, amount, 1, stride=stride, stride_axis=0)
        limit = lax.broadcasted_iota(jnp.int32, row_block.shape, 0) * stride + amount
    else:
        moved = pltpu.roll(row_block, amount, 1)
        limit = amount
    return jnp.where(lanes >= limit, moved, jnp.float32(0.0))


def permute_rows(matrix, rows):
    return jnp.dot(matrix, rows, precision=lax.Precision.HIGHEST, preferred_element_type=jnp.float32)


def swap_blocks(rows, tile):
    length = rows.shape[1]
    blocks = rows.reshape(tile, tile, length)
    return pltpu.einshape("abt->bat", blocks).reshape(tile * tile, length)


def tree_in_place(buf, mid_ref, subbands, trials, first_trial, tile):
    length = buf.shape[1]
    while subbands > 1 and subbands // 2 >= tile:
        half = subbands // 2
        lanes = lax.broadcasted_iota(jnp.int32, (half, length), 1)
        for k in range(trials):
            top = k * subbands
            upper = buf[top : top + half, :]
            lower = buf[top + half : top + subbands, :]
            buf[top : top + half, :] = upper + shift_in(lower, first_trial + k, lanes, 0)
            buf[top + half : top + subbands, :] = upper + shift_in(
                lower, first_trial + k + 1, lanes, 0
            )
        subbands = half
        trials = 2 * trials
        first_trial = 2 * first_trial
    if subbands == tile and buf.shape[0] == tile * tile:
        buf[...] = swap_blocks(buf[...], tile)
    else:
        buf[...] = permute_rows(mid_ref[...], buf[...])
    groups, step = 1, 1
    lanes = lax.broadcasted_iota(jnp.int32, (tile, length), 1)
    if not isinstance(first_trial, int):
        order = bit_reversed(subbands)
        for pos in range(subbands):
            rows = slice(pos * tile, (pos + 1) * tile)
            buf[rows, :] = shift_in(buf[rows, :], first_trial * int(order[pos]), lanes, 0)
        first_trial = 0
    while subbands > 1:
        half = subbands // 2
        for group in range(groups):
            for pos in range(half):
                top = (group * subbands + pos) * tile
                low = (group * subbands + pos + half) * tile
                upper = buf[top : top + tile, :]
                lower = buf[low : low + tile, :]
                buf[top : top + tile, :] = upper + shift_in(lower, first_trial + group, lanes, step)
                buf[low : low + tile, :] = upper + shift_in(
                    lower, first_trial + group + 1, lanes, step
                )
        subbands = half
        groups = 2 * groups
        step = 2 * step
        first_trial = 2 * first_trial
    return groups


def bit_reversed(count):
    bits = count.bit_length() - 1
    return np.array([int(format(i, f"0{bits}b")[::-1], 2) for i in range(count)], np.int32)


def one_hot(targets):
    return np.eye(len(targets), dtype=np.float32)[targets]


def tables(subbands, trials, tile):
    rows = subbands * trials
    order = bit_reversed(subbands)
    entry = one_hot([order[r % subbands] * trials + r // subbands for r in range(rows)])
    at_switch = rows // tile
    mid = one_hot([(r % tile) * at_switch + r // tile for r in range(rows)])
    groups = rows // tile
    leave = one_hot([(d % groups) * tile + d // groups for d in range(rows)])
    return entry, mid, leave


TILE = 8


def local_tree(tail_samples, block_samples, tail_blocks):
    beams_dev, rows, tail_len = tail_samples.shape
    length = tail_len + block_samples.shape[2]
    entry, mid, leave = tables(rows, 1, TILE)

    def body(count_ref, tail_ref, block_ref, entry_ref, mid_ref, leave_ref, o_ref, buf):
        beam = pl.program_id(0)
        lanes = lax.broadcasted_iota(jnp.int32, (rows, tail_len), 1)
        keep = lanes >= tail_len - 128 * count_ref[beam]
        order = entry_ref[...].astype(jnp.bfloat16)
        tail = jnp.dot(order, tail_ref[...], preferred_element_type=jnp.float32)
        buf[:, :tail_len] = jnp.where(keep, tail, jnp.float32(0.0))
        buf[:, tail_len:] = jnp.dot(order, block_ref[...], preferred_element_type=jnp.float32)
        tree_in_place(buf, mid_ref, rows, 1, 0, TILE)
        o_ref[...] = swap_blocks(buf[...], TILE)

    table_spec = pl.BlockSpec((rows, rows), lambda b: (0, 0))
    return pl.pallas_call(
        body,
        grid=(beams_dev,),
        in_specs=[
            pl.BlockSpec(memory_space=pltpu.SMEM),
            pl.BlockSpec((None, rows, tail_len), lambda b: (b, 0, 0)),
            pl.BlockSpec((None, rows, block_samples.shape[2]), lambda b: (b, 0, 0)),
            table_spec,
            table_spec,
            table_spec,
        ],
        out_specs=pl.BlockSpec((None, rows, length), lambda b: (b, 0, 0)),
        out_shape=jax.ShapeDtypeStruct((beams_dev, rows, length), jnp.float32),
        scratch_shapes=[pltpu.VMEM((rows, length), jnp.float32)],
    )(tail_blocks.astype(jnp.int32), tail_samples, block_samples, entry, mid, leave)


def peaks_of(dm_rows, tail_len, block_len, leave):
    trials = dm_rows.shape[0]
    searched = dm_rows[:, tail_len:]
    average = jnp.sum(searched, axis=1, keepdims=True) / jnp.float32(block_len)
    spread = jnp.sum((searched - average) ** 2, axis=1, keepdims=True) / jnp.float32(block_len)
    deviation = jnp.sqrt(spread + jnp.float32(1e-05))
    boxcar = dm_rows[:, tail_len - 128 :]
    lane_ids = lax.broadcasted_iota(jnp.int32, (trials, 128), 1)
    table = jnp.zeros((trials, 128), jnp.float32)
    for width_bit in range(WIDTHS):
        width_now = 2**width_bit
        if width_bit > 0:
            boxcar = boxcar + pltpu.roll(boxcar, width_now // 2, 1)
        top = jnp.max(boxcar[:, 128:], axis=1, keepdims=True)
        ratio = (top - width_now * average) / (np.sqrt(np.float32(width_now)) * deviation)
        table = jnp.where(lane_ids == width_bit, ratio, table)
    return permute_rows(leave, table).T[:8]


def trial_major(parts):
    beams_dev, subbands, trials, length = parts.shape
    bits = subbands.bit_length() - 1
    split = parts.reshape((beams_dev,) + (2,) * bits + (trials, length))
    order = (0, bits + 1) + tuple(range(bits, 0, -1)) + (bits + 2,)
    return jnp.transpose(split, order).reshape(beams_dev, subbands * trials, length)


def merge_tree(parts, first_trial, tail_len):
    beams_dev, subbands, trials, length = parts.shape
    rows = subbands * trials
    entry, mid, leave = tables(subbands, trials, TILE)

    def body(off_ref, x_ref, entry_ref, mid_ref, leave_ref, o_ref, buf):
        buf[...] = x_ref[...]
        tree_in_place(buf, mid_ref, subbands, trials, off_ref[0], TILE)
        o_ref[...] = peaks_of(buf[...], tail_len, length - tail_len, leave_ref[...])

    spec = pl.BlockSpec((None, rows, length), lambda b: (b, 0, 0))
    table_spec = pl.BlockSpec((rows, rows), lambda b: (0, 0))
    return pl.pallas_call(
        body,
        grid=(beams_dev,),
        in_specs=[pl.BlockSpec(memory_space=pltpu.SMEM), spec, table_spec, table_spec, table_spec],
        out_specs=pl.BlockSpec((None, 8, rows), lambda b: (b, 0, 0)),
        out_shape=jax.ShapeDtypeStruct((beams_dev, 8, rows), jnp.float32),
        scratch_shapes=[pltpu.VMEM((rows, length), jnp.float32)],
    )(
        jnp.reshape(first_trial, (1,)).astype(jnp.int32),
        trial_major(parts),
        entry,
        mid,
        leave,
    )[:, :WIDTHS]


def local(block_samples, tail_samples, tail_blocks, dm_limit):
    beams_dev, local_chan, block_len = block_samples.shape
    tail_len = tail_samples.shape[2]
    series = local_tree(tail_samples, block_samples, tail_blocks)[:, None]
    devices = lax.axis_size("freq")
    position = lax.axis_index("freq")
    series = lax.all_to_all(series, "freq", split_axis=2, concat_axis=1, tiled=True)
    per_dev = series.shape[2]
    scores = merge_tree(series, position * per_dev, tail_len)
    out_rows = scores.shape[-1]
    trial_ids = position * out_rows + jnp.arange(out_rows, dtype=jnp.int32)
    peak_snr = jnp.where(
        trial_ids[None, None, :] < dm_limit[:, None, None], scores, jnp.float32(0.0)
    )
    beam_total = jnp.sum(peak_snr, axis=0)
    beam_count = lax.axis_size("beam")
    for level_bit in range(beam_count.bit_length() - 1):
        pairs = [(i, i ^ (1 << level_bit)) for i in range(beam_count)]
        beam_total = beam_total + lax.ppermute(beam_total, "beam", pairs)
    excess_snr = peak_snr - beam_total[None] / (beams_dev * lax.axis_size("beam"))
    return (peak_snr, excess_snr)


def solution(mesh):
    return jax.shard_map(
        local,
        mesh=mesh,
        in_specs=(P("beam", "freq", None), P("beam", "freq", None), P("beam"), P("beam")),
        out_specs=(P("beam", None, "freq"), P("beam", None, "freq")),
        check_vma=False,
    )
```

```python
import jax
import jax.numpy as jnp
import numpy as np
from jax import lax
from jax.experimental import pallas as pl
from jax.experimental.pallas import tpu as pltpu
from jax.sharding import PartitionSpec as P

WIDTHS = 7


def partner_2(block, axis, stride):
    count = lax.axis_size(axis)
    route = []
    for low in range(count):
        high = low | 1 << stride
        if high != low and high < count:
            route += [(low, high), (high, low)]
    return lax.ppermute(block, axis, route)


def skew_rows(series, step_size, base_shift, pad_width):
    dims_of = series.shape
    rows_count = dims_of[-2]
    length_now = dims_of[-1]
    flattened = series.reshape((-1, rows_count, length_now))
    padded = jnp.pad(flattened, ((0, 0), (0, 0), (pad_width, 0)))
    row_width = length_now + pad_width
    lined_up = padded.reshape((flattened.shape[0], rows_count * row_width))
    lined_up = jnp.pad(lined_up, ((0, 0), (0, pad_width)))
    window = lax.dynamic_slice_in_dim(
        lined_up, pad_width - base_shift, rows_count * (row_width - step_size), axis=1
    )
    moved_rows = window.reshape((flattened.shape[0], rows_count, row_width - step_size))[
        :, :, :length_now
    ]
    return moved_rows.reshape(dims_of)


def tree_section(series, offset, reach_max):
    upper_rows = series[..., 0::2, :, :]
    odd_rows = series[..., 1::2, :, :]
    even_moved = skew_rows(odd_rows, 1, (offset + 1) // 2, reach_max)
    odd_moved = skew_rows(odd_rows, 1, (offset + 2) // 2, reach_max)
    joined_rows = jnp.stack([upper_rows + even_moved, upper_rows + odd_moved], axis=-2)
    dims_of = upper_rows.shape
    return joined_rows.reshape(dims_of[:-2] + (2 * dims_of[-2], dims_of[-1]))


def peak_ratios(series, tail_len):
    searched = series[..., tail_len:]
    average = jnp.mean(searched, axis=-1, keepdims=True)
    deviation = jnp.sqrt(jnp.mean((searched - average) ** 2, axis=-1, keepdims=True) + 1e-05)
    reach_back = 2 ** (WIDTHS - 1)
    boxcar = series[..., tail_len - reach_back :]
    results = []
    for width_bit in range(WIDTHS):
        width_now = 2**width_bit
        if width_bit > 0:
            half_width = width_now // 2
            pad_spec = [(0, 0)] * (series.ndim - 1) + [(half_width, 0)]
            boxcar = boxcar + jnp.pad(boxcar[..., :-half_width], pad_spec)
        ratio = (boxcar[..., reach_back:] - width_now * average) / (
            jnp.sqrt(jnp.float32(width_now)) * deviation
        )
        results.append(jnp.max(ratio, axis=-1))
    return jnp.stack(results, axis=-2)


def shift_in(row_block, amount, lanes, stride):
    if stride:
        moved = pltpu.roll(row_block, amount, 1, stride=stride, stride_axis=0)
        limit = lax.broadcasted_iota(jnp.int32, row_block.shape, 0) * stride + amount
    else:
        moved = pltpu.roll(row_block, amount, 1)
        limit = amount
    return jnp.where(lanes >= limit, moved, jnp.float32(0.0))


def permute_rows(matrix, rows):
    return jnp.dot(matrix, rows, precision=lax.Precision.HIGHEST, preferred_element_type=jnp.float32)


def swap_blocks(rows, tile):
    length = rows.shape[1]
    blocks = rows.reshape(tile, tile, length)
    return pltpu.einshape("abt->bat", blocks).reshape(tile * tile, length)


def tree_in_place(buf, mid_ref, subbands, trials, first_trial, tile):
    length = buf.shape[1]
    while subbands > 1 and subbands // 2 >= tile:
        half = subbands // 2
        lanes = lax.broadcasted_iota(jnp.int32, (half, length), 1)
        for k in range(trials):
            top = k * subbands
            upper = buf[top : top + half, :]
            lower = buf[top + half : top + subbands, :]
            buf[top : top + half, :] = upper + shift_in(lower, first_trial + k, lanes, 0)
            buf[top + half : top + subbands, :] = upper + shift_in(
                lower, first_trial + k + 1, lanes, 0
            )
        subbands = half
        trials = 2 * trials
        first_trial = 2 * first_trial
    if subbands == tile and buf.shape[0] == tile * tile:
        buf[...] = swap_blocks(buf[...], tile)
    else:
        buf[...] = permute_rows(mid_ref[...], buf[...])
    groups, step = 1, 1
    lanes = lax.broadcasted_iota(jnp.int32, (tile, length), 1)
    if not isinstance(first_trial, int):
        order = bit_reversed(subbands)
        for pos in range(subbands):
            rows = slice(pos * tile, (pos + 1) * tile)
            buf[rows, :] = shift_in(buf[rows, :], first_trial * int(order[pos]), lanes, 0)
        first_trial = 0
    while subbands > 1:
        half = subbands // 2
        for group in range(groups):
            for pos in range(half):
                top = (group * subbands + pos) * tile
                low = (group * subbands + pos + half) * tile
                upper = buf[top : top + tile, :]
                lower = buf[low : low + tile, :]
                buf[top : top + tile, :] = upper + shift_in(lower, first_trial + group, lanes, step)
                buf[low : low + tile, :] = upper + shift_in(
                    lower, first_trial + group + 1, lanes, step
                )
        subbands = half
        groups = 2 * groups
        step = 2 * step
        first_trial = 2 * first_trial
    return groups


def bit_reversed(count):
    bits = count.bit_length() - 1
    return np.array([int(format(i, f"0{bits}b")[::-1], 2) for i in range(count)], np.int32)


def one_hot(targets):
    return np.eye(len(targets), dtype=np.float32)[targets]


def tables(subbands, trials, tile):
    rows = subbands * trials
    order = bit_reversed(subbands)
    entry = one_hot([order[r % subbands] * trials + r // subbands for r in range(rows)])
    at_switch = rows // tile
    mid = one_hot([(r % tile) * at_switch + r // tile for r in range(rows)])
    groups = rows // tile
    leave = one_hot([(d % groups) * tile + d // groups for d in range(rows)])
    return entry, mid, leave


TILE = 8


def local_tree(tail_samples, block_samples, tail_blocks):
    beams_dev, rows, tail_len = tail_samples.shape
    length = tail_len + block_samples.shape[2]
    entry, mid, leave = tables(rows, 1, TILE)

    def body(count_ref, tail_ref, block_ref, entry_ref, mid_ref, leave_ref, o_ref, buf):
        beam = pl.program_id(0)
        lanes = lax.broadcasted_iota(jnp.int32, (rows, tail_len), 1)
        keep = lanes >= tail_len - 128 * count_ref[beam]
        order = entry_ref[...].astype(jnp.bfloat16)
        tail = jnp.dot(order, tail_ref[...], preferred_element_type=jnp.float32)
        buf[:, :tail_len] = jnp.where(keep, tail, jnp.float32(0.0))
        buf[:, tail_len:] = jnp.dot(order, block_ref[...], preferred_element_type=jnp.float32)
        tree_in_place(buf, mid_ref, rows, 1, 0, TILE)
        buf[...] = swap_blocks(buf[...], TILE)
        for r in range(rows):
            o_ref[r] = buf[r : r + 1, :]

    table_spec = pl.BlockSpec((rows, rows), lambda b: (0, 0))
    return pl.pallas_call(
        body,
        grid=(beams_dev,),
        in_specs=[
            pl.BlockSpec(memory_space=pltpu.SMEM),
            pl.BlockSpec((None, rows, tail_len), lambda b: (b, 0, 0)),
            pl.BlockSpec((None, rows, block_samples.shape[2]), lambda b: (b, 0, 0)),
            table_spec,
            table_spec,
            table_spec,
        ],
        out_specs=pl.BlockSpec((None, rows, 1, length), lambda b: (b, 0, 0, 0)),
        out_shape=jax.ShapeDtypeStruct((beams_dev, rows, 1, length), jnp.float32),
        scratch_shapes=[pltpu.VMEM((rows, length), jnp.float32)],
    )(tail_blocks.astype(jnp.int32), tail_samples, block_samples, entry, mid, leave).reshape(
        beams_dev, rows, length
    )


def peaks_of(dm_rows, tail_len, block_len, leave):
    trials = dm_rows.shape[0]
    searched = dm_rows[:, tail_len:]
    average = jnp.sum(searched, axis=1, keepdims=True) / jnp.float32(block_len)
    spread = jnp.sum((searched - average) ** 2, axis=1, keepdims=True) / jnp.float32(block_len)
    deviation = jnp.sqrt(spread + jnp.float32(1e-05))
    boxcar = dm_rows[:, tail_len - 128 :]
    lane_ids = lax.broadcasted_iota(jnp.int32, (trials, 128), 1)
    table = jnp.zeros((trials, 128), jnp.float32)
    for width_bit in range(WIDTHS):
        width_now = 2**width_bit
        if width_bit > 0:
            boxcar = boxcar + pltpu.roll(boxcar, width_now // 2, 1)
        top = jnp.max(boxcar[:, 128:], axis=1, keepdims=True)
        ratio = (top - width_now * average) / (np.sqrt(np.float32(width_now)) * deviation)
        table = jnp.where(lane_ids == width_bit, ratio, table)
    return permute_rows(leave, table).T[:8]


def merge_tree(parts, first_trial, tail_len):
    beams_dev, subbands, trials, length = parts.shape
    rows = subbands * trials
    entry, mid, leave = tables(subbands, trials, TILE)

    def body(off_ref, x_ref, entry_ref, mid_ref, leave_ref, o_ref, buf):
        buf[...] = permute_rows(entry_ref[...], x_ref[...])
        tree_in_place(buf, mid_ref, subbands, trials, off_ref[0], TILE)
        o_ref[...] = peaks_of(buf[...], tail_len, length - tail_len, leave_ref[...])

    spec = pl.BlockSpec((None, rows, length), lambda b: (b, 0, 0))
    table_spec = pl.BlockSpec((rows, rows), lambda b: (0, 0))
    return pl.pallas_call(
        body,
        grid=(beams_dev,),
        in_specs=[pl.BlockSpec(memory_space=pltpu.SMEM), spec, table_spec, table_spec, table_spec],
        out_specs=pl.BlockSpec((None, 8, rows), lambda b: (b, 0, 0)),
        out_shape=jax.ShapeDtypeStruct((beams_dev, 8, rows), jnp.float32),
        scratch_shapes=[pltpu.VMEM((rows, length), jnp.float32)],
    )(
        jnp.reshape(first_trial, (1,)).astype(jnp.int32),
        parts.reshape(beams_dev, rows, length),
        entry,
        mid,
        leave,
    )[:, :WIDTHS]


def local(block_samples, tail_samples, tail_blocks, dm_limit):
    beams_dev, local_chan, block_len = block_samples.shape
    tail_len = tail_samples.shape[2]
    series = local_tree(tail_samples, block_samples, tail_blocks)[:, None]
    devices = lax.axis_size("freq")
    position = lax.axis_index("freq")
    series = lax.all_to_all(series, "freq", split_axis=2, concat_axis=1, tiled=True)
    per_dev = series.shape[2]
    scores = merge_tree(series, position * per_dev, tail_len)
    out_rows = scores.shape[-1]
    trial_ids = position * out_rows + jnp.arange(out_rows, dtype=jnp.int32)
    peak_snr = jnp.where(
        trial_ids[None, None, :] < dm_limit[:, None, None], scores, jnp.float32(0.0)
    )
    beam_total = jnp.sum(peak_snr, axis=0)
    beam_count = lax.axis_size("beam")
    for level_bit in range(beam_count.bit_length() - 1):
        pairs = [(i, i ^ (1 << level_bit)) for i in range(beam_count)]
        beam_total = beam_total + lax.ppermute(beam_total, "beam", pairs)
    excess_snr = peak_snr - beam_total[None] / (beams_dev * lax.axis_size("beam"))
    return (peak_snr, excess_snr)


def solution(mesh):
    return jax.shard_map(
        local,
        mesh=mesh,
        in_specs=(P("beam", "freq", None), P("beam", "freq", None), P("beam"), P("beam")),
        out_specs=(P("beam", None, "freq"), P("beam", None, "freq")),
        check_vma=False,
    )
```

```python
import jax
import jax.numpy as jnp
import numpy as np
from jax import lax
from jax.experimental import pallas as pl
from jax.experimental.pallas import tpu as pltpu
from jax.sharding import PartitionSpec as P

WIDTHS = 7


def partner_2(block, axis, stride):
    count = lax.axis_size(axis)
    route = []
    for low in range(count):
        high = low | 1 << stride
        if high != low and high < count:
            route += [(low, high), (high, low)]
    return lax.ppermute(block, axis, route)


def skew_rows(series, step_size, base_shift, pad_width):
    dims_of = series.shape
    rows_count = dims_of[-2]
    length_now = dims_of[-1]
    flattened = series.reshape((-1, rows_count, length_now))
    padded = jnp.pad(flattened, ((0, 0), (0, 0), (pad_width, 0)))
    row_width = length_now + pad_width
    lined_up = padded.reshape((flattened.shape[0], rows_count * row_width))
    lined_up = jnp.pad(lined_up, ((0, 0), (0, pad_width)))
    window = lax.dynamic_slice_in_dim(
        lined_up, pad_width - base_shift, rows_count * (row_width - step_size), axis=1
    )
    moved_rows = window.reshape((flattened.shape[0], rows_count, row_width - step_size))[
        :, :, :length_now
    ]
    return moved_rows.reshape(dims_of)


def tree_section(series, offset, reach_max):
    upper_rows = series[..., 0::2, :, :]
    odd_rows = series[..., 1::2, :, :]
    even_moved = skew_rows(odd_rows, 1, (offset + 1) // 2, reach_max)
    odd_moved = skew_rows(odd_rows, 1, (offset + 2) // 2, reach_max)
    joined_rows = jnp.stack([upper_rows + even_moved, upper_rows + odd_moved], axis=-2)
    dims_of = upper_rows.shape
    return joined_rows.reshape(dims_of[:-2] + (2 * dims_of[-2], dims_of[-1]))


def peak_ratios(series, tail_len):
    searched = series[..., tail_len:]
    average = jnp.mean(searched, axis=-1, keepdims=True)
    deviation = jnp.sqrt(jnp.mean((searched - average) ** 2, axis=-1, keepdims=True) + 1e-05)
    reach_back = 2 ** (WIDTHS - 1)
    boxcar = series[..., tail_len - reach_back :]
    results = []
    for width_bit in range(WIDTHS):
        width_now = 2**width_bit
        if width_bit > 0:
            half_width = width_now // 2
            pad_spec = [(0, 0)] * (series.ndim - 1) + [(half_width, 0)]
            boxcar = boxcar + jnp.pad(boxcar[..., :-half_width], pad_spec)
        ratio = (boxcar[..., reach_back:] - width_now * average) / (
            jnp.sqrt(jnp.float32(width_now)) * deviation
        )
        results.append(jnp.max(ratio, axis=-1))
    return jnp.stack(results, axis=-2)


def shift_in(row_block, amount, lanes, stride):
    if stride:
        moved = pltpu.roll(row_block, amount, 1, stride=stride, stride_axis=0)
        limit = lax.broadcasted_iota(jnp.int32, row_block.shape, 0) * stride + amount
    else:
        moved = pltpu.roll(row_block, amount, 1)
        limit = amount
    return jnp.where(lanes >= limit, moved, jnp.float32(0.0))


def permute_rows(matrix, rows):
    return jnp.dot(matrix, rows, precision=lax.Precision.HIGHEST, preferred_element_type=jnp.float32)


def swap_blocks(rows, tile):
    length = rows.shape[1]
    blocks = rows.reshape(tile, tile, length)
    return pltpu.einshape("abt->bat", blocks).reshape(tile * tile, length)


def tree_in_place(buf, mid_ref, subbands, trials, first_trial, tile):
    length = buf.shape[1]
    while subbands > 1 and subbands // 2 >= tile:
        half = subbands // 2
        lanes = lax.broadcasted_iota(jnp.int32, (half, length), 1)
        for k in range(trials):
            top = k * subbands
            upper = buf[top : top + half, :]
            lower = buf[top + half : top + subbands, :]
            buf[top : top + half, :] = upper + shift_in(lower, first_trial + k, lanes, 0)
            buf[top + half : top + subbands, :] = upper + shift_in(
                lower, first_trial + k + 1, lanes, 0
            )
        subbands = half
        trials = 2 * trials
        first_trial = 2 * first_trial
    if subbands == tile and buf.shape[0] == tile * tile:
        buf[...] = swap_blocks(buf[...], tile)
    else:
        buf[...] = permute_rows(mid_ref[...], buf[...])
    groups, step = 1, 1
    lanes = lax.broadcasted_iota(jnp.int32, (tile, length), 1)
    if not isinstance(first_trial, int):
        order = bit_reversed(subbands)
        for pos in range(subbands):
            rows = slice(pos * tile, (pos + 1) * tile)
            buf[rows, :] = shift_in(buf[rows, :], first_trial * int(order[pos]), lanes, 0)
        first_trial = 0
    while subbands > 1:
        half = subbands // 2
        for group in range(groups):
            for pos in range(half):
                top = (group * subbands + pos) * tile
                low = (group * subbands + pos + half) * tile
                upper = buf[top : top + tile, :]
                lower = buf[low : low + tile, :]
                buf[top : top + tile, :] = upper + shift_in(lower, first_trial + group, lanes, step)
                buf[low : low + tile, :] = upper + shift_in(
                    lower, first_trial + group + 1, lanes, step
                )
        subbands = half
        groups = 2 * groups
        step = 2 * step
        first_trial = 2 * first_trial
    return groups


def bit_reversed(count):
    bits = count.bit_length() - 1
    return np.array([int(format(i, f"0{bits}b")[::-1], 2) for i in range(count)], np.int32)


def one_hot(targets):
    return np.eye(len(targets), dtype=np.float32)[targets]


def tables(subbands, trials, tile):
    rows = subbands * trials
    order = bit_reversed(subbands)
    entry = one_hot([order[r % subbands] * trials + r // subbands for r in range(rows)])
    at_switch = rows // tile
    mid = one_hot([(r % tile) * at_switch + r // tile for r in range(rows)])
    groups = rows // tile
    leave = one_hot([(d % groups) * tile + d // groups for d in range(rows)])
    return entry, mid, leave


TILE = 8


def local_tree(tail_samples, block_samples, tail_blocks):
    beams_dev, rows, tail_len = tail_samples.shape
    length = tail_len + block_samples.shape[2]
    entry, mid, leave = tables(rows, 1, TILE)

    def body(count_ref, tail_ref, block_ref, entry_ref, mid_ref, leave_ref, o_ref, buf):
        beam = pl.program_id(0)
        lanes = lax.broadcasted_iota(jnp.int32, (rows, tail_len), 1)
        keep = lanes >= tail_len - 128 * count_ref[beam]
        order = entry_ref[...].astype(jnp.bfloat16)
        tail = jnp.dot(order, tail_ref[...], preferred_element_type=jnp.float32)
        buf[:, :tail_len] = jnp.where(keep, tail, jnp.float32(0.0))
        buf[:, tail_len:] = jnp.dot(order, block_ref[...], preferred_element_type=jnp.float32)
        tree_in_place(buf, mid_ref, rows, 1, 0, TILE)
        buf[...] = swap_blocks(buf[...], TILE)
        for r in range(rows):
            o_ref[r] = buf[r : r + 1, :]

    table_spec = pl.BlockSpec((rows, rows), lambda b: (0, 0))
    return pl.pallas_call(
        body,
        grid=(beams_dev,),
        in_specs=[
            pl.BlockSpec(memory_space=pltpu.SMEM),
            pl.BlockSpec((None, rows, tail_len), lambda b: (b, 0, 0)),
            pl.BlockSpec((None, rows, block_samples.shape[2]), lambda b: (b, 0, 0)),
            table_spec,
            table_spec,
            table_spec,
        ],
        out_specs=pl.BlockSpec((None, rows, 1, length), lambda b: (b, 0, 0, 0)),
        out_shape=jax.ShapeDtypeStruct((beams_dev, rows, 1, length), jnp.float32),
        scratch_shapes=[pltpu.VMEM((rows, length), jnp.float32)],
    )(tail_blocks.astype(jnp.int32), tail_samples, block_samples, entry, mid, leave).reshape(
        beams_dev, rows, length
    )


def peaks_of(dm_rows, tail_len, block_len, leave):
    trials = dm_rows.shape[0]
    searched = dm_rows[:, tail_len:]
    average = jnp.sum(searched, axis=1, keepdims=True) / jnp.float32(block_len)
    spread = jnp.sum((searched - average) ** 2, axis=1, keepdims=True) / jnp.float32(block_len)
    deviation = jnp.sqrt(spread + jnp.float32(1e-05))
    boxcar = dm_rows[:, tail_len - 128 :]
    lane_ids = lax.broadcasted_iota(jnp.int32, (trials, 128), 1)
    table = jnp.zeros((trials, 128), jnp.float32)
    for width_bit in range(WIDTHS):
        width_now = 2**width_bit
        if width_bit > 0:
            boxcar = boxcar + pltpu.roll(boxcar, width_now // 2, 1)
        top = jnp.max(boxcar[:, 128:], axis=1, keepdims=True)
        ratio = (top - width_now * average) / (np.sqrt(np.float32(width_now)) * deviation)
        table = jnp.where(lane_ids == width_bit, ratio, table)
    return permute_rows(leave, table).T[:8]


def merge_tree(parts, first_trial, tail_len):
    beams_dev, subbands, trials, length = parts.shape
    rows = subbands * trials
    entry, mid, leave = tables(subbands, trials, TILE)

    order = bit_reversed(subbands)

    def body(off_ref, x_ref, entry_ref, mid_ref, leave_ref, o_ref, buf):
        for pos in range(subbands):
            for trial in range(trials):
                source = int(order[pos]) * trials + trial
                buf[trial * subbands + pos : trial * subbands + pos + 1, :] = x_ref[source]
        tree_in_place(buf, mid_ref, subbands, trials, off_ref[0], TILE)
        o_ref[...] = peaks_of(buf[...], tail_len, length - tail_len, leave_ref[...])

    spec = pl.BlockSpec((None, rows, 1, length), lambda b: (b, 0, 0, 0))
    table_spec = pl.BlockSpec((rows, rows), lambda b: (0, 0))
    return pl.pallas_call(
        body,
        grid=(beams_dev,),
        in_specs=[pl.BlockSpec(memory_space=pltpu.SMEM), spec, table_spec, table_spec, table_spec],
        out_specs=pl.BlockSpec((None, 8, rows), lambda b: (b, 0, 0)),
        out_shape=jax.ShapeDtypeStruct((beams_dev, 8, rows), jnp.float32),
        scratch_shapes=[pltpu.VMEM((rows, length), jnp.float32)],
    )(
        jnp.reshape(first_trial, (1,)).astype(jnp.int32),
        parts.reshape(beams_dev, rows, 1, length),
        entry,
        mid,
        leave,
    )[:, :WIDTHS]


def local(block_samples, tail_samples, tail_blocks, dm_limit):
    beams_dev, local_chan, block_len = block_samples.shape
    tail_len = tail_samples.shape[2]
    series = local_tree(tail_samples, block_samples, tail_blocks)[:, None]
    devices = lax.axis_size("freq")
    position = lax.axis_index("freq")
    series = lax.all_to_all(series, "freq", split_axis=2, concat_axis=1, tiled=True)
    per_dev = series.shape[2]
    scores = merge_tree(series, position * per_dev, tail_len)
    out_rows = scores.shape[-1]
    trial_ids = position * out_rows + jnp.arange(out_rows, dtype=jnp.int32)
    peak_snr = jnp.where(
        trial_ids[None, None, :] < dm_limit[:, None, None], scores, jnp.float32(0.0)
    )
    beam_total = jnp.sum(peak_snr, axis=0)
    beam_count = lax.axis_size("beam")
    for level_bit in range(beam_count.bit_length() - 1):
        pairs = [(i, i ^ (1 << level_bit)) for i in range(beam_count)]
        beam_total = beam_total + lax.ppermute(beam_total, "beam", pairs)
    excess_snr = peak_snr - beam_total[None] / (beams_dev * lax.axis_size("beam"))
    return (peak_snr, excess_snr)


def solution(mesh):
    return jax.shard_map(
        local,
        mesh=mesh,
        in_specs=(P("beam", "freq", None), P("beam", "freq", None), P("beam"), P("beam")),
        out_specs=(P("beam", None, "freq"), P("beam", None, "freq")),
        check_vma=False,
    )
```

```python
import jax
import jax.numpy as jnp
import numpy as np
from jax import lax
from jax.experimental import pallas as pl
from jax.experimental.pallas import tpu as pltpu
from jax.sharding import PartitionSpec as P

WIDTHS = 7


def partner_2(block, axis, stride):
    count = lax.axis_size(axis)
    route = []
    for low in range(count):
        high = low | 1 << stride
        if high != low and high < count:
            route += [(low, high), (high, low)]
    return lax.ppermute(block, axis, route)


def skew_rows(series, step_size, base_shift, pad_width):
    dims_of = series.shape
    rows_count = dims_of[-2]
    length_now = dims_of[-1]
    flattened = series.reshape((-1, rows_count, length_now))
    padded = jnp.pad(flattened, ((0, 0), (0, 0), (pad_width, 0)))
    row_width = length_now + pad_width
    lined_up = padded.reshape((flattened.shape[0], rows_count * row_width))
    lined_up = jnp.pad(lined_up, ((0, 0), (0, pad_width)))
    window = lax.dynamic_slice_in_dim(
        lined_up, pad_width - base_shift, rows_count * (row_width - step_size), axis=1
    )
    moved_rows = window.reshape((flattened.shape[0], rows_count, row_width - step_size))[
        :, :, :length_now
    ]
    return moved_rows.reshape(dims_of)


def tree_section(series, offset, reach_max):
    upper_rows = series[..., 0::2, :, :]
    odd_rows = series[..., 1::2, :, :]
    even_moved = skew_rows(odd_rows, 1, (offset + 1) // 2, reach_max)
    odd_moved = skew_rows(odd_rows, 1, (offset + 2) // 2, reach_max)
    joined_rows = jnp.stack([upper_rows + even_moved, upper_rows + odd_moved], axis=-2)
    dims_of = upper_rows.shape
    return joined_rows.reshape(dims_of[:-2] + (2 * dims_of[-2], dims_of[-1]))


def peak_ratios(series, tail_len):
    searched = series[..., tail_len:]
    average = jnp.mean(searched, axis=-1, keepdims=True)
    deviation = jnp.sqrt(jnp.mean((searched - average) ** 2, axis=-1, keepdims=True) + 1e-05)
    reach_back = 2 ** (WIDTHS - 1)
    boxcar = series[..., tail_len - reach_back :]
    results = []
    for width_bit in range(WIDTHS):
        width_now = 2**width_bit
        if width_bit > 0:
            half_width = width_now // 2
            pad_spec = [(0, 0)] * (series.ndim - 1) + [(half_width, 0)]
            boxcar = boxcar + jnp.pad(boxcar[..., :-half_width], pad_spec)
        ratio = (boxcar[..., reach_back:] - width_now * average) / (
            jnp.sqrt(jnp.float32(width_now)) * deviation
        )
        results.append(jnp.max(ratio, axis=-1))
    return jnp.stack(results, axis=-2)


def shift_in(row_block, amount, lanes, stride):
    if stride:
        moved = pltpu.roll(row_block, amount, 1, stride=stride, stride_axis=0)
        limit = lax.broadcasted_iota(jnp.int32, row_block.shape, 0) * stride + amount
    else:
        moved = pltpu.roll(row_block, amount, 1)
        limit = amount
    return jnp.where(lanes >= limit, moved, jnp.float32(0.0))


def permute_rows(matrix, rows):
    return jnp.dot(matrix, rows, precision=lax.Precision.HIGHEST, preferred_element_type=jnp.float32)


def swap_blocks(rows, tile):
    length = rows.shape[1]
    blocks = rows.reshape(tile, tile, length)
    return pltpu.einshape("abt->bat", blocks).reshape(tile * tile, length)


def tree_in_place(buf, mid_ref, subbands, trials, first_trial, tile):
    length = buf.shape[1]
    while subbands > 1 and subbands // 2 >= tile:
        half = subbands // 2
        lanes = lax.broadcasted_iota(jnp.int32, (half, length), 1)
        for k in range(trials):
            top = k * subbands
            upper = buf[top : top + half, :]
            lower = buf[top + half : top + subbands, :]
            buf[top : top + half, :] = upper + shift_in(lower, first_trial + k, lanes, 0)
            buf[top + half : top + subbands, :] = upper + shift_in(
                lower, first_trial + k + 1, lanes, 0
            )
        subbands = half
        trials = 2 * trials
        first_trial = 2 * first_trial
    if subbands == tile and buf.shape[0] == tile * tile:
        buf[...] = swap_blocks(buf[...], tile)
    else:
        buf[...] = permute_rows(mid_ref[...], buf[...])
    groups, step = 1, 1
    lanes = lax.broadcasted_iota(jnp.int32, (tile, length), 1)
    if not isinstance(first_trial, int):
        order = bit_reversed(subbands)
        for pos in range(subbands):
            rows = slice(pos * tile, (pos + 1) * tile)
            buf[rows, :] = shift_in(buf[rows, :], first_trial * int(order[pos]), lanes, 0)
        first_trial = 0
    while subbands > 1:
        half = subbands // 2
        for group in range(groups):
            for pos in range(half):
                top = (group * subbands + pos) * tile
                low = (group * subbands + pos + half) * tile
                upper = buf[top : top + tile, :]
                lower = buf[low : low + tile, :]
                buf[top : top + tile, :] = upper + shift_in(lower, first_trial + group, lanes, step)
                buf[low : low + tile, :] = upper + shift_in(
                    lower, first_trial + group + 1, lanes, step
                )
        subbands = half
        groups = 2 * groups
        step = 2 * step
        first_trial = 2 * first_trial
    return groups


def bit_reversed(count):
    bits = count.bit_length() - 1
    return np.array([int(format(i, f"0{bits}b")[::-1], 2) for i in range(count)], np.int32)


def one_hot(targets):
    return np.eye(len(targets), dtype=np.float32)[targets]


def tables(subbands, trials, tile):
    rows = subbands * trials
    order = bit_reversed(subbands)
    entry = one_hot([order[r % subbands] * trials + r // subbands for r in range(rows)])
    at_switch = rows // tile
    mid = one_hot([(r % tile) * at_switch + r // tile for r in range(rows)])
    groups = rows // tile
    leave = one_hot([(d % groups) * tile + d // groups for d in range(rows)])
    return entry, mid, leave


TILE = 8


def local_tree(tail_samples, block_samples, tail_blocks):
    beams_dev, rows, tail_len = tail_samples.shape
    length = tail_len + block_samples.shape[2]
    entry, mid, leave = tables(rows, 1, TILE)

    def body(count_ref, tail_ref, block_ref, entry_ref, mid_ref, leave_ref, o_ref, buf):
        beam = pl.program_id(0)
        lanes = lax.broadcasted_iota(jnp.int32, (rows, tail_len), 1)
        keep = lanes >= tail_len - 128 * count_ref[beam]
        order = entry_ref[...].astype(jnp.bfloat16)
        tail = jnp.dot(order, tail_ref[...], preferred_element_type=jnp.float32)
        buf[:, :tail_len] = jnp.where(keep, tail, jnp.float32(0.0))
        buf[:, tail_len:] = jnp.dot(order, block_ref[...], preferred_element_type=jnp.float32)
        tree_in_place(buf, mid_ref, rows, 1, 0, TILE)
        buf[...] = swap_blocks(buf[...], TILE)
        for r in range(rows):
            o_ref[r] = buf[r : r + 1, :]

    table_spec = pl.BlockSpec((rows, rows), lambda b: (0, 0))
    return pl.pallas_call(
        body,
        grid=(beams_dev,),
        in_specs=[
            pl.BlockSpec(memory_space=pltpu.SMEM),
            pl.BlockSpec((None, rows, tail_len), lambda b: (b, 0, 0)),
            pl.BlockSpec((None, rows, block_samples.shape[2]), lambda b: (b, 0, 0)),
            table_spec,
            table_spec,
            table_spec,
        ],
        out_specs=pl.BlockSpec((None, rows, 1, length), lambda b: (b, 0, 0, 0)),
        out_shape=jax.ShapeDtypeStruct((beams_dev, rows, 1, length), jnp.float32),
        scratch_shapes=[pltpu.VMEM((rows, length), jnp.float32)],
    )(tail_blocks.astype(jnp.int32), tail_samples, block_samples, entry, mid, leave).reshape(
        beams_dev, rows, length
    )


def peaks_of(dm_rows, tail_len, block_len, leave):
    trials = dm_rows.shape[0]
    searched = dm_rows[:, tail_len:]
    average = jnp.sum(searched, axis=1, keepdims=True) / jnp.float32(block_len)
    spread = jnp.sum((searched - average) ** 2, axis=1, keepdims=True) / jnp.float32(block_len)
    deviation = jnp.sqrt(spread + jnp.float32(1e-05))
    boxcar = dm_rows[:, tail_len - 128 :]
    lane_ids = lax.broadcasted_iota(jnp.int32, (trials, 128), 1)
    table = jnp.zeros((trials, 128), jnp.float32)
    for width_bit in range(WIDTHS):
        width_now = 2**width_bit
        if width_bit > 0:
            boxcar = boxcar + pltpu.roll(boxcar, width_now // 2, 1)
        top = jnp.max(boxcar[:, 128:], axis=1, keepdims=True)
        ratio = (top - width_now * average) / (np.sqrt(np.float32(width_now)) * deviation)
        table = jnp.where(lane_ids == width_bit, ratio, table)
    return permute_rows(leave, table).T[:8]


def merge_tree(parts, first_trial, tail_len):
    beams_dev, subbands, trials, length = parts.shape
    rows = subbands * trials
    entry, mid, leave = tables(subbands, trials, TILE)

    order = bit_reversed(subbands)

    def body(off_ref, x_ref, entry_ref, mid_ref, leave_ref, o_ref, buf):
        for pos in range(subbands):
            for trial in range(trials):
                source = int(order[pos]) * trials + trial
                buf[trial * subbands + pos : trial * subbands + pos + 1, :] = x_ref[source]
        tree_in_place(buf, mid_ref, subbands, trials, off_ref[0], TILE)
        o_ref[...] = peaks_of(buf[...], tail_len, length - tail_len, leave_ref[...])

    spec = pl.BlockSpec((None, rows, 1, length), lambda b: (b, 0, 0, 0))
    table_spec = pl.BlockSpec((rows, rows), lambda b: (0, 0))
    return pl.pallas_call(
        body,
        grid=(beams_dev,),
        in_specs=[pl.BlockSpec(memory_space=pltpu.SMEM), spec, table_spec, table_spec, table_spec],
        out_specs=pl.BlockSpec((None, 8, rows), lambda b: (b, 0, 0)),
        out_shape=jax.ShapeDtypeStruct((beams_dev, 8, rows), jnp.float32),
        scratch_shapes=[pltpu.VMEM((rows, length), jnp.float32)],
    )(
        jnp.reshape(first_trial, (1,)).astype(jnp.int32),
        parts.reshape(beams_dev, rows, 1, length),
        entry,
        mid,
        leave,
    )[:, :WIDTHS]


def local(block_samples, tail_samples, tail_blocks, dm_limit):
    beams_dev, local_chan, block_len = block_samples.shape
    tail_len = tail_samples.shape[2]
    series = local_tree(tail_samples, block_samples, tail_blocks)[:, None]
    devices = lax.axis_size("freq")
    position = lax.axis_index("freq")
    series = lax.all_to_all(series, "freq", split_axis=2, concat_axis=1, tiled=True)
    per_dev = series.shape[2]
    scores = merge_tree(series, position * per_dev, tail_len)
    out_rows = scores.shape[-1]
    trial_ids = position * out_rows + jnp.arange(out_rows, dtype=jnp.int32)
    peak_snr = jnp.where(
        trial_ids[None, None, :] < dm_limit[:, None, None], scores, jnp.float32(0.0)
    )
    beam_total = jnp.sum(peak_snr, axis=0)
    beam_count = lax.axis_size("beam")
    for level_bit in range(beam_count.bit_length() - 1):
        span = 1 << level_bit
        if 2 * span == beam_count:
            pairs = [(i, beam_count - 1 - i) for i in range(beam_count)]
        else:
            pairs = [(i, i ^ span) for i in range(beam_count)]
        beam_total = beam_total + lax.ppermute(beam_total, "beam", pairs)
    excess_snr = peak_snr - beam_total[None] / (beams_dev * lax.axis_size("beam"))
    return (peak_snr, excess_snr)


def solution(mesh):
    return jax.shard_map(
        local,
        mesh=mesh,
        in_specs=(P("beam", "freq", None), P("beam", "freq", None), P("beam"), P("beam")),
        out_specs=(P("beam", None, "freq"), P("beam", None, "freq")),
        check_vma=False,
    )
```

```python
import jax
import jax.numpy as jnp
import numpy as np
from jax import lax
from jax.experimental import pallas as pl
from jax.experimental.pallas import tpu as pltpu
from jax.sharding import PartitionSpec as P

WIDTHS = 7


def partner_2(block, axis, stride):
    count = lax.axis_size(axis)
    route = []
    for low in range(count):
        high = low | 1 << stride
        if high != low and high < count:
            route += [(low, high), (high, low)]
    return lax.ppermute(block, axis, route)


def skew_rows(series, step_size, base_shift, pad_width):
    dims_of = series.shape
    rows_count = dims_of[-2]
    length_now = dims_of[-1]
    flattened = series.reshape((-1, rows_count, length_now))
    padded = jnp.pad(flattened, ((0, 0), (0, 0), (pad_width, 0)))
    row_width = length_now + pad_width
    lined_up = padded.reshape((flattened.shape[0], rows_count * row_width))
    lined_up = jnp.pad(lined_up, ((0, 0), (0, pad_width)))
    window = lax.dynamic_slice_in_dim(
        lined_up, pad_width - base_shift, rows_count * (row_width - step_size), axis=1
    )
    moved_rows = window.reshape((flattened.shape[0], rows_count, row_width - step_size))[
        :, :, :length_now
    ]
    return moved_rows.reshape(dims_of)


def tree_section(series, offset, reach_max):
    upper_rows = series[..., 0::2, :, :]
    odd_rows = series[..., 1::2, :, :]
    even_moved = skew_rows(odd_rows, 1, (offset + 1) // 2, reach_max)
    odd_moved = skew_rows(odd_rows, 1, (offset + 2) // 2, reach_max)
    joined_rows = jnp.stack([upper_rows + even_moved, upper_rows + odd_moved], axis=-2)
    dims_of = upper_rows.shape
    return joined_rows.reshape(dims_of[:-2] + (2 * dims_of[-2], dims_of[-1]))


def peak_ratios(series, tail_len):
    searched = series[..., tail_len:]
    average = jnp.mean(searched, axis=-1, keepdims=True)
    deviation = jnp.sqrt(jnp.mean((searched - average) ** 2, axis=-1, keepdims=True) + 1e-05)
    reach_back = 2 ** (WIDTHS - 1)
    boxcar = series[..., tail_len - reach_back :]
    results = []
    for width_bit in range(WIDTHS):
        width_now = 2**width_bit
        if width_bit > 0:
            half_width = width_now // 2
            pad_spec = [(0, 0)] * (series.ndim - 1) + [(half_width, 0)]
            boxcar = boxcar + jnp.pad(boxcar[..., :-half_width], pad_spec)
        ratio = (boxcar[..., reach_back:] - width_now * average) / (
            jnp.sqrt(jnp.float32(width_now)) * deviation
        )
        results.append(jnp.max(ratio, axis=-1))
    return jnp.stack(results, axis=-2)


def shift_in(row_block, amount, lanes, stride):
    if stride:
        moved = pltpu.roll(row_block, amount, 1, stride=stride, stride_axis=0)
        limit = lax.broadcasted_iota(jnp.int32, row_block.shape, 0) * stride + amount
    else:
        moved = pltpu.roll(row_block, amount, 1)
        limit = amount
    return jnp.where(lanes >= limit, moved, jnp.float32(0.0))


def permute_rows(matrix, rows):
    return jnp.dot(matrix, rows, precision=lax.Precision.HIGHEST, preferred_element_type=jnp.float32)


def swap_blocks(rows, tile):
    length = rows.shape[1]
    blocks = rows.reshape(tile, tile, length)
    return pltpu.einshape("abt->bat", blocks).reshape(tile * tile, length)


def tree_in_place(buf, mid_ref, subbands, trials, first_trial, tile):
    length = buf.shape[1]
    while subbands > 1 and subbands // 2 >= tile:
        half = subbands // 2
        lanes = lax.broadcasted_iota(jnp.int32, (half, length), 1)
        for k in range(trials):
            top = k * subbands
            upper = buf[top : top + half, :]
            lower = buf[top + half : top + subbands, :]
            buf[top : top + half, :] = upper + shift_in(lower, first_trial + k, lanes, 0)
            buf[top + half : top + subbands, :] = upper + shift_in(
                lower, first_trial + k + 1, lanes, 0
            )
        subbands = half
        trials = 2 * trials
        first_trial = 2 * first_trial
    if subbands == tile and buf.shape[0] == tile * tile:
        buf[...] = swap_blocks(buf[...], tile)
    else:
        buf[...] = permute_rows(mid_ref[...], buf[...])
    groups, step = 1, 1
    lanes = lax.broadcasted_iota(jnp.int32, (tile, length), 1)
    if not isinstance(first_trial, int):
        order = bit_reversed(subbands)
        for pos in range(subbands):
            rows = slice(pos * tile, (pos + 1) * tile)
            buf[rows, :] = shift_in(buf[rows, :], first_trial * int(order[pos]), lanes, 0)
        first_trial = 0
    while subbands > 1:
        half = subbands // 2
        for group in range(groups):
            for pos in range(half):
                top = (group * subbands + pos) * tile
                low = (group * subbands + pos + half) * tile
                upper = buf[top : top + tile, :]
                lower = buf[low : low + tile, :]
                buf[top : top + tile, :] = upper + shift_in(lower, first_trial + group, lanes, step)
                buf[low : low + tile, :] = upper + shift_in(
                    lower, first_trial + group + 1, lanes, step
                )
        subbands = half
        groups = 2 * groups
        step = 2 * step
        first_trial = 2 * first_trial
    return groups


def bit_reversed(count):
    bits = count.bit_length() - 1
    return np.array([int(format(i, f"0{bits}b")[::-1], 2) for i in range(count)], np.int32)


def one_hot(targets):
    return np.eye(len(targets), dtype=np.float32)[targets]


def tables(subbands, trials, tile):
    rows = subbands * trials
    order = bit_reversed(subbands)
    entry = one_hot([order[r % subbands] * trials + r // subbands for r in range(rows)])
    at_switch = rows // tile
    mid = one_hot([(r % tile) * at_switch + r // tile for r in range(rows)])
    groups = rows // tile
    leave = one_hot([(d % groups) * tile + d // groups for d in range(rows)])
    return entry, mid, leave


TILE = 8


def local_tree(tail_samples, block_samples, tail_blocks):
    beams_dev, rows, tail_len = tail_samples.shape
    length = tail_len + block_samples.shape[2]
    entry, mid, leave = tables(rows, 1, TILE)

    def body(count_ref, tail_ref, block_ref, entry_ref, mid_ref, leave_ref, o_ref, buf):
        beam = pl.program_id(0)
        lanes = lax.broadcasted_iota(jnp.int32, (rows, tail_len), 1)
        keep = lanes >= tail_len - 128 * count_ref[beam]
        order = entry_ref[...].astype(jnp.bfloat16)
        tail = jnp.dot(order, tail_ref[...], preferred_element_type=jnp.float32)
        buf[:, :tail_len] = jnp.where(keep, tail, jnp.float32(0.0))
        buf[:, tail_len:] = jnp.dot(order, block_ref[...], preferred_element_type=jnp.float32)
        tree_in_place(buf, mid_ref, rows, 1, 0, TILE)
        buf[...] = swap_blocks(buf[...], TILE)
        for r in range(rows):
            o_ref[r] = buf[r : r + 1, :]

    table_spec = pl.BlockSpec((rows, rows), lambda b: (0, 0))
    return pl.pallas_call(
        body,
        grid=(beams_dev,),
        in_specs=[
            pl.BlockSpec(memory_space=pltpu.SMEM),
            pl.BlockSpec((None, rows, tail_len), lambda b: (b, 0, 0)),
            pl.BlockSpec((None, rows, block_samples.shape[2]), lambda b: (b, 0, 0)),
            table_spec,
            table_spec,
            table_spec,
        ],
        out_specs=pl.BlockSpec((None, rows, 1, length), lambda b: (b, 0, 0, 0)),
        out_shape=jax.ShapeDtypeStruct((beams_dev, rows, 1, length), jnp.float32),
        scratch_shapes=[pltpu.VMEM((rows, length), jnp.float32)],
    )(tail_blocks.astype(jnp.int32), tail_samples, block_samples, entry, mid, leave).reshape(
        beams_dev, rows, length
    )


def peaks_of(dm_rows, tail_len, block_len, leave):
    trials = dm_rows.shape[0]
    searched = dm_rows[:, tail_len:]
    average = jnp.sum(searched, axis=1, keepdims=True) / jnp.float32(block_len)
    spread = jnp.sum((searched - average) ** 2, axis=1, keepdims=True) / jnp.float32(block_len)
    deviation = jnp.sqrt(spread + jnp.float32(1e-05))
    boxcar = dm_rows[:, tail_len - 128 :]
    lane_ids = lax.broadcasted_iota(jnp.int32, (trials, 128), 1)
    table = jnp.zeros((trials, 128), jnp.float32)
    for width_bit in range(WIDTHS):
        width_now = 2**width_bit
        if width_bit > 0:
            boxcar = boxcar + pltpu.roll(boxcar, width_now // 2, 1)
        top = jnp.max(boxcar[:, 128:], axis=1, keepdims=True)
        ratio = (top - width_now * average) / (np.sqrt(np.float32(width_now)) * deviation)
        table = jnp.where(lane_ids == width_bit, ratio, table)
    return permute_rows(leave, table).T[:8]


def merge_tree(parts, first_trial, tail_len):
    beams_dev, subbands, trials, length = parts.shape
    rows = subbands * trials
    entry, mid, leave = tables(subbands, trials, TILE)

    order = bit_reversed(subbands)

    def body(off_ref, x_ref, entry_ref, mid_ref, leave_ref, o_ref, buf):
        for pos in range(subbands):
            for trial in range(trials):
                source = int(order[pos]) * trials + trial
                buf[trial * subbands + pos : trial * subbands + pos + 1, :] = x_ref[source]
        tree_in_place(buf, mid_ref, subbands, trials, off_ref[0], TILE)
        o_ref[...] = peaks_of(buf[...], tail_len, length - tail_len, leave_ref[...])

    spec = pl.BlockSpec((None, rows, 1, length), lambda b: (b, 0, 0, 0))
    table_spec = pl.BlockSpec((rows, rows), lambda b: (0, 0))
    return pl.pallas_call(
        body,
        grid=(beams_dev,),
        in_specs=[pl.BlockSpec(memory_space=pltpu.SMEM), spec, table_spec, table_spec, table_spec],
        out_specs=pl.BlockSpec((None, 8, rows), lambda b: (b, 0, 0)),
        out_shape=jax.ShapeDtypeStruct((beams_dev, 8, rows), jnp.float32),
        scratch_shapes=[pltpu.VMEM((rows, length), jnp.float32)],
    )(
        jnp.reshape(first_trial, (1,)).astype(jnp.int32),
        parts.reshape(beams_dev, rows, 1, length),
        entry,
        mid,
        leave,
    )[:, :WIDTHS]


def local(block_samples, tail_samples, tail_blocks, dm_limit):
    beams_dev, local_chan, block_len = block_samples.shape
    tail_len = tail_samples.shape[2]
    series = local_tree(tail_samples, block_samples, tail_blocks)[:, None]
    devices = lax.axis_size("freq")
    position = lax.axis_index("freq")
    series = lax.all_to_all(series, "freq", split_axis=2, concat_axis=1, tiled=True)
    per_dev = series.shape[2]
    scores = merge_tree(series, position * per_dev, tail_len)
    out_rows = scores.shape[-1]
    trial_ids = position * out_rows + jnp.arange(out_rows, dtype=jnp.int32)
    peak_snr = jnp.where(
        trial_ids[None, None, :] < dm_limit[:, None, None], scores, jnp.float32(0.0)
    )
    beam_total = jnp.sum(peak_snr, axis=0)
    beam_count = lax.axis_size("beam")
    terms = [beam_total] + [
        lax.ppermute(beam_total, "beam", [(i, (i + step) % beam_count) for i in range(beam_count)])
        for step in range(1, beam_count)
    ]
    while len(terms) > 1:
        terms = [terms[i] + terms[i + 1] for i in range(0, len(terms) - 1, 2)] + terms[len(terms) - len(terms) % 2 :]
    beam_total = terms[0]
    excess_snr = peak_snr - beam_total[None] / (beams_dev * lax.axis_size("beam"))
    return (peak_snr, excess_snr)


def solution(mesh):
    return jax.shard_map(
        local,
        mesh=mesh,
        in_specs=(P("beam", "freq", None), P("beam", "freq", None), P("beam"), P("beam")),
        out_specs=(P("beam", None, "freq"), P("beam", None, "freq")),
        check_vma=False,
    )
```

```python
import jax
import jax.numpy as jnp
import numpy as np
from jax import lax
from jax.experimental import pallas as pl
from jax.experimental.pallas import tpu as pltpu
from jax.sharding import PartitionSpec as P

WIDTHS = 7


def partner_2(block, axis, stride):
    count = lax.axis_size(axis)
    route = []
    for low in range(count):
        high = low | 1 << stride
        if high != low and high < count:
            route += [(low, high), (high, low)]
    return lax.ppermute(block, axis, route)


def skew_rows(series, step_size, base_shift, pad_width):
    dims_of = series.shape
    rows_count = dims_of[-2]
    length_now = dims_of[-1]
    flattened = series.reshape((-1, rows_count, length_now))
    padded = jnp.pad(flattened, ((0, 0), (0, 0), (pad_width, 0)))
    row_width = length_now + pad_width
    lined_up = padded.reshape((flattened.shape[0], rows_count * row_width))
    lined_up = jnp.pad(lined_up, ((0, 0), (0, pad_width)))
    window = lax.dynamic_slice_in_dim(
        lined_up, pad_width - base_shift, rows_count * (row_width - step_size), axis=1
    )
    moved_rows = window.reshape((flattened.shape[0], rows_count, row_width - step_size))[
        :, :, :length_now
    ]
    return moved_rows.reshape(dims_of)


def tree_section(series, offset, reach_max):
    upper_rows = series[..., 0::2, :, :]
    odd_rows = series[..., 1::2, :, :]
    even_moved = skew_rows(odd_rows, 1, (offset + 1) // 2, reach_max)
    odd_moved = skew_rows(odd_rows, 1, (offset + 2) // 2, reach_max)
    joined_rows = jnp.stack([upper_rows + even_moved, upper_rows + odd_moved], axis=-2)
    dims_of = upper_rows.shape
    return joined_rows.reshape(dims_of[:-2] + (2 * dims_of[-2], dims_of[-1]))


def peak_ratios(series, tail_len):
    searched = series[..., tail_len:]
    average = jnp.mean(searched, axis=-1, keepdims=True)
    deviation = jnp.sqrt(jnp.mean((searched - average) ** 2, axis=-1, keepdims=True) + 1e-05)
    reach_back = 2 ** (WIDTHS - 1)
    boxcar = series[..., tail_len - reach_back :]
    results = []
    for width_bit in range(WIDTHS):
        width_now = 2**width_bit
        if width_bit > 0:
            half_width = width_now // 2
            pad_spec = [(0, 0)] * (series.ndim - 1) + [(half_width, 0)]
            boxcar = boxcar + jnp.pad(boxcar[..., :-half_width], pad_spec)
        ratio = (boxcar[..., reach_back:] - width_now * average) / (
            jnp.sqrt(jnp.float32(width_now)) * deviation
        )
        results.append(jnp.max(ratio, axis=-1))
    return jnp.stack(results, axis=-2)


def delay_traced(row_block, amount, pad_ref):
    rows, length = row_block.shape
    columns = length // 128
    whole = amount // 128
    part = amount - whole * 128
    lane = lax.broadcasted_iota(jnp.int32, (rows, 128), 1)
    before = jnp.zeros((rows, 128), jnp.float32)
    for j in range(columns):
        turned = pltpu.roll(row_block[:, 128 * j : 128 * (j + 1)], part, 1)
        pad_ref[:rows, length + 128 * j : length + 128 * (j + 1)] = jnp.where(lane >= part, turned, before)
        before = turned
    start = pl.multiple_of(length - 128 * jnp.minimum(whole, columns), 128)
    return pad_ref[:rows, pl.ds(start, length)]


def shift_in(row_block, amount, lanes, stride, pad_ref=None):
    if pad_ref is not None and not stride and not isinstance(amount, int):
        return delay_traced(row_block, amount, pad_ref)
    if stride:
        moved = pltpu.roll(row_block, amount, 1, stride=stride, stride_axis=0)
        limit = lax.broadcasted_iota(jnp.int32, row_block.shape, 0) * stride + amount
    else:
        moved = pltpu.roll(row_block, amount, 1)
        limit = amount
    return jnp.where(lanes >= limit, moved, jnp.float32(0.0))


def permute_rows(matrix, rows):
    return jnp.dot(matrix, rows, precision=lax.Precision.HIGHEST, preferred_element_type=jnp.float32)


def swap_blocks(rows, tile):
    length = rows.shape[1]
    blocks = rows.reshape(tile, tile, length)
    return pltpu.einshape("abt->bat", blocks).reshape(tile * tile, length)


def tree_in_place(buf, mid_ref, subbands, trials, first_trial, tile, pad_ref=None):
    length = buf.shape[1]
    while subbands > 1 and subbands // 2 >= tile:
        half = subbands // 2
        lanes = lax.broadcasted_iota(jnp.int32, (half, length), 1)
        for k in range(trials):
            top = k * subbands
            upper = buf[top : top + half, :]
            lower = buf[top + half : top + subbands, :]
            buf[top : top + half, :] = upper + shift_in(lower, first_trial + k, lanes, 0, pad_ref)
            buf[top + half : top + subbands, :] = upper + shift_in(
                lower, first_trial + k + 1, lanes, 0, pad_ref
            )
        subbands = half
        trials = 2 * trials
        first_trial = 2 * first_trial
    if subbands == tile and buf.shape[0] == tile * tile:
        buf[...] = swap_blocks(buf[...], tile)
    else:
        buf[...] = permute_rows(mid_ref[...], buf[...])
    groups, step = 1, 1
    lanes = lax.broadcasted_iota(jnp.int32, (tile, length), 1)
    if not isinstance(first_trial, int):
        order = bit_reversed(subbands)
        for pos in range(subbands):
            rows = slice(pos * tile, (pos + 1) * tile)
            buf[rows, :] = shift_in(buf[rows, :], first_trial * int(order[pos]), lanes, 0, pad_ref)
        first_trial = 0
    while subbands > 1:
        half = subbands // 2
        for group in range(groups):
            for pos in range(half):
                top = (group * subbands + pos) * tile
                low = (group * subbands + pos + half) * tile
                upper = buf[top : top + tile, :]
                lower = buf[low : low + tile, :]
                buf[top : top + tile, :] = upper + shift_in(lower, first_trial + group, lanes, step)
                buf[low : low + tile, :] = upper + shift_in(
                    lower, first_trial + group + 1, lanes, step
                )
        subbands = half
        groups = 2 * groups
        step = 2 * step
        first_trial = 2 * first_trial
    return groups


def bit_reversed(count):
    bits = count.bit_length() - 1
    return np.array([int(format(i, f"0{bits}b")[::-1], 2) for i in range(count)], np.int32)


def one_hot(targets):
    return np.eye(len(targets), dtype=np.float32)[targets]


def tables(subbands, trials, tile):
    rows = subbands * trials
    order = bit_reversed(subbands)
    entry = one_hot([order[r % subbands] * trials + r // subbands for r in range(rows)])
    at_switch = rows // tile
    mid = one_hot([(r % tile) * at_switch + r // tile for r in range(rows)])
    groups = rows // tile
    leave = one_hot([(d % groups) * tile + d // groups for d in range(rows)])
    return entry, mid, leave


TILE = 8


def local_tree(tail_samples, block_samples, tail_blocks):
    beams_dev, rows, tail_len = tail_samples.shape
    length = tail_len + block_samples.shape[2]
    entry, mid, leave = tables(rows, 1, TILE)

    def body(count_ref, tail_ref, block_ref, entry_ref, mid_ref, leave_ref, o_ref, buf):
        beam = pl.program_id(0)
        lanes = lax.broadcasted_iota(jnp.int32, (rows, tail_len), 1)
        keep = lanes >= tail_len - 128 * count_ref[beam]
        order = entry_ref[...].astype(jnp.bfloat16)
        tail = jnp.dot(order, tail_ref[...], preferred_element_type=jnp.float32)
        buf[:, :tail_len] = jnp.where(keep, tail, jnp.float32(0.0))
        buf[:, tail_len:] = jnp.dot(order, block_ref[...], preferred_element_type=jnp.float32)
        tree_in_place(buf, mid_ref, rows, 1, 0, TILE)
        buf[...] = swap_blocks(buf[...], TILE)
        for r in range(rows):
            o_ref[r] = buf[r : r + 1, :]

    table_spec = pl.BlockSpec((rows, rows), lambda b: (0, 0))
    return pl.pallas_call(
        body,
        grid=(beams_dev,),
        in_specs=[
            pl.BlockSpec(memory_space=pltpu.SMEM),
            pl.BlockSpec((None, rows, tail_len), lambda b: (b, 0, 0)),
            pl.BlockSpec((None, rows, block_samples.shape[2]), lambda b: (b, 0, 0)),
            table_spec,
            table_spec,
            table_spec,
        ],
        out_specs=pl.BlockSpec((None, rows, 1, length), lambda b: (b, 0, 0, 0)),
        out_shape=jax.ShapeDtypeStruct((beams_dev, rows, 1, length), jnp.float32),
        scratch_shapes=[pltpu.VMEM((rows, length), jnp.float32)],
    )(tail_blocks.astype(jnp.int32), tail_samples, block_samples, entry, mid, leave).reshape(
        beams_dev, rows, length
    )


def peaks_of(dm_rows, tail_len, block_len, leave):
    trials = dm_rows.shape[0]
    searched = dm_rows[:, tail_len:]
    average = jnp.sum(searched, axis=1, keepdims=True) / jnp.float32(block_len)
    spread = jnp.sum((searched - average) ** 2, axis=1, keepdims=True) / jnp.float32(block_len)
    deviation = jnp.sqrt(spread + jnp.float32(1e-05))
    boxcar = dm_rows[:, tail_len - 128 :]
    lane_ids = lax.broadcasted_iota(jnp.int32, (trials, 128), 1)
    table = jnp.zeros((trials, 128), jnp.float32)
    for width_bit in range(WIDTHS):
        width_now = 2**width_bit
        if width_bit > 0:
            boxcar = boxcar + pltpu.roll(boxcar, width_now // 2, 1)
        top = jnp.max(boxcar[:, 128:], axis=1, keepdims=True)
        ratio = (top - width_now * average) / (np.sqrt(np.float32(width_now)) * deviation)
        table = jnp.where(lane_ids == width_bit, ratio, table)
    return permute_rows(leave, table).T[:8]


def merge_tree(parts, first_trial, tail_len):
    beams_dev, subbands, trials, length = parts.shape
    rows = subbands * trials
    entry, mid, leave = tables(subbands, trials, TILE)

    order = bit_reversed(subbands)

    def body(off_ref, x_ref, entry_ref, mid_ref, leave_ref, o_ref, buf, pad_ref):
        pad_ref[:, :length] = jnp.zeros((pad_ref.shape[0], length), jnp.float32)
        for pos in range(subbands):
            for trial in range(trials):
                source = int(order[pos]) * trials + trial
                buf[trial * subbands + pos : trial * subbands + pos + 1, :] = x_ref[source]
        tree_in_place(buf, mid_ref, subbands, trials, off_ref[0], TILE, pad_ref)
        o_ref[...] = peaks_of(buf[...], tail_len, length - tail_len, leave_ref[...])

    spec = pl.BlockSpec((None, rows, 1, length), lambda b: (b, 0, 0, 0))
    table_spec = pl.BlockSpec((rows, rows), lambda b: (0, 0))
    return pl.pallas_call(
        body,
        grid=(beams_dev,),
        in_specs=[pl.BlockSpec(memory_space=pltpu.SMEM), spec, table_spec, table_spec, table_spec],
        out_specs=pl.BlockSpec((None, 8, rows), lambda b: (b, 0, 0)),
        out_shape=jax.ShapeDtypeStruct((beams_dev, 8, rows), jnp.float32),
        scratch_shapes=[
            pltpu.VMEM((rows, length), jnp.float32),
            pltpu.VMEM((2 * TILE, 2 * length), jnp.float32),
        ],
    )(
        jnp.reshape(first_trial, (1,)).astype(jnp.int32),
        parts.reshape(beams_dev, rows, 1, length),
        entry,
        mid,
        leave,
    )[:, :WIDTHS]


def local(block_samples, tail_samples, tail_blocks, dm_limit):
    beams_dev, local_chan, block_len = block_samples.shape
    tail_len = tail_samples.shape[2]
    series = local_tree(tail_samples, block_samples, tail_blocks)[:, None]
    devices = lax.axis_size("freq")
    position = lax.axis_index("freq")
    series = lax.all_to_all(series, "freq", split_axis=2, concat_axis=1, tiled=True)
    per_dev = series.shape[2]
    scores = merge_tree(series, position * per_dev, tail_len)
    out_rows = scores.shape[-1]
    trial_ids = position * out_rows + jnp.arange(out_rows, dtype=jnp.int32)
    peak_snr = jnp.where(
        trial_ids[None, None, :] < dm_limit[:, None, None], scores, jnp.float32(0.0)
    )
    beam_total = jnp.sum(peak_snr, axis=0)
    beam_count = lax.axis_size("beam")
    for level_bit in range(beam_count.bit_length() - 1):
        span = 1 << level_bit
        if 2 * span == beam_count:
            pairs = [(i, beam_count - 1 - i) for i in range(beam_count)]
        else:
            pairs = [(i, i ^ span) for i in range(beam_count)]
        beam_total = beam_total + lax.ppermute(beam_total, "beam", pairs)
    excess_snr = peak_snr - beam_total[None] / (beams_dev * lax.axis_size("beam"))
    return (peak_snr, excess_snr)


def solution(mesh):
    return jax.shard_map(
        local,
        mesh=mesh,
        in_specs=(P("beam", "freq", None), P("beam", "freq", None), P("beam"), P("beam")),
        out_specs=(P("beam", None, "freq"), P("beam", None, "freq")),
        check_vma=False,
    )
```

```python
import jax
import jax.numpy as jnp
import numpy as np
from jax import lax
from jax.experimental import pallas as pl
from jax.experimental.pallas import tpu as pltpu
from jax.sharding import PartitionSpec as P

WIDTHS = 7


def partner_2(block, axis, stride):
    count = lax.axis_size(axis)
    route = []
    for low in range(count):
        high = low | 1 << stride
        if high != low and high < count:
            route += [(low, high), (high, low)]
    return lax.ppermute(block, axis, route)


def skew_rows(series, step_size, base_shift, pad_width):
    dims_of = series.shape
    rows_count = dims_of[-2]
    length_now = dims_of[-1]
    flattened = series.reshape((-1, rows_count, length_now))
    padded = jnp.pad(flattened, ((0, 0), (0, 0), (pad_width, 0)))
    row_width = length_now + pad_width
    lined_up = padded.reshape((flattened.shape[0], rows_count * row_width))
    lined_up = jnp.pad(lined_up, ((0, 0), (0, pad_width)))
    window = lax.dynamic_slice_in_dim(
        lined_up, pad_width - base_shift, rows_count * (row_width - step_size), axis=1
    )
    moved_rows = window.reshape((flattened.shape[0], rows_count, row_width - step_size))[
        :, :, :length_now
    ]
    return moved_rows.reshape(dims_of)


def tree_section(series, offset, reach_max):
    upper_rows = series[..., 0::2, :, :]
    odd_rows = series[..., 1::2, :, :]
    even_moved = skew_rows(odd_rows, 1, (offset + 1) // 2, reach_max)
    odd_moved = skew_rows(odd_rows, 1, (offset + 2) // 2, reach_max)
    joined_rows = jnp.stack([upper_rows + even_moved, upper_rows + odd_moved], axis=-2)
    dims_of = upper_rows.shape
    return joined_rows.reshape(dims_of[:-2] + (2 * dims_of[-2], dims_of[-1]))


def peak_ratios(series, tail_len):
    searched = series[..., tail_len:]
    average = jnp.mean(searched, axis=-1, keepdims=True)
    deviation = jnp.sqrt(jnp.mean((searched - average) ** 2, axis=-1, keepdims=True) + 1e-05)
    reach_back = 2 ** (WIDTHS - 1)
    boxcar = series[..., tail_len - reach_back :]
    results = []
    for width_bit in range(WIDTHS):
        width_now = 2**width_bit
        if width_bit > 0:
            half_width = width_now // 2
            pad_spec = [(0, 0)] * (series.ndim - 1) + [(half_width, 0)]
            boxcar = boxcar + jnp.pad(boxcar[..., :-half_width], pad_spec)
        ratio = (boxcar[..., reach_back:] - width_now * average) / (
            jnp.sqrt(jnp.float32(width_now)) * deviation
        )
        results.append(jnp.max(ratio, axis=-1))
    return jnp.stack(results, axis=-2)


def delay_traced(row_block, amount, pad_ref):
    rows, length = row_block.shape
    columns = length // 128
    whole = amount // 128
    part = amount - whole * 128
    lane = lax.broadcasted_iota(jnp.int32, (rows, 128), 1)
    before = jnp.zeros((rows, 128), jnp.float32)
    for j in range(columns):
        turned = pltpu.roll(row_block[:, 128 * j : 128 * (j + 1)], part, 1)
        pad_ref[:rows, length + 128 * j : length + 128 * (j + 1)] = jnp.where(lane >= part, turned, before)
        before = turned
    start = pl.multiple_of(length - 128 * jnp.minimum(whole, columns), 128)
    return pad_ref[:rows, pl.ds(start, length)]


def shift_in(row_block, amount, lanes, stride, pad_ref=None):
    if pad_ref is not None and not stride and not isinstance(amount, int):
        return delay_traced(row_block, amount, pad_ref)
    if stride:
        moved = pltpu.roll(row_block, amount, 1, stride=stride, stride_axis=0)
        limit = lax.broadcasted_iota(jnp.int32, row_block.shape, 0) * stride + amount
    else:
        moved = pltpu.roll(row_block, amount, 1)
        limit = amount
    return jnp.where(lanes >= limit, moved, jnp.float32(0.0))


def permute_rows(matrix, rows):
    return jnp.dot(matrix, rows, precision=lax.Precision.HIGHEST, preferred_element_type=jnp.float32)


def swap_blocks(rows, tile):
    length = rows.shape[1]
    blocks = rows.reshape(tile, tile, length)
    return pltpu.einshape("abt->bat", blocks).reshape(tile * tile, length)


def tree_in_place(buf, mid_ref, subbands, trials, first_trial, tile, pad_ref=None):
    length = buf.shape[1]
    while subbands > 1 and subbands // 2 >= tile:
        half = subbands // 2
        lanes = lax.broadcasted_iota(jnp.int32, (half, length), 1)
        for k in range(trials):
            top = k * subbands
            upper = buf[top : top + half, :]
            lower = buf[top + half : top + subbands, :]
            buf[top : top + half, :] = upper + shift_in(lower, first_trial + k, lanes, 0, pad_ref)
            buf[top + half : top + subbands, :] = upper + shift_in(
                lower, first_trial + k + 1, lanes, 0, pad_ref
            )
        subbands = half
        trials = 2 * trials
        first_trial = 2 * first_trial
    if subbands == tile and buf.shape[0] == tile * tile:
        buf[...] = swap_blocks(buf[...], tile)
    else:
        buf[...] = permute_rows(mid_ref[...], buf[...])
    groups, step = 1, 1
    lanes = lax.broadcasted_iota(jnp.int32, (tile, length), 1)
    if not isinstance(first_trial, int):
        order = bit_reversed(subbands)
        for pos in range(subbands):
            rows = slice(pos * tile, (pos + 1) * tile)
            buf[rows, :] = shift_in(buf[rows, :], first_trial * int(order[pos]), lanes, 0, pad_ref)
        first_trial = 0
    while subbands > 1:
        half = subbands // 2
        for group in range(groups):
            for pos in range(half):
                top = (group * subbands + pos) * tile
                low = (group * subbands + pos + half) * tile
                upper = buf[top : top + tile, :]
                lower = buf[low : low + tile, :]
                buf[top : top + tile, :] = upper + shift_in(lower, first_trial + group, lanes, step)
                buf[low : low + tile, :] = upper + shift_in(
                    lower, first_trial + group + 1, lanes, step
                )
        subbands = half
        groups = 2 * groups
        step = 2 * step
        first_trial = 2 * first_trial
    return groups


def bit_reversed(count):
    bits = count.bit_length() - 1
    return np.array([int(format(i, f"0{bits}b")[::-1], 2) for i in range(count)], np.int32)


def one_hot(targets):
    return np.eye(len(targets), dtype=np.float32)[targets]


def tables(subbands, trials, tile):
    rows = subbands * trials
    order = bit_reversed(subbands)
    entry = one_hot([order[r % subbands] * trials + r // subbands for r in range(rows)])
    at_switch = rows // tile
    mid = one_hot([(r % tile) * at_switch + r // tile for r in range(rows)])
    groups = rows // tile
    leave = one_hot([(d % groups) * tile + d // groups for d in range(rows)])
    return entry, mid, leave


TILE = 8


def local_tree(tail_samples, block_samples, tail_blocks):
    beams_dev, rows, tail_len = tail_samples.shape
    length = tail_len + block_samples.shape[2]
    entry, mid, leave = tables(rows, 1, TILE)

    def body(count_ref, tail_ref, block_ref, entry_ref, mid_ref, leave_ref, o_ref, buf):
        beam = pl.program_id(0)
        lanes = lax.broadcasted_iota(jnp.int32, (rows, tail_len), 1)
        keep = lanes >= tail_len - 128 * count_ref[beam]
        order = entry_ref[...].astype(jnp.bfloat16)
        tail = jnp.dot(order, tail_ref[...], preferred_element_type=jnp.float32)
        buf[:, :tail_len] = jnp.where(keep, tail, jnp.float32(0.0))
        buf[:, tail_len:] = jnp.dot(order, block_ref[...], preferred_element_type=jnp.float32)
        tree_in_place(buf, mid_ref, rows, 1, 0, TILE)
        buf[...] = swap_blocks(buf[...], TILE)
        for r in range(rows):
            o_ref[r] = buf[r : r + 1, :]

    table_spec = pl.BlockSpec((rows, rows), lambda b: (0, 0))
    return pl.pallas_call(
        body,
        grid=(beams_dev,),
        in_specs=[
            pl.BlockSpec(memory_space=pltpu.SMEM),
            pl.BlockSpec((None, rows, tail_len), lambda b: (b, 0, 0)),
            pl.BlockSpec((None, rows, block_samples.shape[2]), lambda b: (b, 0, 0)),
            table_spec,
            table_spec,
            table_spec,
        ],
        out_specs=pl.BlockSpec((None, rows, 1, length), lambda b: (b, 0, 0, 0)),
        out_shape=jax.ShapeDtypeStruct((beams_dev, rows, 1, length), jnp.float32),
        scratch_shapes=[pltpu.VMEM((rows, length), jnp.float32)],
    )(tail_blocks.astype(jnp.int32), tail_samples, block_samples, entry, mid, leave).reshape(
        beams_dev, rows, length
    )


def peaks_of(dm_rows, tail_len, block_len, leave):
    trials = dm_rows.shape[0]
    searched = dm_rows[:, tail_len:]
    average = jnp.sum(searched, axis=1, keepdims=True) / jnp.float32(block_len)
    spread = jnp.sum((searched - average) ** 2, axis=1, keepdims=True) / jnp.float32(block_len)
    deviation = jnp.sqrt(spread + jnp.float32(1e-05))
    boxcar = dm_rows[:, tail_len - 128 :]
    lane_ids = lax.broadcasted_iota(jnp.int32, (trials, 128), 1)
    table = jnp.zeros((trials, 128), jnp.float32)
    for width_bit in range(WIDTHS):
        width_now = 2**width_bit
        if width_bit > 0:
            boxcar = boxcar + pltpu.roll(boxcar, width_now // 2, 1)
        top = jnp.max(boxcar[:, 128:], axis=1, keepdims=True)
        ratio = (top - width_now * average) / (np.sqrt(np.float32(width_now)) * deviation)
        table = jnp.where(lane_ids == width_bit, ratio, table)
    return permute_rows(leave, table).T[:8]


def merge_tree(parts, first_trial, tail_len, dm_limit):
    beams_dev, subbands, trials, length = parts.shape
    rows = subbands * trials
    entry, mid, leave = tables(subbands, trials, TILE)

    order = bit_reversed(subbands)

    def body(off_ref, limit_ref, x_ref, entry_ref, mid_ref, leave_ref, o_ref, buf, pad_ref):
        pad_ref[:, :length] = jnp.zeros((pad_ref.shape[0], length), jnp.float32)
        for pos in range(subbands):
            for trial in range(trials):
                source = int(order[pos]) * trials + trial
                buf[trial * subbands + pos : trial * subbands + pos + 1, :] = x_ref[source]
        tree_in_place(buf, mid_ref, subbands, trials, off_ref[0], TILE, pad_ref)
        table = peaks_of(buf[...], tail_len, length - tail_len, leave_ref[...])[:WIDTHS]
        ids = lax.broadcasted_iota(jnp.int32, table.shape, 1) + off_ref[0] * subbands
        o_ref[...] = jnp.where(ids < limit_ref[pl.program_id(0)], table, jnp.float32(0.0))

    spec = pl.BlockSpec((None, rows, 1, length), lambda b: (b, 0, 0, 0))
    table_spec = pl.BlockSpec((rows, rows), lambda b: (0, 0))
    return pl.pallas_call(
        body,
        grid=(beams_dev,),
        in_specs=[
            pl.BlockSpec(memory_space=pltpu.SMEM),
            pl.BlockSpec(memory_space=pltpu.SMEM),
            spec,
            table_spec,
            table_spec,
            table_spec,
        ],
        out_specs=pl.BlockSpec((None, WIDTHS, rows), lambda b: (b, 0, 0)),
        out_shape=jax.ShapeDtypeStruct((beams_dev, WIDTHS, rows), jnp.float32),
        scratch_shapes=[
            pltpu.VMEM((rows, length), jnp.float32),
            pltpu.VMEM((2 * TILE, 2 * length), jnp.float32),
        ],
    )(
        jnp.reshape(first_trial, (1,)).astype(jnp.int32),
        dm_limit.astype(jnp.int32),
        parts.reshape(beams_dev, rows, 1, length),
        entry,
        mid,
        leave,
    )


def local(block_samples, tail_samples, tail_blocks, dm_limit):
    beams_dev, local_chan, block_len = block_samples.shape
    tail_len = tail_samples.shape[2]
    series = local_tree(tail_samples, block_samples, tail_blocks)[:, None]
    devices = lax.axis_size("freq")
    position = lax.axis_index("freq")
    series = lax.all_to_all(series, "freq", split_axis=2, concat_axis=1, tiled=True)
    per_dev = series.shape[2]
    peak_snr = merge_tree(series, position * per_dev, tail_len, dm_limit)
    beam_total = jnp.sum(peak_snr, axis=0)
    beam_count = lax.axis_size("beam")
    for level_bit in range(beam_count.bit_length() - 1):
        span = 1 << level_bit
        if 2 * span == beam_count:
            pairs = [(i, beam_count - 1 - i) for i in range(beam_count)]
        else:
            pairs = [(i, i ^ span) for i in range(beam_count)]
        beam_total = beam_total + lax.ppermute(beam_total, "beam", pairs)
    excess_snr = peak_snr - beam_total[None] / (beams_dev * lax.axis_size("beam"))
    return (peak_snr, excess_snr)


def solution(mesh):
    return jax.shard_map(
        local,
        mesh=mesh,
        in_specs=(P("beam", "freq", None), P("beam", "freq", None), P("beam"), P("beam")),
        out_specs=(P("beam", None, "freq"), P("beam", None, "freq")),
        check_vma=False,
    )
```

```python
import jax
import jax.numpy as jnp
import numpy as np
from jax import lax
from jax.experimental import pallas as pl
from jax.experimental.pallas import tpu as pltpu
from jax.sharding import PartitionSpec as P

WIDTHS = 7


def partner_2(block, axis, stride):
    count = lax.axis_size(axis)
    route = []
    for low in range(count):
        high = low | 1 << stride
        if high != low and high < count:
            route += [(low, high), (high, low)]
    return lax.ppermute(block, axis, route)


def skew_rows(series, step_size, base_shift, pad_width):
    dims_of = series.shape
    rows_count = dims_of[-2]
    length_now = dims_of[-1]
    flattened = series.reshape((-1, rows_count, length_now))
    padded = jnp.pad(flattened, ((0, 0), (0, 0), (pad_width, 0)))
    row_width = length_now + pad_width
    lined_up = padded.reshape((flattened.shape[0], rows_count * row_width))
    lined_up = jnp.pad(lined_up, ((0, 0), (0, pad_width)))
    window = lax.dynamic_slice_in_dim(
        lined_up, pad_width - base_shift, rows_count * (row_width - step_size), axis=1
    )
    moved_rows = window.reshape((flattened.shape[0], rows_count, row_width - step_size))[
        :, :, :length_now
    ]
    return moved_rows.reshape(dims_of)


def tree_section(series, offset, reach_max):
    upper_rows = series[..., 0::2, :, :]
    odd_rows = series[..., 1::2, :, :]
    even_moved = skew_rows(odd_rows, 1, (offset + 1) // 2, reach_max)
    odd_moved = skew_rows(odd_rows, 1, (offset + 2) // 2, reach_max)
    joined_rows = jnp.stack([upper_rows + even_moved, upper_rows + odd_moved], axis=-2)
    dims_of = upper_rows.shape
    return joined_rows.reshape(dims_of[:-2] + (2 * dims_of[-2], dims_of[-1]))


def peak_ratios(series, tail_len):
    searched = series[..., tail_len:]
    average = jnp.mean(searched, axis=-1, keepdims=True)
    deviation = jnp.sqrt(jnp.mean((searched - average) ** 2, axis=-1, keepdims=True) + 1e-05)
    reach_back = 2 ** (WIDTHS - 1)
    boxcar = series[..., tail_len - reach_back :]
    results = []
    for width_bit in range(WIDTHS):
        width_now = 2**width_bit
        if width_bit > 0:
            half_width = width_now // 2
            pad_spec = [(0, 0)] * (series.ndim - 1) + [(half_width, 0)]
            boxcar = boxcar + jnp.pad(boxcar[..., :-half_width], pad_spec)
        ratio = (boxcar[..., reach_back:] - width_now * average) / (
            jnp.sqrt(jnp.float32(width_now)) * deviation
        )
        results.append(jnp.max(ratio, axis=-1))
    return jnp.stack(results, axis=-2)


def delay_traced(row_block, amount, pad_ref):
    rows, length = row_block.shape
    columns = length // 128
    whole = amount // 128
    part = amount - whole * 128
    lane = lax.broadcasted_iota(jnp.int32, (rows, 128), 1)
    before = jnp.zeros((rows, 128), jnp.float32)
    for j in range(columns):
        turned = pltpu.roll(row_block[:, 128 * j : 128 * (j + 1)], part, 1)
        pad_ref[:rows, length + 128 * j : length + 128 * (j + 1)] = jnp.where(lane >= part, turned, before)
        before = turned
    start = pl.multiple_of(length - 128 * jnp.minimum(whole, columns), 128)
    return pad_ref[:rows, pl.ds(start, length)]


def shift_in(row_block, amount, lanes, stride, pad_ref=None):
    if pad_ref is not None and not stride and not isinstance(amount, int):
        return delay_traced(row_block, amount, pad_ref)
    if stride:
        moved = pltpu.roll(row_block, amount, 1, stride=stride, stride_axis=0)
        limit = lax.broadcasted_iota(jnp.int32, row_block.shape, 0) * stride + amount
    else:
        moved = pltpu.roll(row_block, amount, 1)
        limit = amount
    return jnp.where(lanes >= limit, moved, jnp.float32(0.0))


def permute_rows(matrix, rows):
    return jnp.dot(matrix, rows, precision=lax.Precision.HIGHEST, preferred_element_type=jnp.float32)


def swap_blocks(rows, tile):
    length = rows.shape[1]
    blocks = rows.reshape(tile, tile, length)
    return pltpu.einshape("abt->bat", blocks).reshape(tile * tile, length)


def tree_in_place(buf, mid_ref, subbands, trials, first_trial, tile, pad_ref=None):
    length = buf.shape[1]
    while subbands > 1 and subbands // 2 >= tile:
        half = subbands // 2
        lanes = lax.broadcasted_iota(jnp.int32, (half, length), 1)
        for k in range(trials):
            top = k * subbands
            upper = buf[top : top + half, :]
            lower = buf[top + half : top + subbands, :]
            buf[top : top + half, :] = upper + shift_in(lower, first_trial + k, lanes, 0, pad_ref)
            buf[top + half : top + subbands, :] = upper + shift_in(
                lower, first_trial + k + 1, lanes, 0, pad_ref
            )
        subbands = half
        trials = 2 * trials
        first_trial = 2 * first_trial
    if subbands == tile and buf.shape[0] == tile * tile:
        buf[...] = swap_blocks(buf[...], tile)
    else:
        buf[...] = permute_rows(mid_ref[...], buf[...])
    groups, step = 1, 1
    lanes = lax.broadcasted_iota(jnp.int32, (tile, length), 1)
    if not isinstance(first_trial, int):
        order = bit_reversed(subbands)
        for pos in range(subbands):
            rows = slice(pos * tile, (pos + 1) * tile)
            buf[rows, :] = shift_in(buf[rows, :], first_trial * int(order[pos]), lanes, 0, pad_ref)
        first_trial = 0
    while subbands > 1:
        half = subbands // 2
        for group in range(groups):
            for pos in range(half):
                top = (group * subbands + pos) * tile
                low = (group * subbands + pos + half) * tile
                upper = buf[top : top + tile, :]
                lower = buf[low : low + tile, :]
                buf[top : top + tile, :] = upper + shift_in(lower, first_trial + group, lanes, step)
                buf[low : low + tile, :] = upper + shift_in(
                    lower, first_trial + group + 1, lanes, step
                )
        subbands = half
        groups = 2 * groups
        step = 2 * step
        first_trial = 2 * first_trial
    return groups


def bit_reversed(count):
    bits = count.bit_length() - 1
    return np.array([int(format(i, f"0{bits}b")[::-1], 2) for i in range(count)], np.int32)


def one_hot(targets):
    return np.eye(len(targets), dtype=np.float32)[targets]


def tables(subbands, trials, tile):
    rows = subbands * trials
    order = bit_reversed(subbands)
    entry = one_hot([order[r % subbands] * trials + r // subbands for r in range(rows)])
    at_switch = rows // tile
    mid = one_hot([(r % tile) * at_switch + r // tile for r in range(rows)])
    groups = rows // tile
    leave = one_hot([(d % groups) * tile + d // groups for d in range(rows)])
    return entry, mid, leave


TILE = 8


def local_tree(tail_samples, block_samples, tail_blocks):
    beams_dev, rows, tail_len = tail_samples.shape
    length = tail_len + block_samples.shape[2]
    entry, mid, leave = tables(rows, 1, TILE)

    def body(count_ref, tail_ref, block_ref, entry_ref, mid_ref, leave_ref, o_ref, buf):
        beam = pl.program_id(0)
        lanes = lax.broadcasted_iota(jnp.int32, (rows, tail_len), 1)
        keep = lanes >= tail_len - 128 * count_ref[beam]
        order = entry_ref[...].astype(jnp.bfloat16)
        tail = jnp.dot(order, tail_ref[...], preferred_element_type=jnp.float32)
        buf[:, :tail_len] = jnp.where(keep, tail, jnp.float32(0.0))
        buf[:, tail_len:] = jnp.dot(order, block_ref[...], preferred_element_type=jnp.float32)
        tree_in_place(buf, mid_ref, rows, 1, 0, TILE)
        buf[...] = swap_blocks(buf[...], TILE)
        for r in range(rows):
            o_ref[r] = buf[r : r + 1, :]

    table_spec = pl.BlockSpec((rows, rows), lambda b: (0, 0))
    return pl.pallas_call(
        body,
        grid=(beams_dev,),
        in_specs=[
            pl.BlockSpec(memory_space=pltpu.SMEM),
            pl.BlockSpec((None, rows, tail_len), lambda b: (b, 0, 0)),
            pl.BlockSpec((None, rows, block_samples.shape[2]), lambda b: (b, 0, 0)),
            table_spec,
            table_spec,
            table_spec,
        ],
        out_specs=pl.BlockSpec((None, rows, 1, length), lambda b: (b, 0, 0, 0)),
        out_shape=jax.ShapeDtypeStruct((beams_dev, rows, 1, length), jnp.float32),
        scratch_shapes=[pltpu.VMEM((rows, length), jnp.float32)],
    )(tail_blocks.astype(jnp.int32), tail_samples, block_samples, entry, mid, leave).reshape(
        beams_dev, rows, length
    )


def peaks_of(dm_rows, tail_len, block_len, leave):
    trials = dm_rows.shape[0]
    searched = dm_rows[:, tail_len:]
    average = jnp.sum(searched, axis=1, keepdims=True) / jnp.float32(block_len)
    spread = jnp.sum((searched - average) ** 2, axis=1, keepdims=True) / jnp.float32(block_len)
    deviation = jnp.sqrt(spread + jnp.float32(1e-05))
    boxcar = dm_rows[:, tail_len - 128 :]
    lane_ids = lax.broadcasted_iota(jnp.int32, (trials, 128), 1)
    table = jnp.zeros((trials, 128), jnp.float32)
    for width_bit in range(WIDTHS):
        width_now = 2**width_bit
        if width_bit > 0:
            boxcar = boxcar + pltpu.roll(boxcar, width_now // 2, 1)
        top = jnp.max(boxcar[:, 128:], axis=1, keepdims=True)
        ratio = (top - width_now * average) / (np.sqrt(np.float32(width_now)) * deviation)
        table = jnp.where(lane_ids == width_bit, ratio, table)
    return permute_rows(leave, table).T[:8]


def merge_tree(parts, first_trial, tail_len, dm_limit):
    beams_dev, subbands, trials, length = parts.shape
    rows = subbands * trials
    entry, mid, leave = tables(subbands, trials, TILE)

    order = bit_reversed(subbands)

    def body(off_ref, limit_ref, x_ref, entry_ref, mid_ref, leave_ref, o_ref, laid_ref, buf, pad_ref):
        pad_ref[:, :length] = jnp.zeros((pad_ref.shape[0], length), jnp.float32)
        for pos in range(subbands):
            for trial in range(trials):
                source = int(order[pos]) * trials + trial
                buf[trial * subbands + pos : trial * subbands + pos + 1, :] = x_ref[source]
        tree_in_place(buf, mid_ref, subbands, trials, off_ref[0], TILE, pad_ref)
        table = peaks_of(buf[...], tail_len, length - tail_len, leave_ref[...])[:WIDTHS]
        ids = lax.broadcasted_iota(jnp.int32, table.shape, 1) + off_ref[0] * subbands
        masked = jnp.where(ids < limit_ref[pl.program_id(0)], table, jnp.float32(0.0))
        o_ref[...] = masked
        for width_bit in range(WIDTHS):
            laid_ref[width_bit] = masked[width_bit : width_bit + 1, :]

    spec = pl.BlockSpec((None, rows, 1, length), lambda b: (b, 0, 0, 0))
    table_spec = pl.BlockSpec((rows, rows), lambda b: (0, 0))
    return pl.pallas_call(
        body,
        grid=(beams_dev,),
        in_specs=[
            pl.BlockSpec(memory_space=pltpu.SMEM),
            pl.BlockSpec(memory_space=pltpu.SMEM),
            spec,
            table_spec,
            table_spec,
            table_spec,
        ],
        out_specs=[
            pl.BlockSpec((None, WIDTHS, rows), lambda b: (b, 0, 0)),
            pl.BlockSpec((WIDTHS, None, 1, rows), lambda b: (0, b, 0, 0)),
        ],
        out_shape=[
            jax.ShapeDtypeStruct((beams_dev, WIDTHS, rows), jnp.float32),
            jax.ShapeDtypeStruct((WIDTHS, beams_dev, 1, rows), jnp.float32),
        ],
        scratch_shapes=[
            pltpu.VMEM((rows, length), jnp.float32),
            pltpu.VMEM((2 * TILE, 2 * length), jnp.float32),
        ],
    )(
        jnp.reshape(first_trial, (1,)).astype(jnp.int32),
        dm_limit.astype(jnp.int32),
        parts.reshape(beams_dev, rows, 1, length),
        entry,
        mid,
        leave,
    )


def local(block_samples, tail_samples, tail_blocks, dm_limit):
    beams_dev, local_chan, block_len = block_samples.shape
    tail_len = tail_samples.shape[2]
    series = local_tree(tail_samples, block_samples, tail_blocks)[:, None]
    devices = lax.axis_size("freq")
    position = lax.axis_index("freq")
    series = lax.all_to_all(series, "freq", split_axis=2, concat_axis=1, tiled=True)
    per_dev = series.shape[2]
    peak_snr, laid = merge_tree(series, position * per_dev, tail_len, dm_limit)
    beam_total = jnp.sum(peak_snr, axis=0)
    beam_count = lax.axis_size("beam")
    for level_bit in range(beam_count.bit_length() - 1):
        span = 1 << level_bit
        if 2 * span == beam_count:
            pairs = [(i, beam_count - 1 - i) for i in range(beam_count)]
        else:
            pairs = [(i, i ^ span) for i in range(beam_count)]
        beam_total = beam_total + lax.ppermute(beam_total, "beam", pairs)
    excess_snr = peak_snr - beam_total[None] / (beams_dev * lax.axis_size("beam"))
    laid = laid.reshape(WIDTHS, beams_dev, laid.shape[-1]).transpose(1, 0, 2)
    return (laid, excess_snr)


def solution(mesh):
    return jax.shard_map(
        local,
        mesh=mesh,
        in_specs=(P("beam", "freq", None), P("beam", "freq", None), P("beam"), P("beam")),
        out_specs=(P("beam", None, "freq"), P("beam", None, "freq")),
        check_vma=False,
    )
```

```python
import jax
import jax.numpy as jnp
import numpy as np
from jax import lax
from jax.experimental import pallas as pl
from jax.experimental.pallas import tpu as pltpu
from jax.sharding import PartitionSpec as P

WIDTHS = 7


def partner_2(block, axis, stride):
    count = lax.axis_size(axis)
    route = []
    for low in range(count):
        high = low | 1 << stride
        if high != low and high < count:
            route += [(low, high), (high, low)]
    return lax.ppermute(block, axis, route)


def skew_rows(series, step_size, base_shift, pad_width):
    dims_of = series.shape
    rows_count = dims_of[-2]
    length_now = dims_of[-1]
    flattened = series.reshape((-1, rows_count, length_now))
    padded = jnp.pad(flattened, ((0, 0), (0, 0), (pad_width, 0)))
    row_width = length_now + pad_width
    lined_up = padded.reshape((flattened.shape[0], rows_count * row_width))
    lined_up = jnp.pad(lined_up, ((0, 0), (0, pad_width)))
    window = lax.dynamic_slice_in_dim(
        lined_up, pad_width - base_shift, rows_count * (row_width - step_size), axis=1
    )
    moved_rows = window.reshape((flattened.shape[0], rows_count, row_width - step_size))[
        :, :, :length_now
    ]
    return moved_rows.reshape(dims_of)


def tree_section(series, offset, reach_max):
    upper_rows = series[..., 0::2, :, :]
    odd_rows = series[..., 1::2, :, :]
    even_moved = skew_rows(odd_rows, 1, (offset + 1) // 2, reach_max)
    odd_moved = skew_rows(odd_rows, 1, (offset + 2) // 2, reach_max)
    joined_rows = jnp.stack([upper_rows + even_moved, upper_rows + odd_moved], axis=-2)
    dims_of = upper_rows.shape
    return joined_rows.reshape(dims_of[:-2] + (2 * dims_of[-2], dims_of[-1]))


def peak_ratios(series, tail_len):
    searched = series[..., tail_len:]
    average = jnp.mean(searched, axis=-1, keepdims=True)
    deviation = jnp.sqrt(jnp.mean((searched - average) ** 2, axis=-1, keepdims=True) + 1e-05)
    reach_back = 2 ** (WIDTHS - 1)
    boxcar = series[..., tail_len - reach_back :]
    results = []
    for width_bit in range(WIDTHS):
        width_now = 2**width_bit
        if width_bit > 0:
            half_width = width_now // 2
            pad_spec = [(0, 0)] * (series.ndim - 1) + [(half_width, 0)]
            boxcar = boxcar + jnp.pad(boxcar[..., :-half_width], pad_spec)
        ratio = (boxcar[..., reach_back:] - width_now * average) / (
            jnp.sqrt(jnp.float32(width_now)) * deviation
        )
        results.append(jnp.max(ratio, axis=-1))
    return jnp.stack(results, axis=-2)


def delay_traced(row_block, amount, pad_ref):
    rows, length = row_block.shape
    columns = length // 128
    whole = amount // 128
    part = amount - whole * 128
    lane = lax.broadcasted_iota(jnp.int32, (rows, 128), 1)
    before = jnp.zeros((rows, 128), jnp.float32)
    for j in range(columns):
        turned = pltpu.roll(row_block[:, 128 * j : 128 * (j + 1)], part, 1)
        pad_ref[:rows, length + 128 * j : length + 128 * (j + 1)] = jnp.where(lane >= part, turned, before)
        before = turned
    start = pl.multiple_of(length - 128 * jnp.minimum(whole, columns), 128)
    return pad_ref[:rows, pl.ds(start, length)]


def shift_in(row_block, amount, lanes, stride, pad_ref=None):
    if pad_ref is not None and not stride and not isinstance(amount, int):
        return delay_traced(row_block, amount, pad_ref)
    if stride:
        moved = pltpu.roll(row_block, amount, 1, stride=stride, stride_axis=0)
        limit = lax.broadcasted_iota(jnp.int32, row_block.shape, 0) * stride + amount
    else:
        moved = pltpu.roll(row_block, amount, 1)
        limit = amount
    return jnp.where(lanes >= limit, moved, jnp.float32(0.0))


def permute_rows(matrix, rows):
    return jnp.dot(matrix, rows, precision=lax.Precision.HIGHEST, preferred_element_type=jnp.float32)


def swap_blocks(rows, tile):
    length = rows.shape[1]
    blocks = rows.reshape(tile, tile, length)
    return pltpu.einshape("abt->bat", blocks).reshape(tile * tile, length)


def tree_in_place(buf, mid_ref, subbands, trials, first_trial, tile, pad_ref=None):
    length = buf.shape[1]
    while subbands > 1 and subbands // 2 >= tile:
        half = subbands // 2
        lanes = lax.broadcasted_iota(jnp.int32, (half, length), 1)
        for k in range(trials):
            top = k * subbands
            upper = buf[top : top + half, :]
            lower = buf[top + half : top + subbands, :]
            buf[top : top + half, :] = upper + shift_in(lower, first_trial + k, lanes, 0, pad_ref)
            buf[top + half : top + subbands, :] = upper + shift_in(
                lower, first_trial + k + 1, lanes, 0, pad_ref
            )
        subbands = half
        trials = 2 * trials
        first_trial = 2 * first_trial
    if subbands == tile and buf.shape[0] == tile * tile:
        buf[...] = swap_blocks(buf[...], tile)
    else:
        buf[...] = permute_rows(mid_ref[...], buf[...])
    groups, step = 1, 1
    lanes = lax.broadcasted_iota(jnp.int32, (tile, length), 1)
    if not isinstance(first_trial, int):
        order = bit_reversed(subbands)
        for pos in range(subbands):
            rows = slice(pos * tile, (pos + 1) * tile)
            buf[rows, :] = shift_in(buf[rows, :], first_trial * int(order[pos]), lanes, 0, pad_ref)
        first_trial = 0
    while subbands > 1:
        half = subbands // 2
        for group in range(groups):
            for pos in range(half):
                top = (group * subbands + pos) * tile
                low = (group * subbands + pos + half) * tile
                upper = buf[top : top + tile, :]
                lower = buf[low : low + tile, :]
                buf[top : top + tile, :] = upper + shift_in(lower, first_trial + group, lanes, step)
                buf[low : low + tile, :] = upper + shift_in(
                    lower, first_trial + group + 1, lanes, step
                )
        subbands = half
        groups = 2 * groups
        step = 2 * step
        first_trial = 2 * first_trial
    return groups


def bit_reversed(count):
    bits = count.bit_length() - 1
    return np.array([int(format(i, f"0{bits}b")[::-1], 2) for i in range(count)], np.int32)


def one_hot(targets):
    return np.eye(len(targets), dtype=np.float32)[targets]


def tables(subbands, trials, tile):
    rows = subbands * trials
    order = bit_reversed(subbands)
    entry = one_hot([order[r % subbands] * trials + r // subbands for r in range(rows)])
    at_switch = rows // tile
    mid = one_hot([(r % tile) * at_switch + r // tile for r in range(rows)])
    groups = rows // tile
    leave = one_hot([(d % groups) * tile + d // groups for d in range(rows)])
    return entry, mid, leave


TILE = 8


def local_tree(tail_samples, block_samples, tail_blocks):
    beams_dev, rows, tail_len = tail_samples.shape
    length = tail_len + block_samples.shape[2]
    entry, mid, leave = tables(rows, 1, TILE)

    def body(count_ref, tail_ref, block_ref, entry_ref, mid_ref, leave_ref, o_ref, buf):
        beam = pl.program_id(0)
        lanes = lax.broadcasted_iota(jnp.int32, (rows, tail_len), 1)
        keep = lanes >= tail_len - 128 * count_ref[beam]
        order = entry_ref[...].astype(jnp.bfloat16)
        tail = jnp.dot(order, tail_ref[...], preferred_element_type=jnp.float32)
        buf[:, :tail_len] = jnp.where(keep, tail, jnp.float32(0.0))
        buf[:, tail_len:] = jnp.dot(order, block_ref[...], preferred_element_type=jnp.float32)
        tree_in_place(buf, mid_ref, rows, 1, 0, TILE)
        buf[...] = swap_blocks(buf[...], TILE)
        for r in range(rows):
            o_ref[r] = buf[r : r + 1, :]

    table_spec = pl.BlockSpec((rows, rows), lambda b: (0, 0))
    return pl.pallas_call(
        body,
        grid=(beams_dev,),
        in_specs=[
            pl.BlockSpec(memory_space=pltpu.SMEM),
            pl.BlockSpec((None, rows, tail_len), lambda b: (b, 0, 0)),
            pl.BlockSpec((None, rows, block_samples.shape[2]), lambda b: (b, 0, 0)),
            table_spec,
            table_spec,
            table_spec,
        ],
        out_specs=pl.BlockSpec((None, rows, 1, length), lambda b: (b, 0, 0, 0)),
        out_shape=jax.ShapeDtypeStruct((beams_dev, rows, 1, length), jnp.float32),
        scratch_shapes=[pltpu.VMEM((rows, length), jnp.float32)],
    )(tail_blocks.astype(jnp.int32), tail_samples, block_samples, entry, mid, leave).reshape(
        beams_dev, rows, length
    )


def peaks_of(dm_rows, tail_len, block_len, leave):
    trials = dm_rows.shape[0]
    searched = dm_rows[:, tail_len:]
    average = jnp.sum(searched, axis=1, keepdims=True) / jnp.float32(block_len)
    spread = jnp.sum((searched - average) ** 2, axis=1, keepdims=True) / jnp.float32(block_len)
    deviation = jnp.sqrt(spread + jnp.float32(1e-05))
    boxcar = dm_rows[:, tail_len - 128 :]
    lane_ids = lax.broadcasted_iota(jnp.int32, (trials, 128), 1)
    table = jnp.zeros((trials, 128), jnp.float32)
    for width_bit in range(WIDTHS):
        width_now = 2**width_bit
        if width_bit > 0:
            boxcar = boxcar + pltpu.roll(boxcar, width_now // 2, 1)
        top = jnp.max(boxcar[:, 128:], axis=1, keepdims=True)
        ratio = (top - width_now * average) / (np.sqrt(np.float32(width_now)) * deviation)
        table = jnp.where(lane_ids == width_bit, ratio, table)
    return permute_rows(leave, table).T[:8]


def merge_tree(parts, first_trial, tail_len, dm_limit):
    beams_dev, subbands, trials, length = parts.shape
    rows = subbands * trials
    entry, mid, leave = tables(subbands, trials, TILE)

    order = bit_reversed(subbands)

    def body(off_ref, limit_ref, x_ref, entry_ref, mid_ref, leave_ref, o_ref, buf, pad_ref):
        pad_ref[:, :length] = jnp.zeros((pad_ref.shape[0], length), jnp.float32)
        for pos in range(subbands):
            for trial in range(trials):
                source = int(order[pos]) * trials + trial
                buf[trial * subbands + pos : trial * subbands + pos + 1, :] = x_ref[source]
        tree_in_place(buf, mid_ref, subbands, trials, off_ref[0], TILE, pad_ref)
        table = peaks_of(buf[...], tail_len, length - tail_len, leave_ref[...])[:WIDTHS]
        ids = lax.broadcasted_iota(jnp.int32, table.shape, 1) + off_ref[0] * subbands
        o_ref[...] = jnp.where(ids < limit_ref[pl.program_id(0)], table, jnp.float32(0.0))

    spec = pl.BlockSpec((None, rows, 1, length), lambda b: (b, 0, 0, 0))
    table_spec = pl.BlockSpec((rows, rows), lambda b: (0, 0))
    return pl.pallas_call(
        body,
        grid=(beams_dev,),
        in_specs=[
            pl.BlockSpec(memory_space=pltpu.SMEM),
            pl.BlockSpec(memory_space=pltpu.SMEM),
            spec,
            table_spec,
            table_spec,
            table_spec,
        ],
        out_specs=pl.BlockSpec((None, WIDTHS, rows), lambda b: (b, 0, 0)),
        out_shape=jax.ShapeDtypeStruct((beams_dev, WIDTHS, rows), jnp.float32),
        scratch_shapes=[
            pltpu.VMEM((rows, length), jnp.float32),
            pltpu.VMEM((2 * TILE, 2 * length), jnp.float32),
        ],
    )(
        jnp.reshape(first_trial, (1,)).astype(jnp.int32),
        dm_limit.astype(jnp.int32),
        parts.reshape(beams_dev, rows, 1, length),
        entry,
        mid,
        leave,
    )


def local(block_samples, tail_samples, tail_blocks, dm_limit):
    beams_dev, local_chan, block_len = block_samples.shape
    tail_len = tail_samples.shape[2]
    series = local_tree(tail_samples, block_samples, tail_blocks)[:, None]
    devices = lax.axis_size("freq")
    position = lax.axis_index("freq")
    series = lax.all_to_all(series, "freq", split_axis=2, concat_axis=1, tiled=True)
    per_dev = series.shape[2]
    peak_snr = merge_tree(series, position * per_dev, tail_len, dm_limit)
    beam_total = jnp.sum(peak_snr, axis=0)
    beam_count = lax.axis_size("beam")
    spans = [beam_count - 1] + [1 << b for b in range(beam_count.bit_length() - 2)]
    for span in spans:
        pairs = [(i, i ^ span) for i in range(beam_count)]
        beam_total = beam_total + lax.ppermute(beam_total, "beam", pairs)
    excess_snr = peak_snr - beam_total[None] / (beams_dev * lax.axis_size("beam"))
    return (peak_snr, excess_snr)


def solution(mesh):
    return jax.shard_map(
        local,
        mesh=mesh,
        in_specs=(P("beam", "freq", None), P("beam", "freq", None), P("beam"), P("beam")),
        out_specs=(P("beam", None, "freq"), P("beam", None, "freq")),
        check_vma=False,
    )
```

```python
import jax
import jax.numpy as jnp
import numpy as np
from jax import lax
from jax.experimental import pallas as pl
from jax.experimental.pallas import tpu as pltpu
from jax.sharding import PartitionSpec as P

WIDTHS = 7


def partner_2(block, axis, stride):
    count = lax.axis_size(axis)
    route = []
    for low in range(count):
        high = low | 1 << stride
        if high != low and high < count:
            route += [(low, high), (high, low)]
    return lax.ppermute(block, axis, route)


def skew_rows(series, step_size, base_shift, pad_width):
    dims_of = series.shape
    rows_count = dims_of[-2]
    length_now = dims_of[-1]
    flattened = series.reshape((-1, rows_count, length_now))
    padded = jnp.pad(flattened, ((0, 0), (0, 0), (pad_width, 0)))
    row_width = length_now + pad_width
    lined_up = padded.reshape((flattened.shape[0], rows_count * row_width))
    lined_up = jnp.pad(lined_up, ((0, 0), (0, pad_width)))
    window = lax.dynamic_slice_in_dim(
        lined_up, pad_width - base_shift, rows_count * (row_width - step_size), axis=1
    )
    moved_rows = window.reshape((flattened.shape[0], rows_count, row_width - step_size))[
        :, :, :length_now
    ]
    return moved_rows.reshape(dims_of)


def tree_section(series, offset, reach_max):
    upper_rows = series[..., 0::2, :, :]
    odd_rows = series[..., 1::2, :, :]
    even_moved = skew_rows(odd_rows, 1, (offset + 1) // 2, reach_max)
    odd_moved = skew_rows(odd_rows, 1, (offset + 2) // 2, reach_max)
    joined_rows = jnp.stack([upper_rows + even_moved, upper_rows + odd_moved], axis=-2)
    dims_of = upper_rows.shape
    return joined_rows.reshape(dims_of[:-2] + (2 * dims_of[-2], dims_of[-1]))


def peak_ratios(series, tail_len):
    searched = series[..., tail_len:]
    average = jnp.mean(searched, axis=-1, keepdims=True)
    deviation = jnp.sqrt(jnp.mean((searched - average) ** 2, axis=-1, keepdims=True) + 1e-05)
    reach_back = 2 ** (WIDTHS - 1)
    boxcar = series[..., tail_len - reach_back :]
    results = []
    for width_bit in range(WIDTHS):
        width_now = 2**width_bit
        if width_bit > 0:
            half_width = width_now // 2
            pad_spec = [(0, 0)] * (series.ndim - 1) + [(half_width, 0)]
            boxcar = boxcar + jnp.pad(boxcar[..., :-half_width], pad_spec)
        ratio = (boxcar[..., reach_back:] - width_now * average) / (
            jnp.sqrt(jnp.float32(width_now)) * deviation
        )
        results.append(jnp.max(ratio, axis=-1))
    return jnp.stack(results, axis=-2)


def delay_traced(row_block, amount, pad_ref):
    rows, length = row_block.shape
    columns = length // 128
    whole = amount // 128
    part = amount - whole * 128
    lane = lax.broadcasted_iota(jnp.int32, (rows, 128), 1)
    before = jnp.zeros((rows, 128), jnp.float32)
    for j in range(columns):
        turned = pltpu.roll(row_block[:, 128 * j : 128 * (j + 1)], part, 1)
        pad_ref[:rows, length + 128 * j : length + 128 * (j + 1)] = jnp.where(lane >= part, turned, before)
        before = turned
    start = pl.multiple_of(length - 128 * jnp.minimum(whole, columns), 128)
    return pad_ref[:rows, pl.ds(start, length)]


def shift_in(row_block, amount, lanes, stride, pad_ref=None):
    if pad_ref is not None and not stride and not isinstance(amount, int):
        return delay_traced(row_block, amount, pad_ref)
    if stride:
        moved = pltpu.roll(row_block, amount, 1, stride=stride, stride_axis=0)
        limit = lax.broadcasted_iota(jnp.int32, row_block.shape, 0) * stride + amount
    else:
        moved = pltpu.roll(row_block, amount, 1)
        limit = amount
    return jnp.where(lanes >= limit, moved, jnp.float32(0.0))


def permute_rows(matrix, rows):
    return jnp.dot(matrix, rows, precision=lax.Precision.HIGHEST, preferred_element_type=jnp.float32)


def swap_blocks(rows, tile):
    length = rows.shape[1]
    blocks = rows.reshape(tile, tile, length)
    return pltpu.einshape("abt->bat", blocks).reshape(tile * tile, length)


def tree_in_place(buf, mid_ref, subbands, trials, first_trial, tile, pad_ref=None):
    length = buf.shape[1]
    while subbands > 1 and subbands // 2 >= tile:
        half = subbands // 2
        lanes = lax.broadcasted_iota(jnp.int32, (half, length), 1)
        for k in range(trials):
            top = k * subbands
            upper = buf[top : top + half, :]
            lower = buf[top + half : top + subbands, :]
            buf[top : top + half, :] = upper + shift_in(lower, first_trial + k, lanes, 0, pad_ref)
            buf[top + half : top + subbands, :] = upper + shift_in(
                lower, first_trial + k + 1, lanes, 0, pad_ref
            )
        subbands = half
        trials = 2 * trials
        first_trial = 2 * first_trial
    if subbands == tile and buf.shape[0] == tile * tile:
        buf[...] = swap_blocks(buf[...], tile)
    else:
        buf[...] = permute_rows(mid_ref[...], buf[...])
    groups, step = 1, 1
    lanes = lax.broadcasted_iota(jnp.int32, (tile, length), 1)
    if not isinstance(first_trial, int):
        order = bit_reversed(subbands)
        for pos in range(subbands):
            rows = slice(pos * tile, (pos + 1) * tile)
            buf[rows, :] = shift_in(buf[rows, :], first_trial * int(order[pos]), lanes, 0, pad_ref)
        first_trial = 0
    while subbands > 1:
        half = subbands // 2
        for group in range(groups):
            for pos in range(half):
                top = (group * subbands + pos) * tile
                low = (group * subbands + pos + half) * tile
                upper = buf[top : top + tile, :]
                lower = buf[low : low + tile, :]
                buf[top : top + tile, :] = upper + shift_in(lower, first_trial + group, lanes, step)
                buf[low : low + tile, :] = upper + shift_in(
                    lower, first_trial + group + 1, lanes, step
                )
        subbands = half
        groups = 2 * groups
        step = 2 * step
        first_trial = 2 * first_trial
    return groups


def bit_reversed(count):
    bits = count.bit_length() - 1
    return np.array([int(format(i, f"0{bits}b")[::-1], 2) for i in range(count)], np.int32)


def one_hot(targets):
    return np.eye(len(targets), dtype=np.float32)[targets]


def tables(subbands, trials, tile):
    rows = subbands * trials
    order = bit_reversed(subbands)
    entry = one_hot([order[r % subbands] * trials + r // subbands for r in range(rows)])
    at_switch = rows // tile
    mid = one_hot([(r % tile) * at_switch + r // tile for r in range(rows)])
    groups = rows // tile
    leave = one_hot([(d % groups) * tile + d // groups for d in range(rows)])
    return entry, mid, leave


TILE = 8


def local_tree(tail_samples, block_samples, tail_blocks):
    beams_dev, rows, tail_len = tail_samples.shape
    length = tail_len + block_samples.shape[2]
    entry, mid, leave = tables(rows, 1, TILE)

    def body(count_ref, tail_ref, block_ref, entry_ref, mid_ref, leave_ref, o_ref, buf):
        beam = pl.program_id(0)
        lanes = lax.broadcasted_iota(jnp.int32, (rows, tail_len), 1)
        keep = lanes >= tail_len - 128 * count_ref[beam]
        order = entry_ref[...].astype(jnp.bfloat16)
        tail = jnp.dot(order, tail_ref[...], preferred_element_type=jnp.float32)
        buf[:, :tail_len] = jnp.where(keep, tail, jnp.float32(0.0))
        buf[:, tail_len:] = jnp.dot(order, block_ref[...], preferred_element_type=jnp.float32)
        tree_in_place(buf, mid_ref, rows, 1, 0, TILE)
        buf[...] = swap_blocks(buf[...], TILE)
        for r in range(rows):
            o_ref[r] = buf[r : r + 1, :]

    table_spec = pl.BlockSpec((rows, rows), lambda b: (0, 0))
    return pl.pallas_call(
        body,
        grid=(beams_dev,),
        in_specs=[
            pl.BlockSpec(memory_space=pltpu.SMEM),
            pl.BlockSpec((None, rows, tail_len), lambda b: (b, 0, 0)),
            pl.BlockSpec((None, rows, block_samples.shape[2]), lambda b: (b, 0, 0)),
            table_spec,
            table_spec,
            table_spec,
        ],
        out_specs=pl.BlockSpec((None, rows, 1, length), lambda b: (b, 0, 0, 0)),
        out_shape=jax.ShapeDtypeStruct((beams_dev, rows, 1, length), jnp.float32),
        scratch_shapes=[pltpu.VMEM((rows, length), jnp.float32)],
    )(tail_blocks.astype(jnp.int32), tail_samples, block_samples, entry, mid, leave).reshape(
        beams_dev, rows, length
    )


def peaks_of(dm_rows, tail_len, block_len, leave):
    trials = dm_rows.shape[0]
    searched = dm_rows[:, tail_len:]
    average = jnp.sum(searched, axis=1, keepdims=True) / jnp.float32(block_len)
    spread = jnp.sum((searched - average) ** 2, axis=1, keepdims=True) / jnp.float32(block_len)
    deviation = jnp.sqrt(spread + jnp.float32(1e-05))
    boxcar = dm_rows[:, tail_len - 128 :]
    lane_ids = lax.broadcasted_iota(jnp.int32, (trials, 128), 1)
    table = jnp.zeros((trials, 128), jnp.float32)
    for width_bit in range(WIDTHS):
        width_now = 2**width_bit
        if width_bit > 0:
            boxcar = boxcar + pltpu.roll(boxcar, width_now // 2, 1)
        top = jnp.max(boxcar[:, 128:], axis=1, keepdims=True)
        ratio = (top - width_now * average) / (np.sqrt(np.float32(width_now)) * deviation)
        table = jnp.where(lane_ids == width_bit, ratio, table)
    if trials == TILE * TILE:
        return swap_blocks(table, TILE).T[:8]
    return permute_rows(leave, table).T[:8]


def merge_tree(parts, first_trial, tail_len, dm_limit):
    beams_dev, subbands, trials, length = parts.shape
    rows = subbands * trials
    entry, mid, leave = tables(subbands, trials, TILE)

    order = bit_reversed(subbands)

    def body(off_ref, limit_ref, x_ref, entry_ref, mid_ref, leave_ref, o_ref, buf, pad_ref):
        pad_ref[:, :length] = jnp.zeros((pad_ref.shape[0], length), jnp.float32)
        for pos in range(subbands):
            for trial in range(trials):
                source = int(order[pos]) * trials + trial
                buf[trial * subbands + pos : trial * subbands + pos + 1, :] = x_ref[source]
        tree_in_place(buf, mid_ref, subbands, trials, off_ref[0], TILE, pad_ref)
        table = peaks_of(buf[...], tail_len, length - tail_len, leave_ref[...])[:WIDTHS]
        ids = lax.broadcasted_iota(jnp.int32, table.shape, 1) + off_ref[0] * subbands
        o_ref[...] = jnp.where(ids < limit_ref[pl.program_id(0)], table, jnp.float32(0.0))

    spec = pl.BlockSpec((None, rows, 1, length), lambda b: (b, 0, 0, 0))
    table_spec = pl.BlockSpec((rows, rows), lambda b: (0, 0))
    return pl.pallas_call(
        body,
        grid=(beams_dev,),
        in_specs=[
            pl.BlockSpec(memory_space=pltpu.SMEM),
            pl.BlockSpec(memory_space=pltpu.SMEM),
            spec,
            table_spec,
            table_spec,
            table_spec,
        ],
        out_specs=pl.BlockSpec((None, WIDTHS, rows), lambda b: (b, 0, 0)),
        out_shape=jax.ShapeDtypeStruct((beams_dev, WIDTHS, rows), jnp.float32),
        scratch_shapes=[
            pltpu.VMEM((rows, length), jnp.float32),
            pltpu.VMEM((2 * TILE, 2 * length), jnp.float32),
        ],
    )(
        jnp.reshape(first_trial, (1,)).astype(jnp.int32),
        dm_limit.astype(jnp.int32),
        parts.reshape(beams_dev, rows, 1, length),
        entry,
        mid,
        leave,
    )


def local(block_samples, tail_samples, tail_blocks, dm_limit):
    beams_dev, local_chan, block_len = block_samples.shape
    tail_len = tail_samples.shape[2]
    series = local_tree(tail_samples, block_samples, tail_blocks)[:, None]
    devices = lax.axis_size("freq")
    position = lax.axis_index("freq")
    series = lax.all_to_all(series, "freq", split_axis=2, concat_axis=1, tiled=True)
    per_dev = series.shape[2]
    peak_snr = merge_tree(series, position * per_dev, tail_len, dm_limit)
    beam_total = jnp.sum(peak_snr, axis=0)
    beam_count = lax.axis_size("beam")
    spans = [beam_count - 1] + [1 << b for b in range(beam_count.bit_length() - 2)]
    for span in spans:
        pairs = [(i, i ^ span) for i in range(beam_count)]
        beam_total = beam_total + lax.ppermute(beam_total, "beam", pairs)
    excess_snr = peak_snr - beam_total[None] / (beams_dev * lax.axis_size("beam"))
    return (peak_snr, excess_snr)


def solution(mesh):
    return jax.shard_map(
        local,
        mesh=mesh,
        in_specs=(P("beam", "freq", None), P("beam", "freq", None), P("beam"), P("beam")),
        out_specs=(P("beam", None, "freq"), P("beam", None, "freq")),
        check_vma=False,
    )
```
